256 devices in a mesh: blocks: 64 (over z, x, core), chan: 4 (over y).
Axes of the slice: x: 4, y: 4, z: 8, core: 2. Of those that a mesh axis runs over, the one named last changes fastest.
Arguments:
- fine_input: bfloat16 [1024, 64, 512], P('blocks', 'chan'), may hold values from -6 to 6
- block_counts: int32 [64], replicated, may hold values from 8 to 16, as said below
- fine_weight: bfloat16 [7, 64, 64], P(None, 'chan'), may hold values from -0.25 to 0.25
- fine_bias: float32 [64], P('chan'), may hold values from -3 to 3
- coarse_weight: bfloat16 [7, 64, 64], P(None, 'chan'), may hold values from -0.25 to 0.25
- coarse_bias: float32 [64], P('chan'), may hold values from -3 to 3
- coarse_cotangent: bfloat16 [128, 64, 512], P('blocks', 'chan'), may hold values from -48 to 48
Outputs:
- coarser_level_output: bfloat16 [128, 64, 512], P('blocks', 'chan')
- fine_grad: bfloat16 [1024, 64, 512], P('blocks', 'chan')
- fine_weight_grad: float32 [7, 64, 64], P(None, 'chan')
- fine_bias_grad: float32 [64], P('chan')
- coarse_weight_grad: float32 [7, 64, 64], P(None, 'chan')
- coarse_bias_grad: float32 [64], P('chan')
The draws below stay inside these ranges and needn't reach their ends.
Inputs may be any that keep to these rules, and one draw needn't show every extreme that they name: `block_counts`: fine blocks held by each device of blocks; they sum to 768, and some device holds exactly 16.
All inputs are finite; a program needn't handle non-finite values.
Results may differ from the reference program's by a relative error of at most 0.017.
Values may be sent and summed in bfloat16 or wider, within the bound.
No kernel may reach another device: no remote copies, remote signals or barrier semaphores. Data moves between devices by JAX's collectives and lax.ppermute only.
A program may use at most 64 MiB of HBM per device.

```python
import math
import jax
import jax.numpy as jnp
from jax import lax

C = 64
EDGE = 8
SLOTS_F = 16
SLOTS_C = 2
NFINE = 768
NCOARSE = 96
N_BLOCKS = 64


def draw_block_counts(key, part):
    half_count = N_BLOCKS // 2
    spare = SLOTS_F - 8
    first_key, second_key, third_key = jax.random.split(key, 3)
    extra = jax.random.randint(first_key, (half_count,), 0, spare + 1)
    forced = jax.random.randint(second_key, (), 0, half_count)
    extra = jnp.where(jnp.arange(half_count) == forced, spare, extra)
    paired = jnp.concatenate([extra, spare - extra])
    shuffle = jax.random.permutation(third_key, N_BLOCKS)
    return (8 + paired[shuffle]).astype(jnp.int32)


def levels(own_key, dims, pieces, least, top_value):
    loudness = 1.0
    for dim, blocks in pieces:
        steps = jax.random.uniform(jax.random.fold_in(jax.random.fold_in(own_key, 6), dim), (blocks,), jnp.float32, least / len(pieces), top_value / len(pieces))
        loudness = loudness * jnp.repeat(jnp.exp(steps), dims[dim] // blocks).reshape((-1,) + (1,) * (len(dims) - 1 - dim))
    return loudness


def gaussian(own_key, extent, scale, reach, pieces=(), kind=jnp.bfloat16):
    drawn = scale * jax.random.normal(own_key, extent, jnp.float32)
    if pieces:
        drawn = drawn * levels(own_key, extent, pieces, -0.22, 0.18)
    return jnp.clip(drawn, -reach, reach).astype(kind)


def setup_inputs(seed: int = 0) -> dict:
    arg_keys = jax.random.split(jax.random.key(seed), 8)
    return {
        "fine_input": gaussian(arg_keys[0], (N_BLOCKS * SLOTS_F, C, EDGE ** 3), 1.0, 6.0, ((0, 64), (1, 4))),
        "block_counts": draw_block_counts(jax.random.fold_in(arg_keys[7], 71), 0),
        "fine_weight": gaussian(arg_keys[2], (7, C, C), (7 * C) ** -0.5, 0.25, ((1, 4),)),
        "fine_bias": gaussian(arg_keys[3], (C,), 0.5, 3.0, ((0, 4),), jnp.float32),
        "coarse_weight": gaussian(arg_keys[4], (7, C, C), (7 * C) ** -0.5, 0.25, ((1, 4),)),
        "coarse_bias": gaussian(arg_keys[5], (C,), 0.5, 3.0, ((0, 4),), jnp.float32),
        "coarse_cotangent": gaussian(arg_keys[6], (N_BLOCKS * SLOTS_C, C, EDGE ** 3), 8.0, 48.0, ((0, 64), (1, 4))),
    }


TAP_PAIRS = (0, 2, 1, 4, 3, 6, 5)

def block_layers(block_cube):
    channels, edge_cells = (block_cube.shape[0], block_cube.shape[1])
    side_layers = [block_cube[:, :, :, 0], block_cube[:, :, :, -1], block_cube[:, :, 0, :], block_cube[:, :, -1, :], block_cube[:, 0], block_cube[:, -1]]
    return jnp.stack(side_layers).reshape(6, channels, edge_cells * edge_cells)

def block_views(block_cube, halo_layers):
    channels, edge_cells = (block_cube.shape[0], block_cube.shape[1])
    sheets = halo_layers.reshape(6, channels, edge_cells, edge_cells)
    minus_x = jnp.concatenate([sheets[0][:, :, :, None], block_cube[:, :, :, :-1]], axis=3)
    plus_x = jnp.concatenate([block_cube[:, :, :, 1:], sheets[1][:, :, :, None]], axis=3)
    minus_y = jnp.concatenate([sheets[2][:, :, None, :], block_cube[:, :, :-1, :]], axis=2)
    plus_y = jnp.concatenate([block_cube[:, :, 1:, :], sheets[3][:, :, None, :]], axis=2)
    minus_z = jnp.concatenate([sheets[4][:, None], block_cube[:, :-1]], axis=1)
    plus_z = jnp.concatenate([block_cube[:, 1:], sheets[5][:, None]], axis=1)
    stacked = jnp.stack([block_cube, minus_x, plus_x, minus_y, plus_y, minus_z, plus_z])
    return stacked.reshape(7 * channels, edge_cells ** 3)

def slope_of(pre_values):
    sigmoid_values = jax.nn.sigmoid(pre_values)
    return sigmoid_values * (1.0 + pre_values * (1.0 - sigmoid_values))

def fine_halos(layer_table, total_blocks):
    block_ids = jnp.arange(total_blocks, dtype=jnp.int32)
    offsets = jnp.array([-1, 1, -2, 2, -4, 4], jnp.int32)
    facing = jnp.array([1, 0, 3, 2, 5, 4], jnp.int32)
    parity_x = block_ids % 2
    parity_y = block_ids // 2 % 2
    keep_mask = jnp.stack([parity_x == 1, parity_x == 0, parity_y == 1, parity_y == 0, block_ids >= 4, block_ids + 4 < total_blocks], axis=1)
    neighbour = jnp.clip(block_ids[:, None] + offsets[None, :], 0, total_blocks - 1).astype(jnp.int32)
    fetched = layer_table[neighbour, facing[None, :]]
    return jnp.where(keep_mask[:, :, None, None], fetched, jnp.zeros((), layer_table.dtype))

def coarse_halos(layer_table, total_blocks):
    coarse_ids = jnp.arange(total_blocks, dtype=jnp.int32)
    zero_value = jnp.zeros((), layer_table.dtype)
    lower_rows = jnp.clip(coarse_ids - 1, 0, total_blocks - 1).astype(jnp.int32)
    upper_rows = jnp.clip(coarse_ids + 1, 0, total_blocks - 1).astype(jnp.int32)
    below_layer = jnp.where((coarse_ids >= 1)[:, None, None], layer_table[lower_rows, 5], zero_value)
    above_layer = jnp.where((coarse_ids + 1 < total_blocks)[:, None, None], layer_table[upper_rows, 4], zero_value)
    flat_zero = jnp.zeros_like(below_layer)
    return jnp.stack([flat_zero, flat_zero, flat_zero, flat_zero, below_layer, above_layer], axis=1)

def apply_blocks(matrix, block_cubes, halo_table):

    def one_block(operands):
        return jnp.dot(matrix, block_views(operands[0], operands[1]), preferred_element_type=jnp.float32)
    return lax.map(one_block, (block_cubes, halo_table))

def weight_terms(block_cubes, halo_table, deltas):

    def one_block(operands):
        tap_views = block_views(operands[0], operands[1])
        return lax.dot_general(operands[2], tap_views, (((1,), (1,)), ((), ())), preferred_element_type=jnp.float32)
    summed = lax.optimization_barrier(jnp.sum(lax.map(one_block, (block_cubes, halo_table, deltas)), axis=0))
    return summed.reshape(C, 7, C).transpose(1, 0, 2)

def reference(fine_input, block_counts, fine_weight, fine_bias, coarse_weight, coarse_bias, coarse_cotangent):
    cell_count = EDGE ** 3
    half_edge = EDGE // 2
    starts = (jnp.cumsum(block_counts) - block_counts).astype(jnp.int32)
    block_ids = jnp.arange(NFINE, dtype=jnp.int32)
    owners = (lax.optimization_barrier(jnp.sum((starts[None, :] <= block_ids[:, None]).astype(jnp.int32), axis=1)) - 1).astype(jnp.int32)
    finer_level_slots = (owners * SLOTS_F + block_ids - starts[owners]).astype(jnp.int32)
    coarse_ids = jnp.arange(NCOARSE, dtype=jnp.int32)
    coarse_owners = owners[coarse_ids * 8]
    coarse_slots = (coarse_owners * SLOTS_C + coarse_ids - (starts[coarse_owners] + 7) // 8).astype(jnp.int32)
    pair_index = jnp.array(TAP_PAIRS, jnp.int32)
    fine_cubes = fine_input[finer_level_slots].reshape(NFINE, C, EDGE, EDGE, EDGE)
    input_halos = fine_halos(jax.vmap(block_layers)(fine_cubes), NFINE)
    forward_fine = fine_weight.transpose(1, 0, 2).reshape(C, 7 * C)
    pre_fine = apply_blocks(forward_fine, fine_cubes, input_halos) + fine_bias.astype(jnp.float32)[None, :, None]
    hidden = jax.nn.silu(pre_fine).astype(jnp.bfloat16)
    shaped = hidden.reshape(NFINE, C, half_edge, 2, half_edge, 2, half_edge, 2)
    octants = (lax.optimization_barrier(jnp.sum(shaped, axis=(3, 5, 7), dtype=jnp.float32)) * 0.125).astype(jnp.bfloat16)
    coarse_input = octants.reshape(NCOARSE, 2, 2, 2, C, half_edge, half_edge, half_edge).transpose(0, 4, 1, 5, 2, 6, 3, 7).reshape(NCOARSE, C, cell_count)
    coarse_cubes = coarse_input.reshape(NCOARSE, C, EDGE, EDGE, EDGE)
    coarse_in_halos = coarse_halos(jax.vmap(block_layers)(coarse_cubes), NCOARSE)
    forward_coarser_level = coarse_weight.transpose(1, 0, 2).reshape(C, 7 * C)
    pre_coarse = apply_blocks(forward_coarser_level, coarse_cubes, coarse_in_halos) + coarse_bias.astype(jnp.float32)[None, :, None]
    coarse_values = jax.nn.silu(pre_coarse).astype(jnp.bfloat16)
    cotangent = coarse_cotangent[coarse_slots].astype(jnp.float32)
    coarser_level_delta = (cotangent * slope_of(pre_coarse)).astype(jnp.bfloat16)
    coarse_norm = math.sqrt(NCOARSE * cell_count)
    coarse_weight_grad = weight_terms(coarse_cubes, coarse_in_halos, coarser_level_delta) / coarse_norm
    coarse_bias_grad = lax.optimization_barrier(jnp.sum(coarser_level_delta.astype(jnp.float32), axis=(0, 2))) / coarse_norm
    delta_cubes = coarser_level_delta.reshape(NCOARSE, C, EDGE, EDGE, EDGE)
    delta_halos = coarse_halos(jax.vmap(block_layers)(delta_cubes), NCOARSE)
    backward_coarser_level = coarse_weight[pair_index].transpose(2, 0, 1).reshape(C, 7 * C)
    coarse_back = apply_blocks(backward_coarser_level, delta_cubes, delta_halos).astype(jnp.bfloat16)
    coarse_octants = coarse_back.reshape(NCOARSE, C, 2, half_edge, 2, half_edge, 2, half_edge).transpose(0, 2, 4, 6, 1, 3, 5, 7).reshape(NFINE, C, half_edge, 1, half_edge, 1, half_edge, 1)
    widened = jnp.broadcast_to(coarse_octants, (NFINE, C, half_edge, 2, half_edge, 2, half_edge, 2)).reshape(NFINE, C, cell_count)
    fine_delta = (widened.astype(jnp.float32) * 0.125 * slope_of(pre_fine)).astype(jnp.bfloat16)
    fine_norm = math.sqrt(NFINE * cell_count)
    fine_weight_grad = weight_terms(fine_cubes, input_halos, fine_delta) / fine_norm
    fine_bias_grad = lax.optimization_barrier(jnp.sum(fine_delta.astype(jnp.float32), axis=(0, 2))) / fine_norm
    fine_delta_cubes = fine_delta.reshape(NFINE, C, EDGE, EDGE, EDGE)
    fine_delta_halos = fine_halos(jax.vmap(block_layers)(fine_delta_cubes), NFINE)
    back_fine = fine_weight[pair_index].transpose(2, 0, 1).reshape(C, 7 * C)
    fine_back = apply_blocks(back_fine, fine_delta_cubes, fine_delta_halos).astype(jnp.bfloat16)
    coarser_level_output = jnp.zeros((N_BLOCKS * SLOTS_C, C, cell_count), jnp.bfloat16).at[coarse_slots].set(coarse_values)
    fine_grad = jnp.zeros((N_BLOCKS * SLOTS_F, C, cell_count), jnp.bfloat16).at[finer_level_slots].set(fine_back)
    return (coarser_level_output, fine_grad, fine_weight_grad, fine_bias_grad, coarse_weight_grad, coarse_bias_grad)
```

```python
import jax
import jax.numpy as jnp
from jax import lax
from jax.sharding import PartitionSpec as P

EDGE = 8


TAP_PAIRS = (0, 2, 1, 4, 3, 6, 5)


def from_behind(block, axis, distance):
    devices = range(lax.axis_size(axis))
    route = [(i - distance, i) for i in devices if i - distance in devices]
    return lax.ppermute(block, axis, route)


def block_layers(block_cube):
    channels, edge_cells = (block_cube.shape[0], block_cube.shape[1])
    side_layers = [
        block_cube[:, :, :, 0],
        block_cube[:, :, :, -1],
        block_cube[:, :, 0, :],
        block_cube[:, :, -1, :],
        block_cube[:, 0],
        block_cube[:, -1],
    ]
    return jnp.stack(side_layers).reshape(6, channels, edge_cells * edge_cells)


def block_views(block_cube, halo_layers):
    channels, edge_cells = (block_cube.shape[0], block_cube.shape[1])
    sheets = halo_layers.reshape(6, channels, edge_cells, edge_cells)
    minus_x = jnp.concatenate([sheets[0][:, :, :, None], block_cube[:, :, :, :-1]], axis=3)
    plus_x = jnp.concatenate([block_cube[:, :, :, 1:], sheets[1][:, :, :, None]], axis=3)
    minus_y = jnp.concatenate([sheets[2][:, :, None, :], block_cube[:, :, :-1, :]], axis=2)
    plus_y = jnp.concatenate([block_cube[:, :, 1:, :], sheets[3][:, :, None, :]], axis=2)
    minus_z = jnp.concatenate([sheets[4][:, None], block_cube[:, :-1]], axis=1)
    plus_z = jnp.concatenate([block_cube[:, 1:], sheets[5][:, None]], axis=1)
    stacked = jnp.stack([block_cube, minus_x, plus_x, minus_y, plus_y, minus_z, plus_z])
    return stacked.reshape(7 * channels, edge_cells**3)


def slope_of(pre_values):
    sigmoid_values = jax.nn.sigmoid(pre_values)
    return sigmoid_values * (1.0 + pre_values * (1.0 - sigmoid_values))


def fine_halo(layer_table, block_ids, first_block, live_count, total_blocks):
    slot_count = layer_table.shape[0]
    plus_side = layer_table[:, 1::2]
    minus_side = layer_table[:, 0::2]
    tail_layers = lax.dynamic_slice_in_dim(plus_side, live_count - 4, 4, 0)
    from_lower = from_behind(tail_layers, "blocks", 1)
    from_upper = from_behind(minus_side[:4], "blocks", -1)
    table_minus = jnp.concatenate([from_lower, plus_side], axis=0)
    table_plus = jnp.concatenate([minus_side, from_upper], axis=0)
    strides = jnp.array([1, 2, 4], jnp.int32)
    lower_ids = block_ids[:, None] - strides[None, :]
    upper_octant_index = block_ids[:, None] + strides[None, :]
    end_block = first_block + live_count
    rows_minus = jnp.clip(lower_ids - first_block + 4, 0, slot_count + 3)
    rows_plus = jnp.clip(
        jnp.where(
            upper_octant_index < end_block,
            upper_octant_index - first_block,
            slot_count + upper_octant_index - end_block,
        ),
        0,
        slot_count + 3,
    )
    columns = jnp.arange(3, dtype=jnp.int32)[None, :]
    got_minus = table_minus[rows_minus, columns]
    got_plus = table_plus[rows_plus, columns]
    parity_x = block_ids % 2
    parity_y = block_ids // 2 % 2
    keep_minus = jnp.stack([parity_x == 1, parity_y == 1, block_ids >= 4], axis=1)
    keep_plus = jnp.stack([parity_x == 0, parity_y == 0, block_ids + 4 < total_blocks], axis=1)
    zero_value = jnp.zeros((), layer_table.dtype)
    got_minus = jnp.where(keep_minus[:, :, None, None], got_minus, zero_value)
    got_plus = jnp.where(keep_plus[:, :, None, None], got_plus, zero_value)
    merged = jnp.stack([got_minus, got_plus], axis=2)
    return merged.reshape(layer_table.shape)


def coarse_halo(layer_table, coarse_ids, coarse_first, coarse_count, coarse_total):
    slot_count = layer_table.shape[0]
    top_layers = layer_table[:, 5]
    bottom_layers = layer_table[:, 4]
    last_top = lax.dynamic_index_in_dim(top_layers, coarse_count - 1, 0, keepdims=False)
    from_lower = from_behind(last_top, "blocks", 1)
    from_upper = from_behind(bottom_layers[0], "blocks", -1)
    table_minus = jnp.concatenate([from_lower[None], top_layers], axis=0)
    table_plus = jnp.concatenate([bottom_layers, from_upper[None]], axis=0)
    rows_minus = jnp.clip(coarse_ids - coarse_first, 0, slot_count)
    rows_plus = jnp.clip(
        jnp.where(
            coarse_ids + 1 < coarse_first + coarse_count, coarse_ids + 1 - coarse_first, slot_count
        ),
        0,
        slot_count,
    )
    zero_value = jnp.zeros((), layer_table.dtype)
    below_layer = jnp.where((coarse_ids >= 1)[:, None, None], table_minus[rows_minus], zero_value)
    above_layer = jnp.where(
        (coarse_ids + 1 < coarse_total)[:, None, None], table_plus[rows_plus], zero_value
    )
    flat_zero = jnp.zeros_like(below_layer)
    return jnp.stack([flat_zero, flat_zero, flat_zero, flat_zero, below_layer, above_layer], axis=1)


def apply_blocks(matrix, block_cubes, halo_table):

    def one_block(operands):
        return jnp.dot(
            matrix, block_views(operands[0], operands[1]), preferred_element_type=jnp.float32
        )

    return lax.map(one_block, (block_cubes, halo_table))


def weight_block(operands):
    tap_views = block_views(operands[0], operands[1])
    return lax.dot_general(
        operands[2], tap_views, (((1,), (1,)), ((), ())), preferred_element_type=jnp.float32
    )


def restrict_blocks(hidden, half_edge):
    count, width = (hidden.shape[0], hidden.shape[1])
    shaped = hidden.reshape(count, width, half_edge, 2, half_edge, 2, half_edge, 2)
    return (
        (jnp.sum(shaped, axis=(3, 5, 7), dtype=jnp.float32) * 0.125)
        .astype(jnp.bfloat16)
        .reshape(count, width, half_edge**3)
    )


def sum_over_blocks(parts):
    chan_index = lax.axis_index("chan")
    chan_count = lax.axis_size("chan")
    flat = jnp.concatenate([part.reshape(-1) for part in parts])
    slots = jnp.zeros((chan_count, flat.shape[0]), flat.dtype)
    slots = lax.dynamic_update_index_in_dim(slots, flat, chan_index, 0)
    summed = lax.psum(slots, ("blocks", "chan"))
    mine = lax.dynamic_index_in_dim(summed, chan_index, 0, keepdims=False)
    pieces = []
    offset = 0
    for part in parts:
        pieces.append(mine[offset : offset + part.size].reshape(part.shape))
        offset += part.size
    return tuple(pieces)


def local(
    fine_input, block_counts, fine_weight, fine_bias, coarse_weight, coarse_bias, coarse_cotangent
):
    slot_count, group_size, cell_count = fine_input.shape
    coarse_slots = coarse_cotangent.shape[0]
    channels = fine_weight.shape[2]
    half_edge = EDGE // 2
    octant_cells = half_edge**3
    pair_index = jnp.array(TAP_PAIRS, jnp.int32)
    device = lax.axis_index("blocks")
    starts = jnp.cumsum(block_counts) - block_counts
    first_block = starts[device]
    live_count = block_counts[device]
    end_block = first_block + live_count
    total_blocks = jnp.sum(block_counts)
    coarse_total = total_blocks // 8
    coarse_first = (first_block + 7) // 8
    coarse_count = (end_block + 7) // 8 - coarse_first
    block_ids = first_block + jnp.arange(slot_count, dtype=jnp.int32)
    coarse_ids = coarse_first + jnp.arange(coarse_slots, dtype=jnp.int32)
    live_mask = (jnp.arange(slot_count) < live_count)[:, None, None]
    coarse_live = (jnp.arange(coarse_slots) < coarse_count)[:, None, None]
    full_input = lax.all_gather(fine_input, "chan", axis=1, tiled=True)
    fine_cubes = full_input.reshape(slot_count, channels, EDGE, EDGE, EDGE)
    input_halos = fine_halo(
        jax.vmap(block_layers)(fine_cubes), block_ids, first_block, live_count, total_blocks
    )
    forward_fine = fine_weight.transpose(1, 0, 2).reshape(group_size, 7 * channels)
    fine_views = jax.vmap(block_views)(fine_cubes, input_halos)
    pre_fine = (
        jnp.einsum("ln,bnp->blp", forward_fine, fine_views, preferred_element_type=jnp.float32)
        + fine_bias[None, :, None]
    )
    octants = restrict_blocks(jax.nn.silu(pre_fine).astype(jnp.bfloat16), half_edge)
    upper_octants = from_behind(octants[:7], "blocks", -1)
    octant_table = jnp.concatenate([octants, upper_octants], axis=0)
    children = coarse_ids[:, None] * 8 + jnp.arange(8, dtype=jnp.int32)[None, :]
    child_rows = jnp.clip(
        jnp.where(children < end_block, children - first_block, slot_count + children - end_block),
        0,
        slot_count + 6,
    )
    gathered = octant_table[child_rows]
    coarse_local = (
        gathered.reshape(coarse_slots, 2, 2, 2, group_size, half_edge, half_edge, half_edge)
        .transpose(0, 4, 1, 5, 2, 6, 3, 7)
        .reshape(coarse_slots, group_size, cell_count)
    )
    coarse_local = jnp.where(coarse_live, coarse_local, jnp.zeros((), jnp.bfloat16))
    coarse_full = lax.all_gather(coarse_local, "chan", axis=1, tiled=True)
    coarse_cubes = coarse_full.reshape(coarse_slots, channels, EDGE, EDGE, EDGE)
    coarse_in_halos = coarse_halo(
        jax.vmap(block_layers)(coarse_cubes), coarse_ids, coarse_first, coarse_count, coarse_total
    )
    coarser_level_views = jax.vmap(block_views)(coarse_cubes, coarse_in_halos)
    forward_coarser_level = coarse_weight.transpose(1, 0, 2).reshape(group_size, 7 * channels)
    pre_coarse = (
        jnp.einsum(
            "ln,enp->elp",
            forward_coarser_level,
            coarser_level_views,
            preferred_element_type=jnp.float32,
        )
        + coarse_bias[None, :, None]
    )
    coarser_level_output = jnp.where(coarse_live, jax.nn.silu(pre_coarse), 0.0).astype(jnp.bfloat16)
    coarser_level_delta = jnp.where(
        coarse_live, coarse_cotangent.astype(jnp.float32) * slope_of(pre_coarse), 0.0
    ).astype(jnp.bfloat16)
    coarse_weight_grad = jnp.einsum(
        "zlc,znc->ln", coarser_level_delta, coarser_level_views, preferred_element_type=jnp.float32
    )
    coarse_weight_grad = coarse_weight_grad.reshape(group_size, 7, channels).transpose(1, 0, 2)
    coarse_bias_grad = jnp.sum(coarser_level_delta, axis=(0, 2), dtype=jnp.float32)
    delta_cubes = coarser_level_delta.reshape(coarse_slots, group_size, EDGE, EDGE, EDGE)
    delta_halos = coarse_halo(
        jax.vmap(block_layers)(delta_cubes), coarse_ids, coarse_first, coarse_count, coarse_total
    )
    delta_window_views = jax.vmap(block_views)(delta_cubes, delta_halos)
    backward_coarser_level = (
        coarse_weight[pair_index].transpose(2, 0, 1).reshape(channels, 7 * group_size)
    )
    partial_sums = jnp.einsum(
        "ur,mre->mue",
        backward_coarser_level,
        delta_window_views,
        preferred_element_type=jnp.float32,
    )
    coarse_back = lax.psum_scatter(
        partial_sums.astype(jnp.bfloat16), "chan", scatter_dimension=1, tiled=True
    ).astype(jnp.float32)
    coarse_back = jnp.where(coarse_live, coarse_back, 0.0).astype(jnp.bfloat16)
    coarse_octants = (
        coarse_back.reshape(coarse_slots, group_size, 2, half_edge, 2, half_edge, 2, half_edge)
        .transpose(0, 2, 4, 6, 1, 3, 5, 7)
        .reshape(coarse_slots * 8, group_size, octant_cells)
    )
    last_octants = lax.dynamic_slice_in_dim(coarse_octants, (coarse_count - 1) * 8 + 1, 7, 0)
    lower_octants = from_behind(last_octants, "blocks", 1)
    back_table = jnp.concatenate([coarse_octants, lower_octants], axis=0)
    parents = block_ids // 8
    octant_ids = block_ids % 8
    back_rows = jnp.clip(
        jnp.where(
            parents >= coarse_first,
            (parents - coarse_first) * 8 + octant_ids,
            coarse_slots * 8 + octant_ids - 1,
        ),
        0,
        coarse_slots * 8 + 6,
    )
    picked_rows = back_table[back_rows]
    picked = picked_rows.reshape(slot_count, group_size, half_edge, 1, half_edge, 1, half_edge, 1)
    widened = jnp.broadcast_to(
        picked, (slot_count, group_size, half_edge, 2, half_edge, 2, half_edge, 2)
    ).reshape(slot_count, group_size, cell_count)
    fine_delta = jnp.where(
        live_mask, widened.astype(jnp.float32) * 0.125 * slope_of(pre_fine), 0.0
    ).astype(jnp.bfloat16)
    fine_weight_grad = jnp.einsum(
        "blp,bnp->ln", fine_delta, fine_views, preferred_element_type=jnp.float32
    )
    fine_weight_grad = fine_weight_grad.reshape(group_size, 7, channels).transpose(1, 0, 2)
    fine_bias_grad = jnp.sum(fine_delta, axis=(0, 2), dtype=jnp.float32)
    fine_delta_cubes = fine_delta.reshape(slot_count, group_size, EDGE, EDGE, EDGE)
    fine_delta_halos = fine_halo(
        jax.vmap(block_layers)(fine_delta_cubes), block_ids, first_block, live_count, total_blocks
    )
    back_fine = fine_weight[pair_index].transpose(2, 0, 1).reshape(channels, 7 * group_size)
    fine_delta_views = jax.vmap(block_views)(fine_delta_cubes, fine_delta_halos)
    fine_partial = jnp.einsum(
        "ur,bre->bue", back_fine, fine_delta_views, preferred_element_type=jnp.float32
    )
    fine_back = lax.psum_scatter(
        fine_partial.astype(jnp.bfloat16), "chan", scatter_dimension=1, tiled=True
    ).astype(jnp.float32)
    fine_grad = jnp.where(live_mask, fine_back, 0.0).astype(jnp.bfloat16)
    fine_weight_grad, fine_bias_grad, coarse_weight_grad, coarse_bias_grad = sum_over_blocks(
        (fine_weight_grad, fine_bias_grad, coarse_weight_grad, coarse_bias_grad)
    )
    fine_norm = jnp.sqrt(total_blocks.astype(jnp.float32) * cell_count)
    coarse_norm = jnp.sqrt(coarse_total.astype(jnp.float32) * cell_count)
    return (
        coarser_level_output,
        fine_grad,
        fine_weight_grad / fine_norm,
        fine_bias_grad / fine_norm,
        coarse_weight_grad / coarse_norm,
        coarse_bias_grad / coarse_norm,
    )


def solution(mesh):
    placed = (
        P("blocks", "chan", None),
        P(),
        P(None, "chan", None),
        P("chan"),
        P(None, "chan", None),
        P("chan"),
        P("blocks", "chan", None),
    )
    return jax.shard_map(
        local,
        mesh=mesh,
        in_specs=placed,
        out_specs=(
            P("blocks", "chan", None),
            P("blocks", "chan", None),
            P(None, "chan", None),
            P("chan"),
            P(None, "chan", None),
            P("chan"),
        ),
        check_vma=False,
    )
```

```python
import jax
import jax.numpy as jnp
from jax import lax
from jax.sharding import PartitionSpec as P

EDGE = 8


TAP_PAIRS = (0, 2, 1, 4, 3, 6, 5)


def from_behind(block, axis, distance):
    devices = range(lax.axis_size(axis))
    route = [(i - distance, i) for i in devices if i - distance in devices]
    return lax.ppermute(block, axis, route)


def block_layers(block_cube):
    channels, edge_cells = (block_cube.shape[0], block_cube.shape[1])
    side_layers = [
        block_cube[:, :, :, 0],
        block_cube[:, :, :, -1],
        block_cube[:, :, 0, :],
        block_cube[:, :, -1, :],
        block_cube[:, 0],
        block_cube[:, -1],
    ]
    return jnp.stack(side_layers).reshape(6, channels, edge_cells * edge_cells)


def block_views(block_cube, halo_layers):
    channels, edge_cells = (block_cube.shape[0], block_cube.shape[1])
    sheets = halo_layers.reshape(6, channels, edge_cells, edge_cells)
    minus_x = jnp.concatenate([sheets[0][:, :, :, None], block_cube[:, :, :, :-1]], axis=3)
    plus_x = jnp.concatenate([block_cube[:, :, :, 1:], sheets[1][:, :, :, None]], axis=3)
    minus_y = jnp.concatenate([sheets[2][:, :, None, :], block_cube[:, :, :-1, :]], axis=2)
    plus_y = jnp.concatenate([block_cube[:, :, 1:, :], sheets[3][:, :, None, :]], axis=2)
    minus_z = jnp.concatenate([sheets[4][:, None], block_cube[:, :-1]], axis=1)
    plus_z = jnp.concatenate([block_cube[:, 1:], sheets[5][:, None]], axis=1)
    stacked = jnp.stack([block_cube, minus_x, plus_x, minus_y, plus_y, minus_z, plus_z])
    return stacked.reshape(7 * channels, edge_cells**3)


def flat_views(cubes, halo_layers):
    count, channels, cells = cubes.shape
    edge = EDGE
    position = jnp.arange(cells, dtype=jnp.int32)
    x_pos = position % edge
    y_pos = position // edge % edge
    z_pos = position // (edge * edge)
    sheets = halo_layers.reshape(count, 6, channels, edge * edge)
    zeros = jnp.zeros((count, channels, edge * edge), cubes.dtype)

    def back(step):
        return jnp.concatenate([zeros[:, :, :step], cubes[:, :, : cells - step]], axis=2)

    def ahead(step):
        return jnp.concatenate([cubes[:, :, step:], zeros[:, :, :step]], axis=2)

    def yz_sheet(sheet):
        return jnp.repeat(sheet, edge, axis=2)

    def zx_sheet(sheet):
        shaped = sheet.reshape(count, channels, edge, 1, edge)
        return jnp.broadcast_to(shaped, (count, channels, edge, edge, edge)).reshape(
            count, channels, cells
        )

    def yx_sheet(sheet):
        return jnp.tile(sheet, (1, 1, edge))

    minus_x = jnp.where(x_pos == 0, yz_sheet(sheets[:, 0]), back(1))
    plus_x = jnp.where(x_pos == edge - 1, yz_sheet(sheets[:, 1]), ahead(1))
    minus_y = jnp.where(y_pos == 0, zx_sheet(sheets[:, 2]), back(edge))
    plus_y = jnp.where(y_pos == edge - 1, zx_sheet(sheets[:, 3]), ahead(edge))
    minus_z = jnp.where(z_pos == 0, yx_sheet(sheets[:, 4]), back(edge * edge))
    plus_z = jnp.where(z_pos == edge - 1, yx_sheet(sheets[:, 5]), ahead(edge * edge))
    stacked = jnp.stack([cubes, minus_x, plus_x, minus_y, plus_y, minus_z, plus_z], axis=1)
    return stacked.reshape(count, 7 * channels, cells)


def butterfly_sum(value, axis):
    size = lax.axis_size(axis)
    if size & (size - 1):
        return lax.psum(value, axis)
    distance = 1
    while distance < size:
        value = value + lax.ppermute(value, axis, [(i, i ^ distance) for i in range(size)])
        distance *= 2
    return value


def slope_of(pre_values):
    sigmoid_values = jax.nn.sigmoid(pre_values)
    return sigmoid_values * (1.0 + pre_values * (1.0 - sigmoid_values))


def fine_halo(layer_table, block_ids, first_block, live_count, total_blocks):
    slot_count = layer_table.shape[0]
    plus_side = layer_table[:, 1::2]
    minus_side = layer_table[:, 0::2]
    tail_layers = lax.dynamic_slice_in_dim(plus_side, live_count - 4, 4, 0)
    from_lower = from_behind(tail_layers, "blocks", 1)
    from_upper = from_behind(minus_side[:4], "blocks", -1)
    table_minus = jnp.concatenate([from_lower, plus_side], axis=0)
    table_plus = jnp.concatenate([minus_side, from_upper], axis=0)
    strides = jnp.array([1, 2, 4], jnp.int32)
    lower_ids = block_ids[:, None] - strides[None, :]
    upper_octant_index = block_ids[:, None] + strides[None, :]
    end_block = first_block + live_count
    rows_minus = jnp.clip(lower_ids - first_block + 4, 0, slot_count + 3)
    rows_plus = jnp.clip(
        jnp.where(
            upper_octant_index < end_block,
            upper_octant_index - first_block,
            slot_count + upper_octant_index - end_block,
        ),
        0,
        slot_count + 3,
    )
    columns = jnp.arange(3, dtype=jnp.int32)[None, :]
    got_minus = table_minus[rows_minus, columns]
    got_plus = table_plus[rows_plus, columns]
    parity_x = block_ids % 2
    parity_y = block_ids // 2 % 2
    keep_minus = jnp.stack([parity_x == 1, parity_y == 1, block_ids >= 4], axis=1)
    keep_plus = jnp.stack([parity_x == 0, parity_y == 0, block_ids + 4 < total_blocks], axis=1)
    zero_value = jnp.zeros((), layer_table.dtype)
    got_minus = jnp.where(keep_minus[:, :, None, None], got_minus, zero_value)
    got_plus = jnp.where(keep_plus[:, :, None, None], got_plus, zero_value)
    merged = jnp.stack([got_minus, got_plus], axis=2)
    return merged.reshape(layer_table.shape)


def coarse_halo(layer_table, coarse_ids, coarse_first, coarse_count, coarse_total):
    slot_count = layer_table.shape[0]
    top_layers = layer_table[:, 5]
    bottom_layers = layer_table[:, 4]
    last_top = lax.dynamic_index_in_dim(top_layers, coarse_count - 1, 0, keepdims=False)
    from_lower = from_behind(last_top, "blocks", 1)
    from_upper = from_behind(bottom_layers[0], "blocks", -1)
    table_minus = jnp.concatenate([from_lower[None], top_layers], axis=0)
    table_plus = jnp.concatenate([bottom_layers, from_upper[None]], axis=0)
    rows_minus = jnp.clip(coarse_ids - coarse_first, 0, slot_count)
    rows_plus = jnp.clip(
        jnp.where(
            coarse_ids + 1 < coarse_first + coarse_count, coarse_ids + 1 - coarse_first, slot_count
        ),
        0,
        slot_count,
    )
    zero_value = jnp.zeros((), layer_table.dtype)
    below_layer = jnp.where((coarse_ids >= 1)[:, None, None], table_minus[rows_minus], zero_value)
    above_layer = jnp.where(
        (coarse_ids + 1 < coarse_total)[:, None, None], table_plus[rows_plus], zero_value
    )
    flat_zero = jnp.zeros_like(below_layer)
    return jnp.stack([flat_zero, flat_zero, flat_zero, flat_zero, below_layer, above_layer], axis=1)


def apply_blocks(matrix, block_cubes, halo_table):

    def one_block(operands):
        return jnp.dot(
            matrix, block_views(operands[0], operands[1]), preferred_element_type=jnp.float32
        )

    return lax.map(one_block, (block_cubes, halo_table))


def weight_block(operands):
    tap_views = block_views(operands[0], operands[1])
    return lax.dot_general(
        operands[2], tap_views, (((1,), (1,)), ((), ())), preferred_element_type=jnp.float32
    )


def restrict_blocks(hidden, half_edge):
    count, width = (hidden.shape[0], hidden.shape[1])
    shaped = hidden.reshape(count, width, half_edge, 2, half_edge, 2, half_edge, 2)
    return (
        (jnp.sum(shaped, axis=(3, 5, 7), dtype=jnp.float32) * 0.125)
        .astype(jnp.bfloat16)
        .reshape(count, width, half_edge**3)
    )


def sum_over_blocks(parts):
    flat = jnp.concatenate([part.reshape(-1) for part in parts])
    summed = butterfly_sum(flat, "blocks")
    pieces = []
    offset = 0
    for part in parts:
        pieces.append(summed[offset : offset + part.size].reshape(part.shape))
        offset += part.size
    return tuple(pieces)


def local(
    fine_input, block_counts, fine_weight, fine_bias, coarse_weight, coarse_bias, coarse_cotangent
):
    slot_count, group_size, cell_count = fine_input.shape
    coarse_slots = coarse_cotangent.shape[0]
    channels = fine_weight.shape[2]
    half_edge = EDGE // 2
    octant_cells = half_edge**3
    pair_index = jnp.array(TAP_PAIRS, jnp.int32)
    device = lax.axis_index("blocks")
    starts = jnp.cumsum(block_counts) - block_counts
    first_block = starts[device]
    live_count = block_counts[device]
    end_block = first_block + live_count
    total_blocks = jnp.sum(block_counts)
    coarse_total = total_blocks // 8
    coarse_first = (first_block + 7) // 8
    coarse_count = (end_block + 7) // 8 - coarse_first
    block_ids = first_block + jnp.arange(slot_count, dtype=jnp.int32)
    coarse_ids = coarse_first + jnp.arange(coarse_slots, dtype=jnp.int32)
    live_mask = (jnp.arange(slot_count) < live_count)[:, None, None]
    coarse_live = (jnp.arange(coarse_slots) < coarse_count)[:, None, None]
    full_input = lax.all_gather(fine_input, "chan", axis=1, tiled=True)
    fine_cubes = full_input.reshape(slot_count, channels, EDGE, EDGE, EDGE)
    input_halos = fine_halo(
        jax.vmap(block_layers)(fine_cubes), block_ids, first_block, live_count, total_blocks
    )
    forward_fine = fine_weight.transpose(1, 0, 2).reshape(group_size, 7 * channels)
    fine_views = flat_views(full_input, input_halos)
    pre_fine = (
        jnp.einsum("ln,bnp->blp", forward_fine, fine_views, preferred_element_type=jnp.float32)
        + fine_bias[None, :, None]
    )
    octants = restrict_blocks(jax.nn.silu(pre_fine).astype(jnp.bfloat16), half_edge)
    upper_octants = from_behind(octants[:7], "blocks", -1)
    octant_table = jnp.concatenate([octants, upper_octants], axis=0)
    children = coarse_ids[:, None] * 8 + jnp.arange(8, dtype=jnp.int32)[None, :]
    child_rows = jnp.clip(
        jnp.where(children < end_block, children - first_block, slot_count + children - end_block),
        0,
        slot_count + 6,
    )
    gathered = octant_table[child_rows]
    coarse_local = (
        gathered.reshape(coarse_slots, 2, 2, 2, group_size, half_edge, half_edge, half_edge)
        .transpose(0, 4, 1, 5, 2, 6, 3, 7)
        .reshape(coarse_slots, group_size, cell_count)
    )
    coarse_local = jnp.where(coarse_live, coarse_local, jnp.zeros((), jnp.bfloat16))
    coarse_full = lax.all_gather(coarse_local, "chan", axis=1, tiled=True)
    coarse_cubes = coarse_full.reshape(coarse_slots, channels, EDGE, EDGE, EDGE)
    coarse_in_halos = coarse_halo(
        jax.vmap(block_layers)(coarse_cubes), coarse_ids, coarse_first, coarse_count, coarse_total
    )
    coarser_level_views = flat_views(coarse_full, coarse_in_halos)
    forward_coarser_level = coarse_weight.transpose(1, 0, 2).reshape(group_size, 7 * channels)
    pre_coarse = (
        jnp.einsum(
            "ln,enp->elp",
            forward_coarser_level,
            coarser_level_views,
            preferred_element_type=jnp.float32,
        )
        + coarse_bias[None, :, None]
    )
    coarser_level_output = jnp.where(coarse_live, jax.nn.silu(pre_coarse), 0.0).astype(jnp.bfloat16)
    coarser_level_delta = jnp.where(
        coarse_live, coarse_cotangent.astype(jnp.float32) * slope_of(pre_coarse), 0.0
    ).astype(jnp.bfloat16)
    coarse_weight_grad = jnp.einsum(
        "zlc,znc->ln", coarser_level_delta, coarser_level_views, preferred_element_type=jnp.float32
    )
    coarse_weight_grad = coarse_weight_grad.reshape(group_size, 7, channels).transpose(1, 0, 2)
    coarse_bias_grad = jnp.sum(coarser_level_delta, axis=(0, 2), dtype=jnp.float32)
    delta_cubes = coarser_level_delta.reshape(coarse_slots, group_size, EDGE, EDGE, EDGE)
    delta_halos = coarse_halo(
        jax.vmap(block_layers)(delta_cubes), coarse_ids, coarse_first, coarse_count, coarse_total
    )
    delta_window_views = flat_views(coarser_level_delta, delta_halos)
    backward_coarser_level = (
        coarse_weight[pair_index].transpose(2, 0, 1).reshape(channels, 7 * group_size)
    )
    partial_sums = jnp.einsum(
        "ur,mre->mue",
        backward_coarser_level,
        delta_window_views,
        preferred_element_type=jnp.float32,
    )
    coarse_back = lax.psum_scatter(
        partial_sums.astype(jnp.bfloat16), "chan", scatter_dimension=1, tiled=True
    ).astype(jnp.float32)
    coarse_back = jnp.where(coarse_live, coarse_back, 0.0).astype(jnp.bfloat16)
    coarse_octants = (
        coarse_back.reshape(coarse_slots, group_size, 2, half_edge, 2, half_edge, 2, half_edge)
        .transpose(0, 2, 4, 6, 1, 3, 5, 7)
        .reshape(coarse_slots * 8, group_size, octant_cells)
    )
    last_octants = lax.dynamic_slice_in_dim(coarse_octants, (coarse_count - 1) * 8 + 1, 7, 0)
    lower_octants = from_behind(last_octants, "blocks", 1)
    back_table = jnp.concatenate([coarse_octants, lower_octants], axis=0)
    parents = block_ids // 8
    octant_ids = block_ids % 8
    back_rows = jnp.clip(
        jnp.where(
            parents >= coarse_first,
            (parents - coarse_first) * 8 + octant_ids,
            coarse_slots * 8 + octant_ids - 1,
        ),
        0,
        coarse_slots * 8 + 6,
    )
    picked_rows = back_table[back_rows]
    picked = picked_rows.reshape(slot_count, group_size, half_edge, 1, half_edge, 1, half_edge, 1)
    widened = jnp.broadcast_to(
        picked, (slot_count, group_size, half_edge, 2, half_edge, 2, half_edge, 2)
    ).reshape(slot_count, group_size, cell_count)
    fine_delta = jnp.where(
        live_mask, widened.astype(jnp.float32) * 0.125 * slope_of(pre_fine), 0.0
    ).astype(jnp.bfloat16)
    fine_weight_grad = jnp.einsum(
        "blp,bnp->bln", fine_delta, fine_views, preferred_element_type=jnp.float32
    ).sum(axis=0)
    fine_weight_grad = fine_weight_grad.reshape(group_size, 7, channels).transpose(1, 0, 2)
    fine_bias_grad = jnp.sum(fine_delta, axis=(0, 2), dtype=jnp.float32)
    fine_delta_cubes = fine_delta.reshape(slot_count, group_size, EDGE, EDGE, EDGE)
    fine_delta_halos = fine_halo(
        jax.vmap(block_layers)(fine_delta_cubes), block_ids, first_block, live_count, total_blocks
    )
    back_fine = fine_weight[pair_index].transpose(2, 0, 1).reshape(channels, 7 * group_size)
    fine_delta_views = flat_views(fine_delta, fine_delta_halos)
    fine_partial = jnp.einsum(
        "ur,bre->bue", back_fine, fine_delta_views, preferred_element_type=jnp.float32
    )
    fine_back = lax.psum_scatter(
        fine_partial.astype(jnp.bfloat16), "chan", scatter_dimension=1, tiled=True
    ).astype(jnp.float32)
    fine_grad = jnp.where(live_mask, fine_back, 0.0).astype(jnp.bfloat16)
    fine_weight_grad, fine_bias_grad, coarse_weight_grad, coarse_bias_grad = sum_over_blocks(
        (fine_weight_grad, fine_bias_grad, coarse_weight_grad, coarse_bias_grad)
    )
    fine_norm = jnp.sqrt(total_blocks.astype(jnp.float32) * cell_count)
    coarse_norm = jnp.sqrt(coarse_total.astype(jnp.float32) * cell_count)
    return (
        coarser_level_output,
        fine_grad,
        fine_weight_grad / fine_norm,
        fine_bias_grad / fine_norm,
        coarse_weight_grad / coarse_norm,
        coarse_bias_grad / coarse_norm,
    )


def solution(mesh):
    placed = (
        P("blocks", "chan", None),
        P(),
        P(None, "chan", None),
        P("chan"),
        P(None, "chan", None),
        P("chan"),
        P("blocks", "chan", None),
    )
    return jax.shard_map(
        local,
        mesh=mesh,
        in_specs=placed,
        out_specs=(
            P("blocks", "chan", None),
            P("blocks", "chan", None),
            P(None, "chan", None),
            P("chan"),
            P(None, "chan", None),
            P("chan"),
        ),
        check_vma=False,
    )
```

```python
import jax
import jax.numpy as jnp
from jax import lax
from jax.sharding import PartitionSpec as P

EDGE = 8


TAP_PAIRS = (0, 2, 1, 4, 3, 6, 5)


def from_behind(block, axis, distance):
    devices = range(lax.axis_size(axis))
    route = [(i - distance, i) for i in devices if i - distance in devices]
    return lax.ppermute(block, axis, route)


def block_layers(block_cube):
    channels, edge_cells = (block_cube.shape[0], block_cube.shape[1])
    side_layers = [
        block_cube[:, :, :, 0],
        block_cube[:, :, :, -1],
        block_cube[:, :, 0, :],
        block_cube[:, :, -1, :],
        block_cube[:, 0],
        block_cube[:, -1],
    ]
    return jnp.stack(side_layers).reshape(6, channels, edge_cells * edge_cells)


def block_views(block_cube, halo_layers):
    channels, edge_cells = (block_cube.shape[0], block_cube.shape[1])
    sheets = halo_layers.reshape(6, channels, edge_cells, edge_cells)
    minus_x = jnp.concatenate([sheets[0][:, :, :, None], block_cube[:, :, :, :-1]], axis=3)
    plus_x = jnp.concatenate([block_cube[:, :, :, 1:], sheets[1][:, :, :, None]], axis=3)
    minus_y = jnp.concatenate([sheets[2][:, :, None, :], block_cube[:, :, :-1, :]], axis=2)
    plus_y = jnp.concatenate([block_cube[:, :, 1:, :], sheets[3][:, :, None, :]], axis=2)
    minus_z = jnp.concatenate([sheets[4][:, None], block_cube[:, :-1]], axis=1)
    plus_z = jnp.concatenate([block_cube[:, 1:], sheets[5][:, None]], axis=1)
    stacked = jnp.stack([block_cube, minus_x, plus_x, minus_y, plus_y, minus_z, plus_z])
    return stacked.reshape(7 * channels, edge_cells**3)


def flat_views(cubes, halo_layers):
    count, channels, cells = cubes.shape
    edge = EDGE
    position = jnp.arange(cells, dtype=jnp.int32)
    x_pos = position % edge
    y_pos = position // edge % edge
    z_pos = position // (edge * edge)
    sheets = halo_layers.reshape(count, 6, channels, edge * edge)
    zeros = jnp.zeros((count, channels, edge * edge), cubes.dtype)

    def back(step):
        return jnp.concatenate([zeros[:, :, :step], cubes[:, :, : cells - step]], axis=2)

    def ahead(step):
        return jnp.concatenate([cubes[:, :, step:], zeros[:, :, :step]], axis=2)

    def yz_sheet(sheet):
        return jnp.repeat(sheet, edge, axis=2)

    def zx_sheet(sheet):
        shaped = sheet.reshape(count, channels, edge, 1, edge)
        return jnp.broadcast_to(shaped, (count, channels, edge, edge, edge)).reshape(
            count, channels, cells
        )

    def yx_sheet(sheet):
        return jnp.tile(sheet, (1, 1, edge))

    minus_x = jnp.where(x_pos == 0, yz_sheet(sheets[:, 0]), back(1))
    plus_x = jnp.where(x_pos == edge - 1, yz_sheet(sheets[:, 1]), ahead(1))
    minus_y = jnp.where(y_pos == 0, zx_sheet(sheets[:, 2]), back(edge))
    plus_y = jnp.where(y_pos == edge - 1, zx_sheet(sheets[:, 3]), ahead(edge))
    minus_z = jnp.where(z_pos == 0, yx_sheet(sheets[:, 4]), back(edge * edge))
    plus_z = jnp.where(z_pos == edge - 1, yx_sheet(sheets[:, 5]), ahead(edge * edge))
    stacked = jnp.stack([cubes, minus_x, plus_x, minus_y, plus_y, minus_z, plus_z], axis=1)
    return stacked.reshape(count, 7 * channels, cells)


def chan_gather(value):
    size = lax.axis_size("chan")
    me = lax.axis_index("chan")
    got = [value] + [
        lax.ppermute(value, "chan", [(j, (j + k) % size) for j in range(size)])
        for k in range(1, size)
    ]
    stacked = jnp.stack(got, axis=1)
    order = (me - jnp.arange(size, dtype=jnp.int32)) % size
    full = jnp.take(stacked, order, axis=1)
    return full.reshape((value.shape[0], size * value.shape[1]) + value.shape[2:])


def chan_scatter_sum(partial):
    size = lax.axis_size("chan")
    me = lax.axis_index("chan")
    width = partial.shape[1] // size
    pieces = partial.reshape((partial.shape[0], size, width) + partial.shape[2:])
    total = lax.dynamic_index_in_dim(pieces, me, 1, keepdims=False)
    for k in range(1, size):
        outgoing = lax.dynamic_index_in_dim(pieces, (me + k) % size, 1, keepdims=False)
        total = total + lax.ppermute(
            outgoing, "chan", [(j, (j + k) % size) for j in range(size)]
        )
    return total


def butterfly_sum(value, axis):
    size = lax.axis_size(axis)
    if size & (size - 1):
        return lax.psum(value, axis)
    distance = 1
    while distance < size:
        value = value + lax.ppermute(value, axis, [(i, i ^ distance) for i in range(size)])
        distance *= 2
    return value


def slope_of(pre_values):
    sigmoid_values = jax.nn.sigmoid(pre_values)
    return sigmoid_values * (1.0 + pre_values * (1.0 - sigmoid_values))


def fine_halo(layer_table, block_ids, first_block, live_count, total_blocks):
    slot_count = layer_table.shape[0]
    plus_side = layer_table[:, 1::2]
    minus_side = layer_table[:, 0::2]
    tail_layers = lax.dynamic_slice_in_dim(plus_side, live_count - 4, 4, 0)
    from_lower = from_behind(tail_layers, "blocks", 1)
    from_upper = from_behind(minus_side[:4], "blocks", -1)
    table_minus = jnp.concatenate([from_lower, plus_side], axis=0)
    table_plus = jnp.concatenate([minus_side, from_upper], axis=0)
    strides = jnp.array([1, 2, 4], jnp.int32)
    lower_ids = block_ids[:, None] - strides[None, :]
    upper_octant_index = block_ids[:, None] + strides[None, :]
    end_block = first_block + live_count
    rows_minus = jnp.clip(lower_ids - first_block + 4, 0, slot_count + 3)
    rows_plus = jnp.clip(
        jnp.where(
            upper_octant_index < end_block,
            upper_octant_index - first_block,
            slot_count + upper_octant_index - end_block,
        ),
        0,
        slot_count + 3,
    )
    columns = jnp.arange(3, dtype=jnp.int32)[None, :]
    got_minus = table_minus[rows_minus, columns]
    got_plus = table_plus[rows_plus, columns]
    parity_x = block_ids % 2
    parity_y = block_ids // 2 % 2
    keep_minus = jnp.stack([parity_x == 1, parity_y == 1, block_ids >= 4], axis=1)
    keep_plus = jnp.stack([parity_x == 0, parity_y == 0, block_ids + 4 < total_blocks], axis=1)
    zero_value = jnp.zeros((), layer_table.dtype)
    got_minus = jnp.where(keep_minus[:, :, None, None], got_minus, zero_value)
    got_plus = jnp.where(keep_plus[:, :, None, None], got_plus, zero_value)
    merged = jnp.stack([got_minus, got_plus], axis=2)
    return merged.reshape(layer_table.shape)


def coarse_halo(layer_table, coarse_ids, coarse_first, coarse_count, coarse_total):
    slot_count = layer_table.shape[0]
    top_layers = layer_table[:, 5]
    bottom_layers = layer_table[:, 4]
    last_top = lax.dynamic_index_in_dim(top_layers, coarse_count - 1, 0, keepdims=False)
    from_lower = from_behind(last_top, "blocks", 1)
    from_upper = from_behind(bottom_layers[0], "blocks", -1)
    table_minus = jnp.concatenate([from_lower[None], top_layers], axis=0)
    table_plus = jnp.concatenate([bottom_layers, from_upper[None]], axis=0)
    rows_minus = jnp.clip(coarse_ids - coarse_first, 0, slot_count)
    rows_plus = jnp.clip(
        jnp.where(
            coarse_ids + 1 < coarse_first + coarse_count, coarse_ids + 1 - coarse_first, slot_count
        ),
        0,
        slot_count,
    )
    zero_value = jnp.zeros((), layer_table.dtype)
    below_layer = jnp.where((coarse_ids >= 1)[:, None, None], table_minus[rows_minus], zero_value)
    above_layer = jnp.where(
        (coarse_ids + 1 < coarse_total)[:, None, None], table_plus[rows_plus], zero_value
    )
    flat_zero = jnp.zeros_like(below_layer)
    return jnp.stack([flat_zero, flat_zero, flat_zero, flat_zero, below_layer, above_layer], axis=1)


def apply_blocks(matrix, block_cubes, halo_table):

    def one_block(operands):
        return jnp.dot(
            matrix, block_views(operands[0], operands[1]), preferred_element_type=jnp.float32
        )

    return lax.map(one_block, (block_cubes, halo_table))


def weight_block(operands):
    tap_views = block_views(operands[0], operands[1])
    return lax.dot_general(
        operands[2], tap_views, (((1,), (1,)), ((), ())), preferred_element_type=jnp.float32
    )


def restrict_blocks(hidden, half_edge):
    count, width = (hidden.shape[0], hidden.shape[1])
    shaped = hidden.reshape(count, width, half_edge, 2, half_edge, 2, half_edge, 2)
    return (
        (jnp.sum(shaped, axis=(3, 5, 7), dtype=jnp.float32) * 0.125)
        .astype(jnp.bfloat16)
        .reshape(count, width, half_edge**3)
    )


def sum_over_blocks(parts):
    flat = jnp.concatenate([part.reshape(-1) for part in parts])
    summed = butterfly_sum(flat, "blocks")
    pieces = []
    offset = 0
    for part in parts:
        pieces.append(summed[offset : offset + part.size].reshape(part.shape))
        offset += part.size
    return tuple(pieces)


def local(
    fine_input, block_counts, fine_weight, fine_bias, coarse_weight, coarse_bias, coarse_cotangent
):
    slot_count, group_size, cell_count = fine_input.shape
    coarse_slots = coarse_cotangent.shape[0]
    channels = fine_weight.shape[2]
    half_edge = EDGE // 2
    octant_cells = half_edge**3
    pair_index = jnp.array(TAP_PAIRS, jnp.int32)
    device = lax.axis_index("blocks")
    starts = jnp.cumsum(block_counts) - block_counts
    first_block = starts[device]
    live_count = block_counts[device]
    end_block = first_block + live_count
    total_blocks = jnp.sum(block_counts)
    coarse_total = total_blocks // 8
    coarse_first = (first_block + 7) // 8
    coarse_count = (end_block + 7) // 8 - coarse_first
    block_ids = first_block + jnp.arange(slot_count, dtype=jnp.int32)
    coarse_ids = coarse_first + jnp.arange(coarse_slots, dtype=jnp.int32)
    live_mask = (jnp.arange(slot_count) < live_count)[:, None, None]
    coarse_live = (jnp.arange(coarse_slots) < coarse_count)[:, None, None]
    full_input = chan_gather(fine_input)
    fine_cubes = full_input.reshape(slot_count, channels, EDGE, EDGE, EDGE)
    input_halos = fine_halo(
        jax.vmap(block_layers)(fine_cubes), block_ids, first_block, live_count, total_blocks
    )
    forward_fine = fine_weight.transpose(1, 0, 2).reshape(group_size, 7 * channels)
    fine_views = flat_views(full_input, input_halos)
    pre_fine = (
        jnp.einsum("ln,bnp->blp", forward_fine, fine_views, preferred_element_type=jnp.float32)
        + fine_bias[None, :, None]
    )
    octants = restrict_blocks(jax.nn.silu(pre_fine).astype(jnp.bfloat16), half_edge)
    upper_octants = from_behind(octants[:7], "blocks", -1)
    octant_table = jnp.concatenate([octants, upper_octants], axis=0)
    children = coarse_ids[:, None] * 8 + jnp.arange(8, dtype=jnp.int32)[None, :]
    child_rows = jnp.clip(
        jnp.where(children < end_block, children - first_block, slot_count + children - end_block),
        0,
        slot_count + 6,
    )
    gathered = octant_table[child_rows]
    coarse_local = (
        gathered.reshape(coarse_slots, 2, 2, 2, group_size, half_edge, half_edge, half_edge)
        .transpose(0, 4, 1, 5, 2, 6, 3, 7)
        .reshape(coarse_slots, group_size, cell_count)
    )
    coarse_local = jnp.where(coarse_live, coarse_local, jnp.zeros((), jnp.bfloat16))
    coarse_full = chan_gather(coarse_local)
    coarse_cubes = coarse_full.reshape(coarse_slots, channels, EDGE, EDGE, EDGE)
    coarse_in_halos = coarse_halo(
        jax.vmap(block_layers)(coarse_cubes), coarse_ids, coarse_first, coarse_count, coarse_total
    )
    coarser_level_views = flat_views(coarse_full, coarse_in_halos)
    forward_coarser_level = coarse_weight.transpose(1, 0, 2).reshape(group_size, 7 * channels)
    pre_coarse = (
        jnp.einsum(
            "ln,enp->elp",
            forward_coarser_level,
            coarser_level_views,
            preferred_element_type=jnp.float32,
        )
        + coarse_bias[None, :, None]
    )
    coarser_level_output = jnp.where(coarse_live, jax.nn.silu(pre_coarse), 0.0).astype(jnp.bfloat16)
    coarser_level_delta = jnp.where(
        coarse_live, coarse_cotangent.astype(jnp.float32) * slope_of(pre_coarse), 0.0
    ).astype(jnp.bfloat16)
    coarse_weight_grad = jnp.einsum(
        "zlc,znc->ln", coarser_level_delta, coarser_level_views, preferred_element_type=jnp.float32
    )
    coarse_weight_grad = coarse_weight_grad.reshape(group_size, 7, channels).transpose(1, 0, 2)
    coarse_bias_grad = jnp.sum(coarser_level_delta, axis=(0, 2), dtype=jnp.float32)
    delta_cubes = coarser_level_delta.reshape(coarse_slots, group_size, EDGE, EDGE, EDGE)
    delta_halos = coarse_halo(
        jax.vmap(block_layers)(delta_cubes), coarse_ids, coarse_first, coarse_count, coarse_total
    )
    delta_window_views = flat_views(coarser_level_delta, delta_halos)
    backward_coarser_level = (
        coarse_weight[pair_index].transpose(2, 0, 1).reshape(channels, 7 * group_size)
    )
    partial_sums = jnp.einsum(
        "ur,mre->mue",
        backward_coarser_level,
        delta_window_views,
        preferred_element_type=jnp.float32,
    )
    coarse_back = chan_scatter_sum(partial_sums)
    coarse_back = jnp.where(coarse_live, coarse_back, 0.0).astype(jnp.bfloat16)
    coarse_octants = (
        coarse_back.reshape(coarse_slots, group_size, 2, half_edge, 2, half_edge, 2, half_edge)
        .transpose(0, 2, 4, 6, 1, 3, 5, 7)
        .reshape(coarse_slots * 8, group_size, octant_cells)
    )
    last_octants = lax.dynamic_slice_in_dim(coarse_octants, (coarse_count - 1) * 8 + 1, 7, 0)
    lower_octants = from_behind(last_octants, "blocks", 1)
    back_table = jnp.concatenate([coarse_octants, lower_octants], axis=0)
    parents = block_ids // 8
    octant_ids = block_ids % 8
    back_rows = jnp.clip(
        jnp.where(
            parents >= coarse_first,
            (parents - coarse_first) * 8 + octant_ids,
            coarse_slots * 8 + octant_ids - 1,
        ),
        0,
        coarse_slots * 8 + 6,
    )
    picked_rows = back_table[back_rows]
    picked = picked_rows.reshape(slot_count, group_size, half_edge, 1, half_edge, 1, half_edge, 1)
    widened = jnp.broadcast_to(
        picked, (slot_count, group_size, half_edge, 2, half_edge, 2, half_edge, 2)
    ).reshape(slot_count, group_size, cell_count)
    fine_delta = jnp.where(
        live_mask, widened.astype(jnp.float32) * 0.125 * slope_of(pre_fine), 0.0
    ).astype(jnp.bfloat16)
    fine_weight_grad = jnp.einsum(
        "blp,bnp->bln", fine_delta, fine_views, preferred_element_type=jnp.float32
    ).sum(axis=0)
    fine_weight_grad = fine_weight_grad.reshape(group_size, 7, channels).transpose(1, 0, 2)
    fine_bias_grad = jnp.sum(fine_delta, axis=(0, 2), dtype=jnp.float32)
    fine_delta_cubes = fine_delta.reshape(slot_count, group_size, EDGE, EDGE, EDGE)
    fine_delta_halos = fine_halo(
        jax.vmap(block_layers)(fine_delta_cubes), block_ids, first_block, live_count, total_blocks
    )
    back_fine = fine_weight[pair_index].transpose(2, 0, 1).reshape(channels, 7 * group_size)
    fine_delta_views = flat_views(fine_delta, fine_delta_halos)
    fine_partial = jnp.einsum(
        "ur,bre->bue", back_fine, fine_delta_views, preferred_element_type=jnp.float32
    )
    fine_back = chan_scatter_sum(fine_partial)
    fine_grad = jnp.where(live_mask, fine_back, 0.0).astype(jnp.bfloat16)
    fine_weight_grad, fine_bias_grad, coarse_weight_grad, coarse_bias_grad = sum_over_blocks(
        (fine_weight_grad, fine_bias_grad, coarse_weight_grad, coarse_bias_grad)
    )
    fine_norm = jnp.sqrt(total_blocks.astype(jnp.float32) * cell_count)
    coarse_norm = jnp.sqrt(coarse_total.astype(jnp.float32) * cell_count)
    return (
        coarser_level_output,
        fine_grad,
        fine_weight_grad / fine_norm,
        fine_bias_grad / fine_norm,
        coarse_weight_grad / coarse_norm,
        coarse_bias_grad / coarse_norm,
    )


def solution(mesh):
    placed = (
        P("blocks", "chan", None),
        P(),
        P(None, "chan", None),
        P("chan"),
        P(None, "chan", None),
        P("chan"),
        P("blocks", "chan", None),
    )
    return jax.shard_map(
        local,
        mesh=mesh,
        in_specs=placed,
        out_specs=(
            P("blocks", "chan", None),
            P("blocks", "chan", None),
            P(None, "chan", None),
            P("chan"),
            P(None, "chan", None),
            P("chan"),
        ),
        check_vma=False,
    )
```

```python
import jax
import jax.numpy as jnp
from jax import lax
from jax.sharding import PartitionSpec as P

EDGE = 8


TAP_PAIRS = (0, 2, 1, 4, 3, 6, 5)


def from_behind(block, axis, distance):
    devices = range(lax.axis_size(axis))
    route = [(i - distance, i) for i in devices if i - distance in devices]
    return lax.ppermute(block, axis, route)


def block_layers(block_cube):
    channels, edge_cells = (block_cube.shape[0], block_cube.shape[1])
    side_layers = [
        block_cube[:, :, :, 0],
        block_cube[:, :, :, -1],
        block_cube[:, :, 0, :],
        block_cube[:, :, -1, :],
        block_cube[:, 0],
        block_cube[:, -1],
    ]
    return jnp.stack(side_layers).reshape(6, channels, edge_cells * edge_cells)


def block_views(block_cube, halo_layers):
    channels, edge_cells = (block_cube.shape[0], block_cube.shape[1])
    sheets = halo_layers.reshape(6, channels, edge_cells, edge_cells)
    minus_x = jnp.concatenate([sheets[0][:, :, :, None], block_cube[:, :, :, :-1]], axis=3)
    plus_x = jnp.concatenate([block_cube[:, :, :, 1:], sheets[1][:, :, :, None]], axis=3)
    minus_y = jnp.concatenate([sheets[2][:, :, None, :], block_cube[:, :, :-1, :]], axis=2)
    plus_y = jnp.concatenate([block_cube[:, :, 1:, :], sheets[3][:, :, None, :]], axis=2)
    minus_z = jnp.concatenate([sheets[4][:, None], block_cube[:, :-1]], axis=1)
    plus_z = jnp.concatenate([block_cube[:, 1:], sheets[5][:, None]], axis=1)
    stacked = jnp.stack([block_cube, minus_x, plus_x, minus_y, plus_y, minus_z, plus_z])
    return stacked.reshape(7 * channels, edge_cells**3)


def flat_views(cubes, halo_layers):
    count, channels, cells = cubes.shape
    edge = EDGE
    position = jnp.arange(cells, dtype=jnp.int32)
    x_pos = position % edge
    y_pos = position // edge % edge
    z_pos = position // (edge * edge)
    sheets = halo_layers.reshape(count, 6, channels, edge * edge)
    zeros = jnp.zeros((count, channels, edge * edge), cubes.dtype)

    def back(step):
        return jnp.concatenate([zeros[:, :, :step], cubes[:, :, : cells - step]], axis=2)

    def ahead(step):
        return jnp.concatenate([cubes[:, :, step:], zeros[:, :, :step]], axis=2)

    def yz_sheet(sheet):
        return jnp.repeat(sheet, edge, axis=2)

    def zx_sheet(sheet):
        shaped = sheet.reshape(count, channels, edge, 1, edge)
        return jnp.broadcast_to(shaped, (count, channels, edge, edge, edge)).reshape(
            count, channels, cells
        )

    def yx_sheet(sheet):
        return jnp.tile(sheet, (1, 1, edge))

    minus_x = jnp.where(x_pos == 0, yz_sheet(sheets[:, 0]), back(1))
    plus_x = jnp.where(x_pos == edge - 1, yz_sheet(sheets[:, 1]), ahead(1))
    minus_y = jnp.where(y_pos == 0, zx_sheet(sheets[:, 2]), back(edge))
    plus_y = jnp.where(y_pos == edge - 1, zx_sheet(sheets[:, 3]), ahead(edge))
    minus_z = jnp.where(z_pos == 0, yx_sheet(sheets[:, 4]), back(edge * edge))
    plus_z = jnp.where(z_pos == edge - 1, yx_sheet(sheets[:, 5]), ahead(edge * edge))
    stacked = jnp.stack([cubes, minus_x, plus_x, minus_y, plus_y, minus_z, plus_z], axis=1)
    return stacked.reshape(count, 7 * channels, cells)


def chan_gather(value):
    size = lax.axis_size("chan")
    me = lax.axis_index("chan")
    got = [value] + [
        lax.ppermute(value, "chan", [(j, (j + k) % size) for j in range(size)])
        for k in range(1, size)
    ]
    return jnp.concatenate(got, axis=1)


def arrival_order(matrix):
    size = lax.axis_size("chan")
    me = lax.axis_index("chan")
    order = (me - jnp.arange(size, dtype=jnp.int32)) % size
    rows, width = matrix.shape
    shaped = matrix.reshape(rows, 7, size, width // (7 * size))
    return jnp.take(shaped, order, axis=2).reshape(rows, width)


def chan_scatter_sum(partial):
    size = lax.axis_size("chan")
    me = lax.axis_index("chan")
    width = partial.shape[1] // size
    pieces = partial.reshape((partial.shape[0], size, width) + partial.shape[2:])
    total = lax.dynamic_index_in_dim(pieces, me, 1, keepdims=False)
    for k in range(1, size):
        outgoing = lax.dynamic_index_in_dim(pieces, (me + k) % size, 1, keepdims=False)
        total = total + lax.ppermute(
            outgoing, "chan", [(j, (j + k) % size) for j in range(size)]
        )
    return total


def butterfly_sum(value, axis):
    size = lax.axis_size(axis)
    if size & (size - 1):
        return lax.psum(value, axis)
    distance = 1
    while distance < size:
        value = value + lax.ppermute(value, axis, [(i, i ^ distance) for i in range(size)])
        distance *= 2
    return value


def slope_of(pre_values):
    sigmoid_values = jax.nn.sigmoid(pre_values)
    return sigmoid_values * (1.0 + pre_values * (1.0 - sigmoid_values))


def fine_halo(layer_table, block_ids, first_block, live_count, total_blocks):
    slot_count = layer_table.shape[0]
    plus_side = layer_table[:, 1::2]
    minus_side = layer_table[:, 0::2]
    tail_layers = lax.dynamic_slice_in_dim(plus_side, live_count - 4, 4, 0)
    from_lower = from_behind(tail_layers, "blocks", 1)
    from_upper = from_behind(minus_side[:4], "blocks", -1)
    table_minus = jnp.concatenate([from_lower, plus_side], axis=0)
    table_plus = jnp.concatenate([minus_side, from_upper], axis=0)
    strides = jnp.array([1, 2, 4], jnp.int32)
    lower_ids = block_ids[:, None] - strides[None, :]
    upper_octant_index = block_ids[:, None] + strides[None, :]
    end_block = first_block + live_count
    rows_minus = jnp.clip(lower_ids - first_block + 4, 0, slot_count + 3)
    rows_plus = jnp.clip(
        jnp.where(
            upper_octant_index < end_block,
            upper_octant_index - first_block,
            slot_count + upper_octant_index - end_block,
        ),
        0,
        slot_count + 3,
    )
    columns = jnp.arange(3, dtype=jnp.int32)[None, :]
    got_minus = table_minus[rows_minus, columns]
    got_plus = table_plus[rows_plus, columns]
    parity_x = block_ids % 2
    parity_y = block_ids // 2 % 2
    keep_minus = jnp.stack([parity_x == 1, parity_y == 1, block_ids >= 4], axis=1)
    keep_plus = jnp.stack([parity_x == 0, parity_y == 0, block_ids + 4 < total_blocks], axis=1)
    zero_value = jnp.zeros((), layer_table.dtype)
    got_minus = jnp.where(keep_minus[:, :, None, None], got_minus, zero_value)
    got_plus = jnp.where(keep_plus[:, :, None, None], got_plus, zero_value)
    merged = jnp.stack([got_minus, got_plus], axis=2)
    return merged.reshape(layer_table.shape)


def coarse_halo(layer_table, coarse_ids, coarse_first, coarse_count, coarse_total):
    slot_count = layer_table.shape[0]
    top_layers = layer_table[:, 5]
    bottom_layers = layer_table[:, 4]
    last_top = lax.dynamic_index_in_dim(top_layers, coarse_count - 1, 0, keepdims=False)
    from_lower = from_behind(last_top, "blocks", 1)
    from_upper = from_behind(bottom_layers[0], "blocks", -1)
    table_minus = jnp.concatenate([from_lower[None], top_layers], axis=0)
    table_plus = jnp.concatenate([bottom_layers, from_upper[None]], axis=0)
    rows_minus = jnp.clip(coarse_ids - coarse_first, 0, slot_count)
    rows_plus = jnp.clip(
        jnp.where(
            coarse_ids + 1 < coarse_first + coarse_count, coarse_ids + 1 - coarse_first, slot_count
        ),
        0,
        slot_count,
    )
    zero_value = jnp.zeros((), layer_table.dtype)
    below_layer = jnp.where((coarse_ids >= 1)[:, None, None], table_minus[rows_minus], zero_value)
    above_layer = jnp.where(
        (coarse_ids + 1 < coarse_total)[:, None, None], table_plus[rows_plus], zero_value
    )
    flat_zero = jnp.zeros_like(below_layer)
    return jnp.stack([flat_zero, flat_zero, flat_zero, flat_zero, below_layer, above_layer], axis=1)


def apply_blocks(matrix, block_cubes, halo_table):

    def one_block(operands):
        return jnp.dot(
            matrix, block_views(operands[0], operands[1]), preferred_element_type=jnp.float32
        )

    return lax.map(one_block, (block_cubes, halo_table))


def weight_block(operands):
    tap_views = block_views(operands[0], operands[1])
    return lax.dot_general(
        operands[2], tap_views, (((1,), (1,)), ((), ())), preferred_element_type=jnp.float32
    )


def restrict_blocks(hidden, half_edge):
    count, width = (hidden.shape[0], hidden.shape[1])
    shaped = hidden.reshape(count, width, half_edge, 2, half_edge, 2, half_edge, 2)
    return (
        (jnp.sum(shaped, axis=(3, 5, 7), dtype=jnp.float32) * 0.125)
        .astype(jnp.bfloat16)
        .reshape(count, width, half_edge**3)
    )


def sum_over_blocks(parts):
    flat = jnp.concatenate([part.reshape(-1) for part in parts])
    summed = butterfly_sum(flat, "blocks")
    pieces = []
    offset = 0
    for part in parts:
        pieces.append(summed[offset : offset + part.size].reshape(part.shape))
        offset += part.size
    return tuple(pieces)


def local(
    fine_input, block_counts, fine_weight, fine_bias, coarse_weight, coarse_bias, coarse_cotangent
):
    slot_count, group_size, cell_count = fine_input.shape
    coarse_slots = coarse_cotangent.shape[0]
    channels = fine_weight.shape[2]
    half_edge = EDGE // 2
    octant_cells = half_edge**3
    pair_index = jnp.array(TAP_PAIRS, jnp.int32)
    device = lax.axis_index("blocks")
    starts = jnp.cumsum(block_counts) - block_counts
    first_block = starts[device]
    live_count = block_counts[device]
    end_block = first_block + live_count
    total_blocks = jnp.sum(block_counts)
    coarse_total = total_blocks // 8
    coarse_first = (first_block + 7) // 8
    coarse_count = (end_block + 7) // 8 - coarse_first
    block_ids = first_block + jnp.arange(slot_count, dtype=jnp.int32)
    coarse_ids = coarse_first + jnp.arange(coarse_slots, dtype=jnp.int32)
    live_mask = (jnp.arange(slot_count) < live_count)[:, None, None]
    coarse_live = (jnp.arange(coarse_slots) < coarse_count)[:, None, None]
    full_input = chan_gather(fine_input)
    fine_cubes = full_input.reshape(slot_count, channels, EDGE, EDGE, EDGE)
    input_halos = fine_halo(
        jax.vmap(block_layers)(fine_cubes), block_ids, first_block, live_count, total_blocks
    )
    forward_fine = arrival_order(fine_weight.transpose(1, 0, 2).reshape(group_size, 7 * channels))
    fine_views = flat_views(full_input, input_halos)
    pre_fine = (
        jnp.einsum("ln,bnp->blp", forward_fine, fine_views, preferred_element_type=jnp.float32)
        + fine_bias[None, :, None]
    )
    octants = restrict_blocks(jax.nn.silu(pre_fine).astype(jnp.bfloat16), half_edge)
    upper_octants = from_behind(octants[:7], "blocks", -1)
    octant_table = jnp.concatenate([octants, upper_octants], axis=0)
    children = coarse_ids[:, None] * 8 + jnp.arange(8, dtype=jnp.int32)[None, :]
    child_rows = jnp.clip(
        jnp.where(children < end_block, children - first_block, slot_count + children - end_block),
        0,
        slot_count + 6,
    )
    gathered = octant_table[child_rows]
    coarse_local = (
        gathered.reshape(coarse_slots, 2, 2, 2, group_size, half_edge, half_edge, half_edge)
        .transpose(0, 4, 1, 5, 2, 6, 3, 7)
        .reshape(coarse_slots, group_size, cell_count)
    )
    coarse_local = jnp.where(coarse_live, coarse_local, jnp.zeros((), jnp.bfloat16))
    coarse_full = chan_gather(coarse_local)
    coarse_cubes = coarse_full.reshape(coarse_slots, channels, EDGE, EDGE, EDGE)
    coarse_in_halos = coarse_halo(
        jax.vmap(block_layers)(coarse_cubes), coarse_ids, coarse_first, coarse_count, coarse_total
    )
    coarser_level_views = flat_views(coarse_full, coarse_in_halos)
    forward_coarser_level = arrival_order(
        coarse_weight.transpose(1, 0, 2).reshape(group_size, 7 * channels)
    )
    pre_coarse = (
        jnp.einsum(
            "ln,enp->elp",
            forward_coarser_level,
            coarser_level_views,
            preferred_element_type=jnp.float32,
        )
        + coarse_bias[None, :, None]
    )
    coarser_level_output = jnp.where(coarse_live, jax.nn.silu(pre_coarse), 0.0).astype(jnp.bfloat16)
    coarser_level_delta = jnp.where(
        coarse_live, coarse_cotangent.astype(jnp.float32) * slope_of(pre_coarse), 0.0
    ).astype(jnp.bfloat16)
    coarse_weight_grad = jnp.einsum(
        "zlc,znc->ln", coarser_level_delta, coarser_level_views, preferred_element_type=jnp.float32
    )
    coarse_weight_grad = (
        arrival_order(coarse_weight_grad).reshape(group_size, 7, channels).transpose(1, 0, 2)
    )
    coarse_bias_grad = jnp.sum(coarser_level_delta, axis=(0, 2), dtype=jnp.float32)
    delta_cubes = coarser_level_delta.reshape(coarse_slots, group_size, EDGE, EDGE, EDGE)
    delta_halos = coarse_halo(
        jax.vmap(block_layers)(delta_cubes), coarse_ids, coarse_first, coarse_count, coarse_total
    )
    delta_window_views = flat_views(coarser_level_delta, delta_halos)
    backward_coarser_level = (
        coarse_weight[pair_index].transpose(2, 0, 1).reshape(channels, 7 * group_size)
    )
    partial_sums = jnp.einsum(
        "ur,mre->mue",
        backward_coarser_level,
        delta_window_views,
        preferred_element_type=jnp.float32,
    )
    coarse_back = chan_scatter_sum(partial_sums)
    coarse_back = jnp.where(coarse_live, coarse_back, 0.0).astype(jnp.bfloat16)
    coarse_octants = (
        coarse_back.reshape(coarse_slots, group_size, 2, half_edge, 2, half_edge, 2, half_edge)
        .transpose(0, 2, 4, 6, 1, 3, 5, 7)
        .reshape(coarse_slots * 8, group_size, octant_cells)
    )
    last_octants = lax.dynamic_slice_in_dim(coarse_octants, (coarse_count - 1) * 8 + 1, 7, 0)
    lower_octants = from_behind(last_octants, "blocks", 1)
    back_table = jnp.concatenate([coarse_octants, lower_octants], axis=0)
    parents = block_ids // 8
    octant_ids = block_ids % 8
    back_rows = jnp.clip(
        jnp.where(
            parents >= coarse_first,
            (parents - coarse_first) * 8 + octant_ids,
            coarse_slots * 8 + octant_ids - 1,
        ),
        0,
        coarse_slots * 8 + 6,
    )
    picked_rows = back_table[back_rows]
    picked = picked_rows.reshape(slot_count, group_size, half_edge, 1, half_edge, 1, half_edge, 1)
    widened = jnp.broadcast_to(
        picked, (slot_count, group_size, half_edge, 2, half_edge, 2, half_edge, 2)
    ).reshape(slot_count, group_size, cell_count)
    fine_delta = jnp.where(
        live_mask, widened.astype(jnp.float32) * 0.125 * slope_of(pre_fine), 0.0
    ).astype(jnp.bfloat16)
    fine_weight_grad = jnp.einsum(
        "blp,bnp->bln", fine_delta, fine_views, preferred_element_type=jnp.float32
    ).sum(axis=0)
    fine_weight_grad = (
        arrival_order(fine_weight_grad).reshape(group_size, 7, channels).transpose(1, 0, 2)
    )
    fine_bias_grad = jnp.sum(fine_delta, axis=(0, 2), dtype=jnp.float32)
    fine_delta_cubes = fine_delta.reshape(slot_count, group_size, EDGE, EDGE, EDGE)
    fine_delta_halos = fine_halo(
        jax.vmap(block_layers)(fine_delta_cubes), block_ids, first_block, live_count, total_blocks
    )
    back_fine = fine_weight[pair_index].transpose(2, 0, 1).reshape(channels, 7 * group_size)
    fine_delta_views = flat_views(fine_delta, fine_delta_halos)
    fine_partial = jnp.einsum(
        "ur,bre->bue", back_fine, fine_delta_views, preferred_element_type=jnp.float32
    )
    fine_back = chan_scatter_sum(fine_partial)
    fine_grad = jnp.where(live_mask, fine_back, 0.0).astype(jnp.bfloat16)
    fine_weight_grad, fine_bias_grad, coarse_weight_grad, coarse_bias_grad = sum_over_blocks(
        (fine_weight_grad, fine_bias_grad, coarse_weight_grad, coarse_bias_grad)
    )
    fine_norm = jnp.sqrt(total_blocks.astype(jnp.float32) * cell_count)
    coarse_norm = jnp.sqrt(coarse_total.astype(jnp.float32) * cell_count)
    return (
        coarser_level_output,
        fine_grad,
        fine_weight_grad / fine_norm,
        fine_bias_grad / fine_norm,
        coarse_weight_grad / coarse_norm,
        coarse_bias_grad / coarse_norm,
    )


def solution(mesh):
    placed = (
        P("blocks", "chan", None),
        P(),
        P(None, "chan", None),
        P("chan"),
        P(None, "chan", None),
        P("chan"),
        P("blocks", "chan", None),
    )
    return jax.shard_map(
        local,
        mesh=mesh,
        in_specs=placed,
        out_specs=(
            P("blocks", "chan", None),
            P("blocks", "chan", None),
            P(None, "chan", None),
            P("chan"),
            P(None, "chan", None),
            P("chan"),
        ),
        check_vma=False,
    )
```

```python
import jax
import jax.numpy as jnp
from jax import lax
from jax.sharding import PartitionSpec as P

EDGE = 8


TAP_PAIRS = (0, 2, 1, 4, 3, 6, 5)


def from_behind(block, axis, distance):
    devices = range(lax.axis_size(axis))
    route = [(i - distance, i) for i in devices if i - distance in devices]
    return lax.ppermute(block, axis, route)


def block_layers(block_cube):
    channels, edge_cells = (block_cube.shape[0], block_cube.shape[1])
    side_layers = [
        block_cube[:, :, :, 0],
        block_cube[:, :, :, -1],
        block_cube[:, :, 0, :],
        block_cube[:, :, -1, :],
        block_cube[:, 0],
        block_cube[:, -1],
    ]
    return jnp.stack(side_layers).reshape(6, channels, edge_cells * edge_cells)


def block_views(block_cube, halo_layers):
    channels, edge_cells = (block_cube.shape[0], block_cube.shape[1])
    sheets = halo_layers.reshape(6, channels, edge_cells, edge_cells)
    minus_x = jnp.concatenate([sheets[0][:, :, :, None], block_cube[:, :, :, :-1]], axis=3)
    plus_x = jnp.concatenate([block_cube[:, :, :, 1:], sheets[1][:, :, :, None]], axis=3)
    minus_y = jnp.concatenate([sheets[2][:, :, None, :], block_cube[:, :, :-1, :]], axis=2)
    plus_y = jnp.concatenate([block_cube[:, :, 1:, :], sheets[3][:, :, None, :]], axis=2)
    minus_z = jnp.concatenate([sheets[4][:, None], block_cube[:, :-1]], axis=1)
    plus_z = jnp.concatenate([block_cube[:, 1:], sheets[5][:, None]], axis=1)
    stacked = jnp.stack([block_cube, minus_x, plus_x, minus_y, plus_y, minus_z, plus_z])
    return stacked.reshape(7 * channels, edge_cells**3)


def flat_views(cubes, halo_layers):
    count, channels, cells = cubes.shape
    edge = EDGE
    position = jnp.arange(cells, dtype=jnp.int32)
    x_pos = position % edge
    y_pos = position // edge % edge
    z_pos = position // (edge * edge)
    sheets = halo_layers.reshape(count, 6, channels, edge * edge)
    zeros = jnp.zeros((count, channels, edge * edge), cubes.dtype)

    def back(step):
        return jnp.concatenate([zeros[:, :, :step], cubes[:, :, : cells - step]], axis=2)

    def ahead(step):
        return jnp.concatenate([cubes[:, :, step:], zeros[:, :, :step]], axis=2)

    def yz_sheet(sheet):
        return jnp.repeat(sheet, edge, axis=2)

    def zx_sheet(sheet):
        shaped = sheet.reshape(count, channels, edge, 1, edge)
        return jnp.broadcast_to(shaped, (count, channels, edge, edge, edge)).reshape(
            count, channels, cells
        )

    def yx_sheet(sheet):
        return jnp.tile(sheet, (1, 1, edge))

    minus_x = jnp.where(x_pos == 0, yz_sheet(sheets[:, 0]), back(1))
    plus_x = jnp.where(x_pos == edge - 1, yz_sheet(sheets[:, 1]), ahead(1))
    minus_y = jnp.where(y_pos == 0, zx_sheet(sheets[:, 2]), back(edge))
    plus_y = jnp.where(y_pos == edge - 1, zx_sheet(sheets[:, 3]), ahead(edge))
    minus_z = jnp.where(z_pos == 0, yx_sheet(sheets[:, 4]), back(edge * edge))
    plus_z = jnp.where(z_pos == edge - 1, yx_sheet(sheets[:, 5]), ahead(edge * edge))
    stacked = jnp.stack([cubes, minus_x, plus_x, minus_y, plus_y, minus_z, plus_z], axis=1)
    return stacked.reshape(count, 7 * channels, cells)


def chan_gather(value):
    size = lax.axis_size("chan")
    me = lax.axis_index("chan")
    got = [value] + [
        lax.ppermute(value, "chan", [(j, (j + k) % size) for j in range(size)])
        for k in range(1, size)
    ]
    return jnp.concatenate(got, axis=1)


def arrival_order(matrix):
    size = lax.axis_size("chan")
    me = lax.axis_index("chan")
    order = (me - jnp.arange(size, dtype=jnp.int32)) % size
    rows, width = matrix.shape
    shaped = matrix.reshape(rows, 7, size, width // (7 * size))
    return jnp.take(shaped, order, axis=2).reshape(rows, width)


def chan_scatter_sum(partial):
    size = lax.axis_size("chan")
    me = lax.axis_index("chan")
    width = partial.shape[1] // size
    pieces = partial.reshape((partial.shape[0], size, width) + partial.shape[2:])
    total = lax.dynamic_index_in_dim(pieces, me, 1, keepdims=False)
    for k in range(1, size):
        outgoing = lax.dynamic_index_in_dim(pieces, (me + k) % size, 1, keepdims=False)
        total = total + lax.ppermute(
            outgoing, "chan", [(j, (j + k) % size) for j in range(size)]
        )
    return total


def natural_order(grad):
    taps, rows, width = grad.shape
    return arrival_order(grad.transpose(1, 0, 2).reshape(rows, taps * width)).reshape(
        rows, taps, width
    ).transpose(1, 0, 2)


def butterfly_sum(value, axis):
    size = lax.axis_size(axis)
    me = lax.axis_index(axis)
    radix = 4
    stride = 1
    while stride * radix <= size and size % (stride * radix) == 0:
        digit = me // stride % radix
        got = [value]
        for k in range(1, radix):
            route = [
                (i, i - (i // stride % radix) * stride + ((i // stride + k) % radix) * stride)
                for i in range(size)
            ]
            got.append(lax.ppermute(value, axis, route))
        stacked = jnp.stack(got)
        ordered = [
            lax.dynamic_index_in_dim(stacked, (digit - m) % radix, 0, keepdims=False)
            for m in range(radix)
        ]
        value = ordered[0]
        for m in range(1, radix):
            value = value + ordered[m]
        stride *= radix
    distance = stride
    while distance < size:
        if size % (distance * 2):
            return lax.psum(value, axis)
        value = value + lax.ppermute(value, axis, [(i, i ^ distance) for i in range(size)])
        distance *= 2
    return value


def slope_of(pre_values):
    sigmoid_values = jax.nn.sigmoid(pre_values)
    return sigmoid_values * (1.0 + pre_values * (1.0 - sigmoid_values))


def fine_halo(layer_table, block_ids, first_block, live_count, total_blocks):
    slot_count = layer_table.shape[0]
    plus_side = layer_table[:, 1::2]
    minus_side = layer_table[:, 0::2]
    tail_layers = lax.dynamic_slice_in_dim(plus_side, live_count - 4, 4, 0)
    from_lower = from_behind(tail_layers, "blocks", 1)
    from_upper = from_behind(minus_side[:4], "blocks", -1)
    table_minus = jnp.concatenate([from_lower, plus_side], axis=0)
    table_plus = jnp.concatenate([minus_side, from_upper], axis=0)
    strides = jnp.array([1, 2, 4], jnp.int32)
    lower_ids = block_ids[:, None] - strides[None, :]
    upper_octant_index = block_ids[:, None] + strides[None, :]
    end_block = first_block + live_count
    rows_minus = jnp.clip(lower_ids - first_block + 4, 0, slot_count + 3)
    rows_plus = jnp.clip(
        jnp.where(
            upper_octant_index < end_block,
            upper_octant_index - first_block,
            slot_count + upper_octant_index - end_block,
        ),
        0,
        slot_count + 3,
    )
    columns = jnp.arange(3, dtype=jnp.int32)[None, :]
    got_minus = table_minus[rows_minus, columns]
    got_plus = table_plus[rows_plus, columns]
    parity_x = block_ids % 2
    parity_y = block_ids // 2 % 2
    keep_minus = jnp.stack([parity_x == 1, parity_y == 1, block_ids >= 4], axis=1)
    keep_plus = jnp.stack([parity_x == 0, parity_y == 0, block_ids + 4 < total_blocks], axis=1)
    zero_value = jnp.zeros((), layer_table.dtype)
    got_minus = jnp.where(keep_minus[:, :, None, None], got_minus, zero_value)
    got_plus = jnp.where(keep_plus[:, :, None, None], got_plus, zero_value)
    merged = jnp.stack([got_minus, got_plus], axis=2)
    return merged.reshape(layer_table.shape)


def coarse_halo(layer_table, coarse_ids, coarse_first, coarse_count, coarse_total):
    slot_count = layer_table.shape[0]
    top_layers = layer_table[:, 5]
    bottom_layers = layer_table[:, 4]
    last_top = lax.dynamic_index_in_dim(top_layers, coarse_count - 1, 0, keepdims=False)
    from_lower = from_behind(last_top, "blocks", 1)
    from_upper = from_behind(bottom_layers[0], "blocks", -1)
    table_minus = jnp.concatenate([from_lower[None], top_layers], axis=0)
    table_plus = jnp.concatenate([bottom_layers, from_upper[None]], axis=0)
    rows_minus = jnp.clip(coarse_ids - coarse_first, 0, slot_count)
    rows_plus = jnp.clip(
        jnp.where(
            coarse_ids + 1 < coarse_first + coarse_count, coarse_ids + 1 - coarse_first, slot_count
        ),
        0,
        slot_count,
    )
    zero_value = jnp.zeros((), layer_table.dtype)
    below_layer = jnp.where((coarse_ids >= 1)[:, None, None], table_minus[rows_minus], zero_value)
    above_layer = jnp.where(
        (coarse_ids + 1 < coarse_total)[:, None, None], table_plus[rows_plus], zero_value
    )
    flat_zero = jnp.zeros_like(below_layer)
    return jnp.stack([flat_zero, flat_zero, flat_zero, flat_zero, below_layer, above_layer], axis=1)


def apply_blocks(matrix, block_cubes, halo_table):

    def one_block(operands):
        return jnp.dot(
            matrix, block_views(operands[0], operands[1]), preferred_element_type=jnp.float32
        )

    return lax.map(one_block, (block_cubes, halo_table))


def weight_block(operands):
    tap_views = block_views(operands[0], operands[1])
    return lax.dot_general(
        operands[2], tap_views, (((1,), (1,)), ((), ())), preferred_element_type=jnp.float32
    )


def restrict_blocks(hidden, half_edge):
    count, width = (hidden.shape[0], hidden.shape[1])
    shaped = hidden.reshape(count, width, half_edge, 2, half_edge, 2, half_edge, 2)
    return (
        (jnp.sum(shaped, axis=(3, 5, 7), dtype=jnp.float32) * 0.125)
        .astype(jnp.bfloat16)
        .reshape(count, width, half_edge**3)
    )


def sum_over_blocks(parts):
    flat = jnp.concatenate([part.reshape(-1) for part in parts])
    summed = butterfly_sum(flat, "blocks")
    pieces = []
    offset = 0
    for part in parts:
        pieces.append(summed[offset : offset + part.size].reshape(part.shape))
        offset += part.size
    return tuple(pieces)


def local(
    fine_input, block_counts, fine_weight, fine_bias, coarse_weight, coarse_bias, coarse_cotangent
):
    slot_count, group_size, cell_count = fine_input.shape
    coarse_slots = coarse_cotangent.shape[0]
    channels = fine_weight.shape[2]
    half_edge = EDGE // 2
    octant_cells = half_edge**3
    pair_index = jnp.array(TAP_PAIRS, jnp.int32)
    device = lax.axis_index("blocks")
    starts = jnp.cumsum(block_counts) - block_counts
    first_block = starts[device]
    live_count = block_counts[device]
    end_block = first_block + live_count
    total_blocks = jnp.sum(block_counts)
    coarse_total = total_blocks // 8
    coarse_first = (first_block + 7) // 8
    coarse_count = (end_block + 7) // 8 - coarse_first
    block_ids = first_block + jnp.arange(slot_count, dtype=jnp.int32)
    coarse_ids = coarse_first + jnp.arange(coarse_slots, dtype=jnp.int32)
    live_mask = (jnp.arange(slot_count) < live_count)[:, None, None]
    coarse_live = (jnp.arange(coarse_slots) < coarse_count)[:, None, None]
    full_input = chan_gather(fine_input)
    fine_cubes = full_input.reshape(slot_count, channels, EDGE, EDGE, EDGE)
    input_halos = fine_halo(
        jax.vmap(block_layers)(fine_cubes), block_ids, first_block, live_count, total_blocks
    )
    forward_fine = arrival_order(fine_weight.transpose(1, 0, 2).reshape(group_size, 7 * channels))
    fine_views = flat_views(full_input, input_halos)
    pre_fine = (
        jnp.einsum("ln,bnp->blp", forward_fine, fine_views, preferred_element_type=jnp.float32)
        + fine_bias[None, :, None]
    )
    octants = restrict_blocks(jax.nn.silu(pre_fine).astype(jnp.bfloat16), half_edge)
    upper_octants = from_behind(octants[:7], "blocks", -1)
    octant_table = jnp.concatenate([octants, upper_octants], axis=0)
    children = coarse_ids[:, None] * 8 + jnp.arange(8, dtype=jnp.int32)[None, :]
    child_rows = jnp.clip(
        jnp.where(children < end_block, children - first_block, slot_count + children - end_block),
        0,
        slot_count + 6,
    )
    gathered = octant_table[child_rows]
    coarse_local = (
        gathered.reshape(coarse_slots, 2, 2, 2, group_size, half_edge, half_edge, half_edge)
        .transpose(0, 4, 1, 5, 2, 6, 3, 7)
        .reshape(coarse_slots, group_size, cell_count)
    )
    coarse_local = jnp.where(coarse_live, coarse_local, jnp.zeros((), jnp.bfloat16))
    coarse_full = chan_gather(coarse_local)
    coarse_cubes = coarse_full.reshape(coarse_slots, channels, EDGE, EDGE, EDGE)
    coarse_in_halos = coarse_halo(
        jax.vmap(block_layers)(coarse_cubes), coarse_ids, coarse_first, coarse_count, coarse_total
    )
    coarser_level_views = flat_views(coarse_full, coarse_in_halos)
    forward_coarser_level = arrival_order(
        coarse_weight.transpose(1, 0, 2).reshape(group_size, 7 * channels)
    )
    pre_coarse = (
        jnp.einsum(
            "ln,enp->elp",
            forward_coarser_level,
            coarser_level_views,
            preferred_element_type=jnp.float32,
        )
        + coarse_bias[None, :, None]
    )
    coarser_level_output = jnp.where(coarse_live, jax.nn.silu(pre_coarse), 0.0).astype(jnp.bfloat16)
    coarser_level_delta = jnp.where(
        coarse_live, coarse_cotangent.astype(jnp.float32) * slope_of(pre_coarse), 0.0
    ).astype(jnp.bfloat16)
    coarse_weight_grad = jnp.einsum(
        "zlc,znc->ln", coarser_level_delta, coarser_level_views, preferred_element_type=jnp.float32
    )
    coarse_weight_grad = coarse_weight_grad.reshape(group_size, 7, channels).transpose(1, 0, 2)
    coarse_bias_grad = jnp.sum(coarser_level_delta, axis=(0, 2), dtype=jnp.float32)
    delta_cubes = coarser_level_delta.reshape(coarse_slots, group_size, EDGE, EDGE, EDGE)
    delta_halos = coarse_halo(
        jax.vmap(block_layers)(delta_cubes), coarse_ids, coarse_first, coarse_count, coarse_total
    )
    delta_window_views = flat_views(coarser_level_delta, delta_halos)
    backward_coarser_level = (
        coarse_weight[pair_index].transpose(2, 0, 1).reshape(channels, 7 * group_size)
    )
    partial_sums = jnp.einsum(
        "ur,mre->mue",
        backward_coarser_level,
        delta_window_views,
        preferred_element_type=jnp.float32,
    )
    coarse_back = chan_scatter_sum(partial_sums)
    coarse_back = jnp.where(coarse_live, coarse_back, 0.0).astype(jnp.bfloat16)
    coarse_octants = (
        coarse_back.reshape(coarse_slots, group_size, 2, half_edge, 2, half_edge, 2, half_edge)
        .transpose(0, 2, 4, 6, 1, 3, 5, 7)
        .reshape(coarse_slots * 8, group_size, octant_cells)
    )
    last_octants = lax.dynamic_slice_in_dim(coarse_octants, (coarse_count - 1) * 8 + 1, 7, 0)
    lower_octants = from_behind(last_octants, "blocks", 1)
    back_table = jnp.concatenate([coarse_octants, lower_octants], axis=0)
    parents = block_ids // 8
    octant_ids = block_ids % 8
    back_rows = jnp.clip(
        jnp.where(
            parents >= coarse_first,
            (parents - coarse_first) * 8 + octant_ids,
            coarse_slots * 8 + octant_ids - 1,
        ),
        0,
        coarse_slots * 8 + 6,
    )
    picked_rows = back_table[back_rows]
    picked = picked_rows.reshape(slot_count, group_size, half_edge, 1, half_edge, 1, half_edge, 1)
    widened = jnp.broadcast_to(
        picked, (slot_count, group_size, half_edge, 2, half_edge, 2, half_edge, 2)
    ).reshape(slot_count, group_size, cell_count)
    fine_delta = jnp.where(
        live_mask, widened.astype(jnp.float32) * 0.125 * slope_of(pre_fine), 0.0
    ).astype(jnp.bfloat16)
    fine_weight_grad = jnp.einsum(
        "blp,bnp->bln", fine_delta, fine_views, preferred_element_type=jnp.float32
    ).sum(axis=0)
    fine_weight_grad = fine_weight_grad.reshape(group_size, 7, channels).transpose(1, 0, 2)
    fine_bias_grad = jnp.sum(fine_delta, axis=(0, 2), dtype=jnp.float32)
    fine_delta_cubes = fine_delta.reshape(slot_count, group_size, EDGE, EDGE, EDGE)
    fine_delta_halos = fine_halo(
        jax.vmap(block_layers)(fine_delta_cubes), block_ids, first_block, live_count, total_blocks
    )
    back_fine = fine_weight[pair_index].transpose(2, 0, 1).reshape(channels, 7 * group_size)
    fine_delta_views = flat_views(fine_delta, fine_delta_halos)
    fine_partial = jnp.einsum(
        "ur,bre->bue", back_fine, fine_delta_views, preferred_element_type=jnp.float32
    )
    fine_back = chan_scatter_sum(fine_partial)
    fine_grad = jnp.where(live_mask, fine_back, 0.0).astype(jnp.bfloat16)
    fine_weight_grad, fine_bias_grad, coarse_weight_grad, coarse_bias_grad = sum_over_blocks(
        (fine_weight_grad, fine_bias_grad, coarse_weight_grad, coarse_bias_grad)
    )
    fine_weight_grad = natural_order(fine_weight_grad)
    coarse_weight_grad = natural_order(coarse_weight_grad)
    fine_norm = jnp.sqrt(total_blocks.astype(jnp.float32) * cell_count)
    coarse_norm = jnp.sqrt(coarse_total.astype(jnp.float32) * cell_count)
    return (
        coarser_level_output,
        fine_grad,
        fine_weight_grad / fine_norm,
        fine_bias_grad / fine_norm,
        coarse_weight_grad / coarse_norm,
        coarse_bias_grad / coarse_norm,
    )


def solution(mesh):
    placed = (
        P("blocks", "chan", None),
        P(),
        P(None, "chan", None),
        P("chan"),
        P(None, "chan", None),
        P("chan"),
        P("blocks", "chan", None),
    )
    return jax.shard_map(
        local,
        mesh=mesh,
        in_specs=placed,
        out_specs=(
            P("blocks", "chan", None),
            P("blocks", "chan", None),
            P(None, "chan", None),
            P("chan"),
            P(None, "chan", None),
            P("chan"),
        ),
        check_vma=False,
    )
```

```python
import jax
import jax.numpy as jnp
from jax import lax
from jax.sharding import PartitionSpec as P

EDGE = 8


TAP_PAIRS = (0, 2, 1, 4, 3, 6, 5)


def from_behind(block, axis, distance):
    devices = range(lax.axis_size(axis))
    route = [(i - distance, i) for i in devices if i - distance in devices]
    return lax.ppermute(block, axis, route)


def block_layers(block_cube):
    channels, edge_cells = (block_cube.shape[0], block_cube.shape[1])
    side_layers = [
        block_cube[:, :, :, 0],
        block_cube[:, :, :, -1],
        block_cube[:, :, 0, :],
        block_cube[:, :, -1, :],
        block_cube[:, 0],
        block_cube[:, -1],
    ]
    return jnp.stack(side_layers).reshape(6, channels, edge_cells * edge_cells)


def block_views(block_cube, halo_layers):
    channels, edge_cells = (block_cube.shape[0], block_cube.shape[1])
    sheets = halo_layers.reshape(6, channels, edge_cells, edge_cells)
    minus_x = jnp.concatenate([sheets[0][:, :, :, None], block_cube[:, :, :, :-1]], axis=3)
    plus_x = jnp.concatenate([block_cube[:, :, :, 1:], sheets[1][:, :, :, None]], axis=3)
    minus_y = jnp.concatenate([sheets[2][:, :, None, :], block_cube[:, :, :-1, :]], axis=2)
    plus_y = jnp.concatenate([block_cube[:, :, 1:, :], sheets[3][:, :, None, :]], axis=2)
    minus_z = jnp.concatenate([sheets[4][:, None], block_cube[:, :-1]], axis=1)
    plus_z = jnp.concatenate([block_cube[:, 1:], sheets[5][:, None]], axis=1)
    stacked = jnp.stack([block_cube, minus_x, plus_x, minus_y, plus_y, minus_z, plus_z])
    return stacked.reshape(7 * channels, edge_cells**3)


def flat_views(cubes, halo_layers):
    count, channels, cells = cubes.shape
    edge = EDGE
    position = jnp.arange(cells, dtype=jnp.int32)
    x_pos = position % edge
    y_pos = position // edge % edge
    z_pos = position // (edge * edge)
    sheets = halo_layers.reshape(count, 6, channels, edge * edge)
    zeros = jnp.zeros((count, channels, edge * edge), cubes.dtype)

    def back(step):
        return jnp.concatenate([zeros[:, :, :step], cubes[:, :, : cells - step]], axis=2)

    def ahead(step):
        return jnp.concatenate([cubes[:, :, step:], zeros[:, :, :step]], axis=2)

    def yz_sheet(sheet):
        return jnp.repeat(sheet, edge, axis=2)

    def zx_sheet(sheet):
        shaped = sheet.reshape(count, channels, edge, 1, edge)
        return jnp.broadcast_to(shaped, (count, channels, edge, edge, edge)).reshape(
            count, channels, cells
        )

    def yx_sheet(sheet):
        return jnp.tile(sheet, (1, 1, edge))

    minus_x = jnp.where(x_pos == 0, yz_sheet(sheets[:, 0]), back(1))
    plus_x = jnp.where(x_pos == edge - 1, yz_sheet(sheets[:, 1]), ahead(1))
    minus_y = jnp.where(y_pos == 0, zx_sheet(sheets[:, 2]), back(edge))
    plus_y = jnp.where(y_pos == edge - 1, zx_sheet(sheets[:, 3]), ahead(edge))
    minus_z = jnp.where(z_pos == 0, yx_sheet(sheets[:, 4]), back(edge * edge))
    plus_z = jnp.where(z_pos == edge - 1, yx_sheet(sheets[:, 5]), ahead(edge * edge))
    stacked = jnp.stack([cubes, minus_x, plus_x, minus_y, plus_y, minus_z, plus_z], axis=1)
    return stacked.reshape(count, 7 * channels, cells)


def chan_gather(value):
    size = lax.axis_size("chan")
    me = lax.axis_index("chan")
    got = [value] + [
        lax.ppermute(value, "chan", [(j, (j + k) % size) for j in range(size)])
        for k in range(1, size)
    ]
    return jnp.concatenate(got, axis=1)


def arrival_order(matrix):
    size = lax.axis_size("chan")
    me = lax.axis_index("chan")
    order = (me - jnp.arange(size, dtype=jnp.int32)) % size
    rows, width = matrix.shape
    shaped = matrix.reshape(rows, 7, size, width // (7 * size))
    return jnp.take(shaped, order, axis=2).reshape(rows, width)


def chan_scatter_sum(partial):
    size = lax.axis_size("chan")
    me = lax.axis_index("chan")
    width = partial.shape[1] // size
    pieces = partial.reshape((partial.shape[0], size, width) + partial.shape[2:])
    total = lax.dynamic_index_in_dim(pieces, me, 1, keepdims=False)
    for k in range(1, size):
        outgoing = lax.dynamic_index_in_dim(pieces, (me + k) % size, 1, keepdims=False)
        total = total + lax.ppermute(
            outgoing, "chan", [(j, (j + k) % size) for j in range(size)]
        )
    return total


def natural_order(grad):
    taps, rows, width = grad.shape
    return arrival_order(grad.transpose(1, 0, 2).reshape(rows, taps * width)).reshape(
        rows, taps, width
    ).transpose(1, 0, 2)


def butterfly_sum(value, axis):
    size = lax.axis_size(axis)
    me = lax.axis_index(axis)
    radix = 4
    stride = 1
    while stride * radix <= size and size % (stride * radix) == 0:
        digit = me // stride % radix
        got = [value]
        for k in range(1, radix):
            route = [
                (i, i - (i // stride % radix) * stride + ((i // stride + k) % radix) * stride)
                for i in range(size)
            ]
            got.append(lax.ppermute(value, axis, route))
        stacked = jnp.stack(got)
        ordered = [
            lax.dynamic_index_in_dim(stacked, (digit - m) % radix, 0, keepdims=False)
            for m in range(radix)
        ]
        value = ordered[0]
        for m in range(1, radix):
            value = value + ordered[m]
        stride *= radix
    distance = stride
    while distance < size:
        if size % (distance * 2):
            return lax.psum(value, axis)
        value = value + lax.ppermute(value, axis, [(i, i ^ distance) for i in range(size)])
        distance *= 2
    return value


def slope_of(pre_values):
    sigmoid_values = jax.nn.sigmoid(pre_values)
    return sigmoid_values * (1.0 + pre_values * (1.0 - sigmoid_values))


def fine_halo(layer_table, block_ids, first_block, live_count, total_blocks):
    slot_count = layer_table.shape[0]
    plus_side = layer_table[:, 1::2]
    minus_side = layer_table[:, 0::2]
    tail_layers = lax.dynamic_slice_in_dim(plus_side, live_count - 4, 4, 0)
    from_lower = from_behind(tail_layers, "blocks", 1)
    from_upper = from_behind(minus_side[:4], "blocks", -1)
    table_minus = jnp.concatenate([from_lower, plus_side], axis=0)
    table_plus = jnp.concatenate([minus_side, from_upper], axis=0)
    strides = jnp.array([1, 2, 4], jnp.int32)
    lower_ids = block_ids[:, None] - strides[None, :]
    upper_octant_index = block_ids[:, None] + strides[None, :]
    end_block = first_block + live_count
    rows_minus = jnp.clip(lower_ids - first_block + 4, 0, slot_count + 3)
    rows_plus = jnp.clip(
        jnp.where(
            upper_octant_index < end_block,
            upper_octant_index - first_block,
            slot_count + upper_octant_index - end_block,
        ),
        0,
        slot_count + 3,
    )
    columns = jnp.arange(3, dtype=jnp.int32)[None, :]
    got_minus = table_minus[rows_minus, columns]
    got_plus = table_plus[rows_plus, columns]
    parity_x = block_ids % 2
    parity_y = block_ids // 2 % 2
    keep_minus = jnp.stack([parity_x == 1, parity_y == 1, block_ids >= 4], axis=1)
    keep_plus = jnp.stack([parity_x == 0, parity_y == 0, block_ids + 4 < total_blocks], axis=1)
    zero_value = jnp.zeros((), layer_table.dtype)
    got_minus = jnp.where(keep_minus[:, :, None, None], got_minus, zero_value)
    got_plus = jnp.where(keep_plus[:, :, None, None], got_plus, zero_value)
    merged = jnp.stack([got_minus, got_plus], axis=2)
    return merged.reshape(layer_table.shape)


def coarse_halo(layer_table, coarse_ids, coarse_first, coarse_count, coarse_total):
    slot_count = layer_table.shape[0]
    top_layers = layer_table[:, 5]
    bottom_layers = layer_table[:, 4]
    last_top = lax.dynamic_index_in_dim(top_layers, coarse_count - 1, 0, keepdims=False)
    from_lower = from_behind(last_top, "blocks", 1)
    from_upper = from_behind(bottom_layers[0], "blocks", -1)
    table_minus = jnp.concatenate([from_lower[None], top_layers], axis=0)
    table_plus = jnp.concatenate([bottom_layers, from_upper[None]], axis=0)
    rows_minus = jnp.clip(coarse_ids - coarse_first, 0, slot_count)
    rows_plus = jnp.clip(
        jnp.where(
            coarse_ids + 1 < coarse_first + coarse_count, coarse_ids + 1 - coarse_first, slot_count
        ),
        0,
        slot_count,
    )
    zero_value = jnp.zeros((), layer_table.dtype)
    below_layer = jnp.where((coarse_ids >= 1)[:, None, None], table_minus[rows_minus], zero_value)
    above_layer = jnp.where(
        (coarse_ids + 1 < coarse_total)[:, None, None], table_plus[rows_plus], zero_value
    )
    flat_zero = jnp.zeros_like(below_layer)
    return jnp.stack([flat_zero, flat_zero, flat_zero, flat_zero, below_layer, above_layer], axis=1)


def apply_blocks(matrix, block_cubes, halo_table):

    def one_block(operands):
        return jnp.dot(
            matrix, block_views(operands[0], operands[1]), preferred_element_type=jnp.float32
        )

    return lax.map(one_block, (block_cubes, halo_table))


def weight_block(operands):
    tap_views = block_views(operands[0], operands[1])
    return lax.dot_general(
        operands[2], tap_views, (((1,), (1,)), ((), ())), preferred_element_type=jnp.float32
    )


def restrict_blocks(hidden, half_edge):
    count, width = (hidden.shape[0], hidden.shape[1])
    shaped = hidden.reshape(count, width, half_edge, 2, half_edge, 2, half_edge, 2)
    return (
        (jnp.sum(shaped, axis=(3, 5, 7), dtype=jnp.float32) * 0.125)
        .astype(jnp.bfloat16)
        .reshape(count, width, half_edge**3)
    )


def sum_over_blocks(parts):
    flat = jnp.concatenate([part.reshape(-1) for part in parts])
    summed = butterfly_sum(flat, "blocks")
    pieces = []
    offset = 0
    for part in parts:
        pieces.append(summed[offset : offset + part.size].reshape(part.shape))
        offset += part.size
    return tuple(pieces)


def chan_rows(payload):
    size = lax.axis_size("chan")
    got = [payload] + [
        lax.ppermute(payload, "chan", [(j, (j + k) % size) for j in range(size)])
        for k in range(1, size)
    ]
    return jnp.stack(got)


def input_order(weight):
    size = lax.axis_size("chan")
    me = lax.axis_index("chan")
    order = (me - jnp.arange(size, dtype=jnp.int32)) % size
    taps, rows, width = weight.shape
    shaped = weight.reshape(taps, rows, size, width // size)
    return jnp.take(shaped, order, axis=2).reshape(taps, rows, width)


def local(
    fine_input, block_counts, fine_weight, fine_bias, coarse_weight, coarse_bias, coarse_cotangent
):
    slot_count, group_size, cell_count = fine_input.shape
    coarse_slots = coarse_cotangent.shape[0]
    channels = fine_weight.shape[2]
    size = lax.axis_size("chan")
    half_edge = EDGE // 2
    octant_cells = half_edge**3
    pair_index = jnp.array(TAP_PAIRS, jnp.int32)
    device = lax.axis_index("blocks")
    starts = jnp.cumsum(block_counts) - block_counts
    first_block = starts[device]
    live_count = block_counts[device]
    end_block = first_block + live_count
    total_blocks = jnp.sum(block_counts)
    coarse_total = total_blocks // 8
    coarse_first = (first_block + 7) // 8
    coarse_count = (end_block + 7) // 8 - coarse_first
    block_ids = first_block + jnp.arange(slot_count, dtype=jnp.int32)
    coarse_ids = coarse_first + jnp.arange(coarse_slots, dtype=jnp.int32)
    live_mask = (jnp.arange(slot_count) < live_count)[:, None, None]
    coarse_live = (jnp.arange(coarse_slots) < coarse_count)[:, None, None]

    pieces = (fine_input, coarse_cotangent, fine_weight, coarse_weight)
    rows = chan_rows(jnp.concatenate([piece.reshape(-1) for piece in pieces]))
    bias_rows = chan_rows(jnp.concatenate([fine_bias, coarse_bias]))
    gathered = []
    offset = 0
    for piece, axis in zip(pieces, (1, 1, 1, 1)):
        block = rows[:, offset : offset + piece.size].reshape((size,) + piece.shape)
        offset += piece.size
        block = jnp.moveaxis(block, 0, axis)
        gathered.append(
            block.reshape(piece.shape[:axis] + (size * piece.shape[axis],) + piece.shape[axis + 1 :])
        )
    full_input, full_cotangent, fine_w, coarse_w = gathered
    fine_w = input_order(fine_w)
    coarse_w = input_order(coarse_w)
    fine_b = bias_rows[:, :group_size].reshape(-1)
    coarse_b = bias_rows[:, group_size:].reshape(-1)

    fine_cubes = full_input.reshape(slot_count, channels, EDGE, EDGE, EDGE)
    input_halos = fine_halo(
        jax.vmap(block_layers)(fine_cubes), block_ids, first_block, live_count, total_blocks
    )
    forward_fine = fine_w.transpose(1, 0, 2).reshape(channels, 7 * channels)
    fine_views = flat_views(full_input, input_halos)
    pre_fine = (
        jnp.einsum("ln,bnp->blp", forward_fine, fine_views, preferred_element_type=jnp.float32)
        + fine_b[None, :, None]
    )
    octants = restrict_blocks(jax.nn.silu(pre_fine).astype(jnp.bfloat16), half_edge)
    upper_octants = from_behind(octants[:7], "blocks", -1)
    octant_table = jnp.concatenate([octants, upper_octants], axis=0)
    children = coarse_ids[:, None] * 8 + jnp.arange(8, dtype=jnp.int32)[None, :]
    child_rows = jnp.clip(
        jnp.where(children < end_block, children - first_block, slot_count + children - end_block),
        0,
        slot_count + 6,
    )
    gathered_octants = octant_table[child_rows]
    coarse_full = (
        gathered_octants.reshape(coarse_slots, 2, 2, 2, channels, half_edge, half_edge, half_edge)
        .transpose(0, 4, 1, 5, 2, 6, 3, 7)
        .reshape(coarse_slots, channels, cell_count)
    )
    coarse_full = jnp.where(coarse_live, coarse_full, jnp.zeros((), jnp.bfloat16))
    coarse_cubes = coarse_full.reshape(coarse_slots, channels, EDGE, EDGE, EDGE)
    coarse_in_halos = coarse_halo(
        jax.vmap(block_layers)(coarse_cubes), coarse_ids, coarse_first, coarse_count, coarse_total
    )
    coarser_level_views = flat_views(coarse_full, coarse_in_halos)
    forward_coarser_level = coarse_w.transpose(1, 0, 2).reshape(channels, 7 * channels)
    pre_coarse = (
        jnp.einsum(
            "ln,enp->elp",
            forward_coarser_level,
            coarser_level_views,
            preferred_element_type=jnp.float32,
        )
        + coarse_b[None, :, None]
    )
    coarser_level_output = jnp.where(
        coarse_live, jax.nn.silu(pre_coarse[:, :group_size]), 0.0
    ).astype(jnp.bfloat16)
    coarser_level_delta = jnp.where(
        coarse_live, full_cotangent.astype(jnp.float32) * slope_of(pre_coarse), 0.0
    ).astype(jnp.bfloat16)
    own_coarse_delta = coarser_level_delta[:, :group_size]
    coarse_weight_grad = jnp.einsum(
        "zlc,znc->ln", own_coarse_delta, coarser_level_views, preferred_element_type=jnp.float32
    )
    coarse_weight_grad = coarse_weight_grad.reshape(group_size, 7, channels).transpose(1, 0, 2)
    coarse_bias_grad = jnp.sum(own_coarse_delta, axis=(0, 2), dtype=jnp.float32)
    delta_cubes = coarser_level_delta.reshape(coarse_slots, channels, EDGE, EDGE, EDGE)
    delta_halos = coarse_halo(
        jax.vmap(block_layers)(delta_cubes), coarse_ids, coarse_first, coarse_count, coarse_total
    )
    delta_window_views = flat_views(coarser_level_delta, delta_halos)
    backward_coarser_level = coarse_w[pair_index].transpose(2, 0, 1).reshape(channels, 7 * channels)
    coarse_back = jnp.einsum(
        "ur,mre->mue",
        backward_coarser_level,
        delta_window_views,
        preferred_element_type=jnp.float32,
    )
    coarse_back = jnp.where(coarse_live, coarse_back, 0.0).astype(jnp.bfloat16)
    coarse_octants = (
        coarse_back.reshape(coarse_slots, channels, 2, half_edge, 2, half_edge, 2, half_edge)
        .transpose(0, 2, 4, 6, 1, 3, 5, 7)
        .reshape(coarse_slots * 8, channels, octant_cells)
    )
    last_octants = lax.dynamic_slice_in_dim(coarse_octants, (coarse_count - 1) * 8 + 1, 7, 0)
    lower_octants = from_behind(last_octants, "blocks", 1)
    back_table = jnp.concatenate([coarse_octants, lower_octants], axis=0)
    parents = block_ids // 8
    octant_ids = block_ids % 8
    back_rows = jnp.clip(
        jnp.where(
            parents >= coarse_first,
            (parents - coarse_first) * 8 + octant_ids,
            coarse_slots * 8 + octant_ids - 1,
        ),
        0,
        coarse_slots * 8 + 6,
    )
    picked_rows = back_table[back_rows]
    picked = picked_rows.reshape(slot_count, channels, half_edge, 1, half_edge, 1, half_edge, 1)
    widened = jnp.broadcast_to(
        picked, (slot_count, channels, half_edge, 2, half_edge, 2, half_edge, 2)
    ).reshape(slot_count, channels, cell_count)
    fine_delta = jnp.where(
        live_mask, widened.astype(jnp.float32) * 0.125 * slope_of(pre_fine), 0.0
    ).astype(jnp.bfloat16)
    own_fine_delta = fine_delta[:, :group_size]
    fine_weight_grad = jnp.einsum(
        "blp,bnp->bln", own_fine_delta, fine_views, preferred_element_type=jnp.float32
    ).sum(axis=0)
    fine_weight_grad = fine_weight_grad.reshape(group_size, 7, channels).transpose(1, 0, 2)
    fine_bias_grad = jnp.sum(own_fine_delta, axis=(0, 2), dtype=jnp.float32)
    fine_delta_cubes = fine_delta.reshape(slot_count, channels, EDGE, EDGE, EDGE)
    fine_delta_halos = fine_halo(
        jax.vmap(block_layers)(fine_delta_cubes), block_ids, first_block, live_count, total_blocks
    )
    fine_delta_views = flat_views(fine_delta, fine_delta_halos)
    back_fine = fine_w[pair_index].transpose(2, 0, 1)[:group_size].reshape(group_size, 7 * channels)
    fine_back = jnp.einsum(
        "ur,bre->bue", back_fine, fine_delta_views, preferred_element_type=jnp.float32
    )
    fine_grad = jnp.where(live_mask, fine_back, 0.0).astype(jnp.bfloat16)
    fine_weight_grad, fine_bias_grad, coarse_weight_grad, coarse_bias_grad = sum_over_blocks(
        (fine_weight_grad, fine_bias_grad, coarse_weight_grad, coarse_bias_grad)
    )
    fine_weight_grad = natural_order(fine_weight_grad)
    coarse_weight_grad = natural_order(coarse_weight_grad)
    fine_norm = jnp.sqrt(total_blocks.astype(jnp.float32) * cell_count)
    coarse_norm = jnp.sqrt(coarse_total.astype(jnp.float32) * cell_count)
    return (
        coarser_level_output,
        fine_grad,
        fine_weight_grad / fine_norm,
        fine_bias_grad / fine_norm,
        coarse_weight_grad / coarse_norm,
        coarse_bias_grad / coarse_norm,
    )


def solution(mesh):
    placed = (
        P("blocks", "chan", None),
        P(),
        P(None, "chan", None),
        P("chan"),
        P(None, "chan", None),
        P("chan"),
        P("blocks", "chan", None),
    )
    return jax.shard_map(
        local,
        mesh=mesh,
        in_specs=placed,
        out_specs=(
            P("blocks", "chan", None),
            P("blocks", "chan", None),
            P(None, "chan", None),
            P("chan"),
            P(None, "chan", None),
            P("chan"),
        ),
        check_vma=False,
    )
```

```python
import jax
import jax.numpy as jnp
from jax import lax
from jax.sharding import PartitionSpec as P

EDGE = 8


TAP_PAIRS = (0, 2, 1, 4, 3, 6, 5)


def from_behind(block, axis, distance):
    devices = range(lax.axis_size(axis))
    route = [(i - distance, i) for i in devices if i - distance in devices]
    return lax.ppermute(block, axis, route)


def block_layers(block_cube):
    channels, edge_cells = (block_cube.shape[0], block_cube.shape[1])
    side_layers = [
        block_cube[:, :, :, 0],
        block_cube[:, :, :, -1],
        block_cube[:, :, 0, :],
        block_cube[:, :, -1, :],
        block_cube[:, 0],
        block_cube[:, -1],
    ]
    return jnp.stack(side_layers).reshape(6, channels, edge_cells * edge_cells)


def block_views(block_cube, halo_layers):
    channels, edge_cells = (block_cube.shape[0], block_cube.shape[1])
    sheets = halo_layers.reshape(6, channels, edge_cells, edge_cells)
    minus_x = jnp.concatenate([sheets[0][:, :, :, None], block_cube[:, :, :, :-1]], axis=3)
    plus_x = jnp.concatenate([block_cube[:, :, :, 1:], sheets[1][:, :, :, None]], axis=3)
    minus_y = jnp.concatenate([sheets[2][:, :, None, :], block_cube[:, :, :-1, :]], axis=2)
    plus_y = jnp.concatenate([block_cube[:, :, 1:, :], sheets[3][:, :, None, :]], axis=2)
    minus_z = jnp.concatenate([sheets[4][:, None], block_cube[:, :-1]], axis=1)
    plus_z = jnp.concatenate([block_cube[:, 1:], sheets[5][:, None]], axis=1)
    stacked = jnp.stack([block_cube, minus_x, plus_x, minus_y, plus_y, minus_z, plus_z])
    return stacked.reshape(7 * channels, edge_cells**3)


def flat_taps(cubes, halo_layers):
    count, channels, cells = cubes.shape
    edge = EDGE
    position = jnp.arange(cells, dtype=jnp.int32)
    x_pos = position % edge
    y_pos = position // edge % edge
    z_pos = position // (edge * edge)
    sheets = halo_layers.reshape(count, 6, channels, edge * edge)
    zeros = jnp.zeros((count, channels, edge * edge), cubes.dtype)

    def back(step):
        return jnp.concatenate([zeros[:, :, :step], cubes[:, :, : cells - step]], axis=2)

    def ahead(step):
        return jnp.concatenate([cubes[:, :, step:], zeros[:, :, :step]], axis=2)

    def yz_sheet(sheet):
        return jnp.repeat(sheet, edge, axis=2)

    def zx_sheet(sheet):
        shaped = sheet.reshape(count, channels, edge, 1, edge)
        return jnp.broadcast_to(shaped, (count, channels, edge, edge, edge)).reshape(
            count, channels, cells
        )

    def yx_sheet(sheet):
        return jnp.tile(sheet, (1, 1, edge))

    minus_x = jnp.where(x_pos == 0, yz_sheet(sheets[:, 0]), back(1))
    plus_x = jnp.where(x_pos == edge - 1, yz_sheet(sheets[:, 1]), ahead(1))
    minus_y = jnp.where(y_pos == 0, zx_sheet(sheets[:, 2]), back(edge))
    plus_y = jnp.where(y_pos == edge - 1, zx_sheet(sheets[:, 3]), ahead(edge))
    minus_z = jnp.where(z_pos == 0, yx_sheet(sheets[:, 4]), back(edge * edge))
    plus_z = jnp.where(z_pos == edge - 1, yx_sheet(sheets[:, 5]), ahead(edge * edge))
    return [cubes, minus_x, plus_x, minus_y, plus_y, minus_z, plus_z]


def flat_views(cubes, halo_layers):
    count, channels, cells = cubes.shape
    stacked = jnp.stack(flat_taps(cubes, halo_layers), axis=1)
    return stacked.reshape(count, 7 * channels, cells)


def chan_gather(value):
    size = lax.axis_size("chan")
    me = lax.axis_index("chan")
    got = [value] + [
        lax.ppermute(value, "chan", [(j, (j + k) % size) for j in range(size)])
        for k in range(1, size)
    ]
    return jnp.concatenate(got, axis=1)


def arrival_order(matrix):
    size = lax.axis_size("chan")
    me = lax.axis_index("chan")
    order = (me - jnp.arange(size, dtype=jnp.int32)) % size
    rows, width = matrix.shape
    shaped = matrix.reshape(rows, 7, size, width // (7 * size))
    return jnp.take(shaped, order, axis=2).reshape(rows, width)


def chan_scatter_sum(partial):
    size = lax.axis_size("chan")
    me = lax.axis_index("chan")
    width = partial.shape[1] // size
    pieces = partial.reshape((partial.shape[0], size, width) + partial.shape[2:])
    total = lax.dynamic_index_in_dim(pieces, me, 1, keepdims=False)
    for k in range(1, size):
        outgoing = lax.dynamic_index_in_dim(pieces, (me + k) % size, 1, keepdims=False)
        total = total + lax.ppermute(
            outgoing, "chan", [(j, (j + k) % size) for j in range(size)]
        )
    return total


def natural_order(grad):
    taps, rows, width = grad.shape
    return arrival_order(grad.transpose(1, 0, 2).reshape(rows, taps * width)).reshape(
        rows, taps, width
    ).transpose(1, 0, 2)


def butterfly_sum(value, axis):
    size = lax.axis_size(axis)
    me = lax.axis_index(axis)
    radix = 4
    stride = 1
    while stride * radix <= size and size % (stride * radix) == 0:
        digit = me // stride % radix
        got = [value]
        for k in range(1, radix):
            route = [
                (i, i - (i // stride % radix) * stride + ((i // stride + k) % radix) * stride)
                for i in range(size)
            ]
            got.append(lax.ppermute(value, axis, route))
        stacked = jnp.stack(got)
        ordered = [
            lax.dynamic_index_in_dim(stacked, (digit - m) % radix, 0, keepdims=False)
            for m in range(radix)
        ]
        value = ordered[0]
        for m in range(1, radix):
            value = value + ordered[m]
        stride *= radix
    distance = stride
    while distance < size:
        if size % (distance * 2):
            return lax.psum(value, axis)
        value = value + lax.ppermute(value, axis, [(i, i ^ distance) for i in range(size)])
        distance *= 2
    return value


def slope_of(pre_values):
    sigmoid_values = jax.nn.sigmoid(pre_values)
    return sigmoid_values * (1.0 + pre_values * (1.0 - sigmoid_values))


def fine_halo(layer_table, block_ids, first_block, live_count, total_blocks):
    slot_count = layer_table.shape[0]
    plus_side = layer_table[:, 1::2]
    minus_side = layer_table[:, 0::2]
    tail_layers = lax.dynamic_slice_in_dim(plus_side, live_count - 4, 4, 0)
    from_lower = from_behind(tail_layers, "blocks", 1)
    from_upper = from_behind(minus_side[:4], "blocks", -1)
    table_minus = jnp.concatenate([from_lower, plus_side], axis=0)
    table_plus = jnp.concatenate([minus_side, from_upper], axis=0)
    strides = jnp.array([1, 2, 4], jnp.int32)
    lower_ids = block_ids[:, None] - strides[None, :]
    upper_octant_index = block_ids[:, None] + strides[None, :]
    end_block = first_block + live_count
    rows_minus = jnp.clip(lower_ids - first_block + 4, 0, slot_count + 3)
    rows_plus = jnp.clip(
        jnp.where(
            upper_octant_index < end_block,
            upper_octant_index - first_block,
            slot_count + upper_octant_index - end_block,
        ),
        0,
        slot_count + 3,
    )
    columns = jnp.arange(3, dtype=jnp.int32)[None, :]
    got_minus = table_minus[rows_minus, columns]
    got_plus = table_plus[rows_plus, columns]
    parity_x = block_ids % 2
    parity_y = block_ids // 2 % 2
    keep_minus = jnp.stack([parity_x == 1, parity_y == 1, block_ids >= 4], axis=1)
    keep_plus = jnp.stack([parity_x == 0, parity_y == 0, block_ids + 4 < total_blocks], axis=1)
    zero_value = jnp.zeros((), layer_table.dtype)
    got_minus = jnp.where(keep_minus[:, :, None, None], got_minus, zero_value)
    got_plus = jnp.where(keep_plus[:, :, None, None], got_plus, zero_value)
    merged = jnp.stack([got_minus, got_plus], axis=2)
    return merged.reshape(layer_table.shape)


def coarse_halo(layer_table, coarse_ids, coarse_first, coarse_count, coarse_total):
    slot_count = layer_table.shape[0]
    top_layers = layer_table[:, 5]
    bottom_layers = layer_table[:, 4]
    last_top = lax.dynamic_index_in_dim(top_layers, coarse_count - 1, 0, keepdims=False)
    from_lower = from_behind(last_top, "blocks", 1)
    from_upper = from_behind(bottom_layers[0], "blocks", -1)
    table_minus = jnp.concatenate([from_lower[None], top_layers], axis=0)
    table_plus = jnp.concatenate([bottom_layers, from_upper[None]], axis=0)
    rows_minus = jnp.clip(coarse_ids - coarse_first, 0, slot_count)
    rows_plus = jnp.clip(
        jnp.where(
            coarse_ids + 1 < coarse_first + coarse_count, coarse_ids + 1 - coarse_first, slot_count
        ),
        0,
        slot_count,
    )
    zero_value = jnp.zeros((), layer_table.dtype)
    below_layer = jnp.where((coarse_ids >= 1)[:, None, None], table_minus[rows_minus], zero_value)
    above_layer = jnp.where(
        (coarse_ids + 1 < coarse_total)[:, None, None], table_plus[rows_plus], zero_value
    )
    flat_zero = jnp.zeros_like(below_layer)
    return jnp.stack([flat_zero, flat_zero, flat_zero, flat_zero, below_layer, above_layer], axis=1)


def apply_blocks(matrix, block_cubes, halo_table):

    def one_block(operands):
        return jnp.dot(
            matrix, block_views(operands[0], operands[1]), preferred_element_type=jnp.float32
        )

    return lax.map(one_block, (block_cubes, halo_table))


def weight_block(operands):
    tap_views = block_views(operands[0], operands[1])
    return lax.dot_general(
        operands[2], tap_views, (((1,), (1,)), ((), ())), preferred_element_type=jnp.float32
    )


def restrict_blocks(hidden, half_edge):
    count, width = (hidden.shape[0], hidden.shape[1])
    shaped = hidden.reshape(count, width, half_edge, 2, half_edge, 2, half_edge, 2)
    return (
        (jnp.sum(shaped, axis=(3, 5, 7), dtype=jnp.float32) * 0.125)
        .astype(jnp.bfloat16)
        .reshape(count, width, half_edge**3)
    )


def sum_over_blocks(parts):
    flat = jnp.concatenate([part.reshape(-1) for part in parts])
    summed = butterfly_sum(flat, "blocks")
    pieces = []
    offset = 0
    for part in parts:
        pieces.append(summed[offset : offset + part.size].reshape(part.shape))
        offset += part.size
    return tuple(pieces)


def local(
    fine_input, block_counts, fine_weight, fine_bias, coarse_weight, coarse_bias, coarse_cotangent
):
    slot_count, group_size, cell_count = fine_input.shape
    coarse_slots = coarse_cotangent.shape[0]
    channels = fine_weight.shape[2]
    half_edge = EDGE // 2
    octant_cells = half_edge**3
    pair_index = jnp.array(TAP_PAIRS, jnp.int32)
    device = lax.axis_index("blocks")
    starts = jnp.cumsum(block_counts) - block_counts
    first_block = starts[device]
    live_count = block_counts[device]
    end_block = first_block + live_count
    total_blocks = jnp.sum(block_counts)
    coarse_total = total_blocks // 8
    coarse_first = (first_block + 7) // 8
    coarse_count = (end_block + 7) // 8 - coarse_first
    block_ids = first_block + jnp.arange(slot_count, dtype=jnp.int32)
    coarse_ids = coarse_first + jnp.arange(coarse_slots, dtype=jnp.int32)
    live_mask = (jnp.arange(slot_count) < live_count)[:, None, None]
    coarse_live = (jnp.arange(coarse_slots) < coarse_count)[:, None, None]
    full_input = chan_gather(fine_input)
    fine_cubes = full_input.reshape(slot_count, channels, EDGE, EDGE, EDGE)
    input_halos = fine_halo(
        jax.vmap(block_layers)(fine_cubes), block_ids, first_block, live_count, total_blocks
    )
    forward_fine = arrival_order(fine_weight.transpose(1, 0, 2).reshape(group_size, 7 * channels))
    fine_taps = flat_taps(full_input, input_halos)
    tap_weights = forward_fine.reshape(group_size, 7, channels)
    pre_fine = fine_bias[None, :, None]
    for tap in range(7):
        pre_fine = pre_fine + jnp.einsum(
            "lc,bcp->blp", tap_weights[:, tap], fine_taps[tap], preferred_element_type=jnp.float32
        )
    octants = restrict_blocks(jax.nn.silu(pre_fine).astype(jnp.bfloat16), half_edge)
    upper_octants = from_behind(octants[:7], "blocks", -1)
    octant_table = jnp.concatenate([octants, upper_octants], axis=0)
    children = coarse_ids[:, None] * 8 + jnp.arange(8, dtype=jnp.int32)[None, :]
    child_rows = jnp.clip(
        jnp.where(children < end_block, children - first_block, slot_count + children - end_block),
        0,
        slot_count + 6,
    )
    gathered = octant_table[child_rows]
    coarse_local = (
        gathered.reshape(coarse_slots, 2, 2, 2, group_size, half_edge, half_edge, half_edge)
        .transpose(0, 4, 1, 5, 2, 6, 3, 7)
        .reshape(coarse_slots, group_size, cell_count)
    )
    coarse_local = jnp.where(coarse_live, coarse_local, jnp.zeros((), jnp.bfloat16))
    coarse_full = chan_gather(coarse_local)
    coarse_cubes = coarse_full.reshape(coarse_slots, channels, EDGE, EDGE, EDGE)
    coarse_in_halos = coarse_halo(
        jax.vmap(block_layers)(coarse_cubes), coarse_ids, coarse_first, coarse_count, coarse_total
    )
    coarser_level_views = flat_views(coarse_full, coarse_in_halos)
    forward_coarser_level = arrival_order(
        coarse_weight.transpose(1, 0, 2).reshape(group_size, 7 * channels)
    )
    pre_coarse = (
        jnp.einsum(
            "ln,enp->elp",
            forward_coarser_level,
            coarser_level_views,
            preferred_element_type=jnp.float32,
        )
        + coarse_bias[None, :, None]
    )
    coarser_level_output = jnp.where(coarse_live, jax.nn.silu(pre_coarse), 0.0).astype(jnp.bfloat16)
    coarser_level_delta = jnp.where(
        coarse_live, coarse_cotangent.astype(jnp.float32) * slope_of(pre_coarse), 0.0
    ).astype(jnp.bfloat16)
    coarse_weight_grad = jnp.einsum(
        "zlc,znc->ln", coarser_level_delta, coarser_level_views, preferred_element_type=jnp.float32
    )
    coarse_weight_grad = coarse_weight_grad.reshape(group_size, 7, channels).transpose(1, 0, 2)
    coarse_bias_grad = jnp.sum(coarser_level_delta, axis=(0, 2), dtype=jnp.float32)
    delta_cubes = coarser_level_delta.reshape(coarse_slots, group_size, EDGE, EDGE, EDGE)
    delta_halos = coarse_halo(
        jax.vmap(block_layers)(delta_cubes), coarse_ids, coarse_first, coarse_count, coarse_total
    )
    delta_window_views = flat_views(coarser_level_delta, delta_halos)
    backward_coarser_level = (
        coarse_weight[pair_index].transpose(2, 0, 1).reshape(channels, 7 * group_size)
    )
    partial_sums = jnp.einsum(
        "ur,mre->mue",
        backward_coarser_level,
        delta_window_views,
        preferred_element_type=jnp.float32,
    )
    coarse_back = chan_scatter_sum(partial_sums)
    coarse_back = jnp.where(coarse_live, coarse_back, 0.0).astype(jnp.bfloat16)
    coarse_octants = (
        coarse_back.reshape(coarse_slots, group_size, 2, half_edge, 2, half_edge, 2, half_edge)
        .transpose(0, 2, 4, 6, 1, 3, 5, 7)
        .reshape(coarse_slots * 8, group_size, octant_cells)
    )
    last_octants = lax.dynamic_slice_in_dim(coarse_octants, (coarse_count - 1) * 8 + 1, 7, 0)
    lower_octants = from_behind(last_octants, "blocks", 1)
    back_table = jnp.concatenate([coarse_octants, lower_octants], axis=0)
    parents = block_ids // 8
    octant_ids = block_ids % 8
    back_rows = jnp.clip(
        jnp.where(
            parents >= coarse_first,
            (parents - coarse_first) * 8 + octant_ids,
            coarse_slots * 8 + octant_ids - 1,
        ),
        0,
        coarse_slots * 8 + 6,
    )
    picked_rows = back_table[back_rows]
    picked = picked_rows.reshape(slot_count, group_size, half_edge, 1, half_edge, 1, half_edge, 1)
    widened = jnp.broadcast_to(
        picked, (slot_count, group_size, half_edge, 2, half_edge, 2, half_edge, 2)
    ).reshape(slot_count, group_size, cell_count)
    fine_delta = jnp.where(
        live_mask, widened.astype(jnp.float32) * 0.125 * slope_of(pre_fine), 0.0
    ).astype(jnp.bfloat16)
    fine_weight_grad = jnp.stack(
        [
            jnp.einsum("blp,bcp->blc", fine_delta, tap_view, preferred_element_type=jnp.float32).sum(
                axis=0
            )
            for tap_view in fine_taps
        ],
        axis=1,
    ).reshape(group_size, 7 * channels)
    fine_weight_grad = fine_weight_grad.reshape(group_size, 7, channels).transpose(1, 0, 2)
    fine_bias_grad = jnp.sum(fine_delta, axis=(0, 2), dtype=jnp.float32)
    fine_delta_cubes = fine_delta.reshape(slot_count, group_size, EDGE, EDGE, EDGE)
    fine_delta_halos = fine_halo(
        jax.vmap(block_layers)(fine_delta_cubes), block_ids, first_block, live_count, total_blocks
    )
    back_fine = fine_weight[pair_index].transpose(2, 0, 1).reshape(channels, 7 * group_size)
    fine_delta_views = flat_views(fine_delta, fine_delta_halos)
    fine_partial = jnp.einsum(
        "ur,bre->bue", back_fine, fine_delta_views, preferred_element_type=jnp.float32
    )
    fine_back = chan_scatter_sum(fine_partial)
    fine_grad = jnp.where(live_mask, fine_back, 0.0).astype(jnp.bfloat16)
    fine_weight_grad, fine_bias_grad, coarse_weight_grad, coarse_bias_grad = sum_over_blocks(
        (fine_weight_grad, fine_bias_grad, coarse_weight_grad, coarse_bias_grad)
    )
    fine_weight_grad = natural_order(fine_weight_grad)
    coarse_weight_grad = natural_order(coarse_weight_grad)
    fine_norm = jnp.sqrt(total_blocks.astype(jnp.float32) * cell_count)
    coarse_norm = jnp.sqrt(coarse_total.astype(jnp.float32) * cell_count)
    return (
        coarser_level_output,
        fine_grad,
        fine_weight_grad / fine_norm,
        fine_bias_grad / fine_norm,
        coarse_weight_grad / coarse_norm,
        coarse_bias_grad / coarse_norm,
    )


def solution(mesh):
    placed = (
        P("blocks", "chan", None),
        P(),
        P(None, "chan", None),
        P("chan"),
        P(None, "chan", None),
        P("chan"),
        P("blocks", "chan", None),
    )
    return jax.shard_map(
        local,
        mesh=mesh,
        in_specs=placed,
        out_specs=(
            P("blocks", "chan", None),
            P("blocks", "chan", None),
            P(None, "chan", None),
            P("chan"),
            P(None, "chan", None),
            P("chan"),
        ),
        check_vma=False,
    )
```

```python
import jax
import jax.numpy as jnp
from jax import lax
from jax.sharding import PartitionSpec as P

EDGE = 8


TAP_PAIRS = (0, 2, 1, 4, 3, 6, 5)


def from_behind(block, axis, distance):
    devices = range(lax.axis_size(axis))
    route = [(i - distance, i) for i in devices if i - distance in devices]
    return lax.ppermute(block, axis, route)


def block_layers(block_cube):
    channels, edge_cells = (block_cube.shape[0], block_cube.shape[1])
    side_layers = [
        block_cube[:, :, :, 0],
        block_cube[:, :, :, -1],
        block_cube[:, :, 0, :],
        block_cube[:, :, -1, :],
        block_cube[:, 0],
        block_cube[:, -1],
    ]
    return jnp.stack(side_layers).reshape(6, channels, edge_cells * edge_cells)


def block_views(block_cube, halo_layers):
    channels, edge_cells = (block_cube.shape[0], block_cube.shape[1])
    sheets = halo_layers.reshape(6, channels, edge_cells, edge_cells)
    minus_x = jnp.concatenate([sheets[0][:, :, :, None], block_cube[:, :, :, :-1]], axis=3)
    plus_x = jnp.concatenate([block_cube[:, :, :, 1:], sheets[1][:, :, :, None]], axis=3)
    minus_y = jnp.concatenate([sheets[2][:, :, None, :], block_cube[:, :, :-1, :]], axis=2)
    plus_y = jnp.concatenate([block_cube[:, :, 1:, :], sheets[3][:, :, None, :]], axis=2)
    minus_z = jnp.concatenate([sheets[4][:, None], block_cube[:, :-1]], axis=1)
    plus_z = jnp.concatenate([block_cube[:, 1:], sheets[5][:, None]], axis=1)
    stacked = jnp.stack([block_cube, minus_x, plus_x, minus_y, plus_y, minus_z, plus_z])
    return stacked.reshape(7 * channels, edge_cells**3)


def flat_views(cubes, halo_layers):
    count, channels, cells = cubes.shape
    edge = EDGE
    position = jnp.arange(cells, dtype=jnp.int32)
    x_pos = position % edge
    y_pos = position // edge % edge
    z_pos = position // (edge * edge)
    sheets = halo_layers.reshape(count, 6, channels, edge * edge)
    zeros = jnp.zeros((count, channels, edge * edge), cubes.dtype)

    def back(step):
        return jnp.concatenate([zeros[:, :, :step], cubes[:, :, : cells - step]], axis=2)

    def ahead(step):
        return jnp.concatenate([cubes[:, :, step:], zeros[:, :, :step]], axis=2)

    def yz_sheet(sheet):
        return jnp.repeat(sheet, edge, axis=2)

    def zx_sheet(sheet):
        shaped = sheet.reshape(count, channels, edge, 1, edge)
        return jnp.broadcast_to(shaped, (count, channels, edge, edge, edge)).reshape(
            count, channels, cells
        )

    def yx_sheet(sheet):
        return jnp.tile(sheet, (1, 1, edge))

    minus_x = jnp.where(x_pos == 0, yz_sheet(sheets[:, 0]), back(1))
    plus_x = jnp.where(x_pos == edge - 1, yz_sheet(sheets[:, 1]), ahead(1))
    minus_y = jnp.where(y_pos == 0, zx_sheet(sheets[:, 2]), back(edge))
    plus_y = jnp.where(y_pos == edge - 1, zx_sheet(sheets[:, 3]), ahead(edge))
    minus_z = jnp.where(z_pos == 0, yx_sheet(sheets[:, 4]), back(edge * edge))
    plus_z = jnp.where(z_pos == edge - 1, yx_sheet(sheets[:, 5]), ahead(edge * edge))
    stacked = jnp.stack([cubes, minus_x, plus_x, minus_y, plus_y, minus_z, plus_z], axis=1)
    return stacked.reshape(count, 7 * channels, cells)


def chan_gather(value):
    size = lax.axis_size("chan")
    me = lax.axis_index("chan")
    got = [value] + [
        lax.ppermute(value, "chan", [(j, (j + k) % size) for j in range(size)])
        for k in range(1, size)
    ]
    return jnp.concatenate(got, axis=1)


def arrival_order(matrix):
    size = lax.axis_size("chan")
    me = lax.axis_index("chan")
    order = (me - jnp.arange(size, dtype=jnp.int32)) % size
    rows, width = matrix.shape
    shaped = matrix.reshape(rows, 7, size, width // (7 * size))
    return jnp.take(shaped, order, axis=2).reshape(rows, width)


def chan_scatter_sum(partial, wire=None):
    size = lax.axis_size("chan")
    me = lax.axis_index("chan")
    width = partial.shape[1] // size
    pieces = partial.reshape((partial.shape[0], size, width) + partial.shape[2:])
    total = lax.dynamic_index_in_dim(pieces, me, 1, keepdims=False)
    for k in range(1, size):
        outgoing = lax.dynamic_index_in_dim(pieces, (me + k) % size, 1, keepdims=False)
        if wire is not None:
            outgoing = outgoing.astype(wire)
        total = total + lax.ppermute(
            outgoing, "chan", [(j, (j + k) % size) for j in range(size)]
        ).astype(total.dtype)
    return total


def natural_order(grad):
    taps, rows, width = grad.shape
    return arrival_order(grad.transpose(1, 0, 2).reshape(rows, taps * width)).reshape(
        rows, taps, width
    ).transpose(1, 0, 2)


def butterfly_sum(value, axis):
    size = lax.axis_size(axis)
    me = lax.axis_index(axis)
    radix = 4
    stride = 1
    while stride * radix <= size and size % (stride * radix) == 0:
        digit = me // stride % radix
        got = [value]
        for k in range(1, radix):
            route = [
                (i, i - (i // stride % radix) * stride + ((i // stride + k) % radix) * stride)
                for i in range(size)
            ]
            got.append(lax.ppermute(value, axis, route))
        stacked = jnp.stack(got)
        ordered = [
            lax.dynamic_index_in_dim(stacked, (digit - m) % radix, 0, keepdims=False)
            for m in range(radix)
        ]
        value = ordered[0]
        for m in range(1, radix):
            value = value + ordered[m]
        stride *= radix
    distance = stride
    while distance < size:
        if size % (distance * 2):
            return lax.psum(value, axis)
        value = value + lax.ppermute(value, axis, [(i, i ^ distance) for i in range(size)])
        distance *= 2
    return value


def slope_of(pre_values):
    sigmoid_values = jax.nn.sigmoid(pre_values)
    return sigmoid_values * (1.0 + pre_values * (1.0 - sigmoid_values))


def fine_halo(layer_table, block_ids, first_block, live_count, total_blocks):
    slot_count = layer_table.shape[0]
    plus_side = layer_table[:, 1::2]
    minus_side = layer_table[:, 0::2]
    tail_layers = lax.dynamic_slice_in_dim(plus_side, live_count - 4, 4, 0)
    from_lower = from_behind(tail_layers, "blocks", 1)
    from_upper = from_behind(minus_side[:4], "blocks", -1)
    table_minus = jnp.concatenate([from_lower, plus_side], axis=0)
    table_plus = jnp.concatenate([minus_side, from_upper], axis=0)
    strides = jnp.array([1, 2, 4], jnp.int32)
    lower_ids = block_ids[:, None] - strides[None, :]
    upper_octant_index = block_ids[:, None] + strides[None, :]
    end_block = first_block + live_count
    rows_minus = jnp.clip(lower_ids - first_block + 4, 0, slot_count + 3)
    rows_plus = jnp.clip(
        jnp.where(
            upper_octant_index < end_block,
            upper_octant_index - first_block,
            slot_count + upper_octant_index - end_block,
        ),
        0,
        slot_count + 3,
    )
    columns = jnp.arange(3, dtype=jnp.int32)[None, :]
    got_minus = table_minus[rows_minus, columns]
    got_plus = table_plus[rows_plus, columns]
    parity_x = block_ids % 2
    parity_y = block_ids // 2 % 2
    keep_minus = jnp.stack([parity_x == 1, parity_y == 1, block_ids >= 4], axis=1)
    keep_plus = jnp.stack([parity_x == 0, parity_y == 0, block_ids + 4 < total_blocks], axis=1)
    zero_value = jnp.zeros((), layer_table.dtype)
    got_minus = jnp.where(keep_minus[:, :, None, None], got_minus, zero_value)
    got_plus = jnp.where(keep_plus[:, :, None, None], got_plus, zero_value)
    merged = jnp.stack([got_minus, got_plus], axis=2)
    return merged.reshape(layer_table.shape)


def coarse_halo(layer_table, coarse_ids, coarse_first, coarse_count, coarse_total):
    slot_count = layer_table.shape[0]
    top_layers = layer_table[:, 5]
    bottom_layers = layer_table[:, 4]
    last_top = lax.dynamic_index_in_dim(top_layers, coarse_count - 1, 0, keepdims=False)
    from_lower = from_behind(last_top, "blocks", 1)
    from_upper = from_behind(bottom_layers[0], "blocks", -1)
    table_minus = jnp.concatenate([from_lower[None], top_layers], axis=0)
    table_plus = jnp.concatenate([bottom_layers, from_upper[None]], axis=0)
    rows_minus = jnp.clip(coarse_ids - coarse_first, 0, slot_count)
    rows_plus = jnp.clip(
        jnp.where(
            coarse_ids + 1 < coarse_first + coarse_count, coarse_ids + 1 - coarse_first, slot_count
        ),
        0,
        slot_count,
    )
    zero_value = jnp.zeros((), layer_table.dtype)
    below_layer = jnp.where((coarse_ids >= 1)[:, None, None], table_minus[rows_minus], zero_value)
    above_layer = jnp.where(
        (coarse_ids + 1 < coarse_total)[:, None, None], table_plus[rows_plus], zero_value
    )
    flat_zero = jnp.zeros_like(below_layer)
    return jnp.stack([flat_zero, flat_zero, flat_zero, flat_zero, below_layer, above_layer], axis=1)


def apply_blocks(matrix, block_cubes, halo_table):

    def one_block(operands):
        return jnp.dot(
            matrix, block_views(operands[0], operands[1]), preferred_element_type=jnp.float32
        )

    return lax.map(one_block, (block_cubes, halo_table))


def weight_block(operands):
    tap_views = block_views(operands[0], operands[1])
    return lax.dot_general(
        operands[2], tap_views, (((1,), (1,)), ((), ())), preferred_element_type=jnp.float32
    )


def restrict_blocks(hidden, half_edge):
    count, width = (hidden.shape[0], hidden.shape[1])
    shaped = hidden.reshape(count, width, half_edge, 2, half_edge, 2, half_edge, 2)
    return (
        (jnp.sum(shaped, axis=(3, 5, 7), dtype=jnp.float32) * 0.125)
        .astype(jnp.bfloat16)
        .reshape(count, width, half_edge**3)
    )


def sum_over_blocks(parts):
    flat = jnp.concatenate([part.reshape(-1) for part in parts])
    summed = butterfly_sum(flat, "blocks")
    pieces = []
    offset = 0
    for part in parts:
        pieces.append(summed[offset : offset + part.size].reshape(part.shape))
        offset += part.size
    return tuple(pieces)


def local(
    fine_input, block_counts, fine_weight, fine_bias, coarse_weight, coarse_bias, coarse_cotangent
):
    slot_count, group_size, cell_count = fine_input.shape
    coarse_slots = coarse_cotangent.shape[0]
    channels = fine_weight.shape[2]
    half_edge = EDGE // 2
    octant_cells = half_edge**3
    pair_index = jnp.array(TAP_PAIRS, jnp.int32)
    device = lax.axis_index("blocks")
    starts = jnp.cumsum(block_counts) - block_counts
    first_block = starts[device]
    live_count = block_counts[device]
    end_block = first_block + live_count
    total_blocks = jnp.sum(block_counts)
    coarse_total = total_blocks // 8
    coarse_first = (first_block + 7) // 8
    coarse_count = (end_block + 7) // 8 - coarse_first
    block_ids = first_block + jnp.arange(slot_count, dtype=jnp.int32)
    coarse_ids = coarse_first + jnp.arange(coarse_slots, dtype=jnp.int32)
    live_mask = (jnp.arange(slot_count) < live_count)[:, None, None]
    coarse_live = (jnp.arange(coarse_slots) < coarse_count)[:, None, None]
    full_input = chan_gather(fine_input)
    fine_cubes = full_input.reshape(slot_count, channels, EDGE, EDGE, EDGE)
    input_halos = fine_halo(
        jax.vmap(block_layers)(fine_cubes), block_ids, first_block, live_count, total_blocks
    )
    forward_fine = arrival_order(fine_weight.transpose(1, 0, 2).reshape(group_size, 7 * channels))
    fine_views = flat_views(full_input, input_halos)
    pre_fine = (
        jnp.einsum("ln,bnp->blp", forward_fine, fine_views, preferred_element_type=jnp.float32)
        + fine_bias[None, :, None]
    )
    octants = restrict_blocks(jax.nn.silu(pre_fine).astype(jnp.bfloat16), half_edge)
    upper_octants = from_behind(octants[:7], "blocks", -1)
    octant_table = jnp.concatenate([octants, upper_octants], axis=0)
    children = coarse_ids[:, None] * 8 + jnp.arange(8, dtype=jnp.int32)[None, :]
    child_rows = jnp.clip(
        jnp.where(children < end_block, children - first_block, slot_count + children - end_block),
        0,
        slot_count + 6,
    )
    gathered = octant_table[child_rows]
    coarse_local = (
        gathered.reshape(coarse_slots, 2, 2, 2, group_size, half_edge, half_edge, half_edge)
        .transpose(0, 4, 1, 5, 2, 6, 3, 7)
        .reshape(coarse_slots, group_size, cell_count)
    )
    coarse_local = jnp.where(coarse_live, coarse_local, jnp.zeros((), jnp.bfloat16))
    coarse_full = chan_gather(coarse_local)
    coarse_cubes = coarse_full.reshape(coarse_slots, channels, EDGE, EDGE, EDGE)
    coarse_in_halos = coarse_halo(
        jax.vmap(block_layers)(coarse_cubes), coarse_ids, coarse_first, coarse_count, coarse_total
    )
    coarser_level_views = flat_views(coarse_full, coarse_in_halos)
    forward_coarser_level = arrival_order(
        coarse_weight.transpose(1, 0, 2).reshape(group_size, 7 * channels)
    )
    pre_coarse = (
        jnp.einsum(
            "ln,enp->elp",
            forward_coarser_level,
            coarser_level_views,
            preferred_element_type=jnp.float32,
        )
        + coarse_bias[None, :, None]
    )
    coarser_level_output = jnp.where(coarse_live, jax.nn.silu(pre_coarse), 0.0).astype(jnp.bfloat16)
    coarser_level_delta = jnp.where(
        coarse_live, coarse_cotangent.astype(jnp.float32) * slope_of(pre_coarse), 0.0
    ).astype(jnp.bfloat16)
    coarse_weight_grad = jnp.einsum(
        "zlc,znc->ln", coarser_level_delta, coarser_level_views, preferred_element_type=jnp.float32
    )
    coarse_weight_grad = coarse_weight_grad.reshape(group_size, 7, channels).transpose(1, 0, 2)
    coarse_bias_grad = jnp.sum(coarser_level_delta, axis=(0, 2), dtype=jnp.float32)
    delta_cubes = coarser_level_delta.reshape(coarse_slots, group_size, EDGE, EDGE, EDGE)
    delta_halos = coarse_halo(
        jax.vmap(block_layers)(delta_cubes), coarse_ids, coarse_first, coarse_count, coarse_total
    )
    delta_window_views = flat_views(coarser_level_delta, delta_halos)
    backward_coarser_level = (
        coarse_weight[pair_index].transpose(2, 0, 1).reshape(channels, 7 * group_size)
    )
    partial_sums = jnp.einsum(
        "ur,mre->mue",
        backward_coarser_level,
        delta_window_views,
        preferred_element_type=jnp.float32,
    )
    coarse_back = chan_scatter_sum(partial_sums)
    coarse_back = jnp.where(coarse_live, coarse_back, 0.0).astype(jnp.bfloat16)
    coarse_octants = (
        coarse_back.reshape(coarse_slots, group_size, 2, half_edge, 2, half_edge, 2, half_edge)
        .transpose(0, 2, 4, 6, 1, 3, 5, 7)
        .reshape(coarse_slots * 8, group_size, octant_cells)
    )
    last_octants = lax.dynamic_slice_in_dim(coarse_octants, (coarse_count - 1) * 8 + 1, 7, 0)
    lower_octants = from_behind(last_octants, "blocks", 1)
    back_table = jnp.concatenate([coarse_octants, lower_octants], axis=0)
    parents = block_ids // 8
    octant_ids = block_ids % 8
    back_rows = jnp.clip(
        jnp.where(
            parents >= coarse_first,
            (parents - coarse_first) * 8 + octant_ids,
            coarse_slots * 8 + octant_ids - 1,
        ),
        0,
        coarse_slots * 8 + 6,
    )
    picked_rows = back_table[back_rows]
    picked = picked_rows.reshape(slot_count, group_size, half_edge, 1, half_edge, 1, half_edge, 1)
    widened = jnp.broadcast_to(
        picked, (slot_count, group_size, half_edge, 2, half_edge, 2, half_edge, 2)
    ).reshape(slot_count, group_size, cell_count)
    fine_delta = jnp.where(
        live_mask, widened.astype(jnp.float32) * 0.125 * slope_of(pre_fine), 0.0
    ).astype(jnp.bfloat16)
    fine_weight_grad = jnp.einsum(
        "blp,bnp->bln", fine_delta, fine_views, preferred_element_type=jnp.float32
    ).sum(axis=0)
    fine_weight_grad = fine_weight_grad.reshape(group_size, 7, channels).transpose(1, 0, 2)
    fine_bias_grad = jnp.sum(fine_delta, axis=(0, 2), dtype=jnp.float32)
    fine_delta_cubes = fine_delta.reshape(slot_count, group_size, EDGE, EDGE, EDGE)
    fine_delta_halos = fine_halo(
        jax.vmap(block_layers)(fine_delta_cubes), block_ids, first_block, live_count, total_blocks
    )
    back_fine = fine_weight[pair_index].transpose(2, 0, 1).reshape(channels, 7 * group_size)
    fine_delta_views = flat_views(fine_delta, fine_delta_halos)
    fine_partial = jnp.einsum(
        "ur,bre->bue", back_fine, fine_delta_views, preferred_element_type=jnp.float32
    )
    fine_back = chan_scatter_sum(fine_partial, jnp.bfloat16)
    fine_grad = jnp.where(live_mask, fine_back, 0.0).astype(jnp.bfloat16)
    fine_weight_grad, fine_bias_grad, coarse_weight_grad, coarse_bias_grad = sum_over_blocks(
        (fine_weight_grad, fine_bias_grad, coarse_weight_grad, coarse_bias_grad)
    )
    fine_weight_grad = natural_order(fine_weight_grad)
    coarse_weight_grad = natural_order(coarse_weight_grad)
    fine_norm = jnp.sqrt(total_blocks.astype(jnp.float32) * cell_count)
    coarse_norm = jnp.sqrt(coarse_total.astype(jnp.float32) * cell_count)
    return (
        coarser_level_output,
        fine_grad,
        fine_weight_grad / fine_norm,
        fine_bias_grad / fine_norm,
        coarse_weight_grad / coarse_norm,
        coarse_bias_grad / coarse_norm,
    )


def solution(mesh):
    placed = (
        P("blocks", "chan", None),
        P(),
        P(None, "chan", None),
        P("chan"),
        P(None, "chan", None),
        P("chan"),
        P("blocks", "chan", None),
    )
    return jax.shard_map(
        local,
        mesh=mesh,
        in_specs=placed,
        out_specs=(
            P("blocks", "chan", None),
            P("blocks", "chan", None),
            P(None, "chan", None),
            P("chan"),
            P(None, "chan", None),
            P("chan"),
        ),
        check_vma=False,
    )
```

```python
import jax
import jax.numpy as jnp
from jax import lax
from jax.sharding import PartitionSpec as P

EDGE = 8


TAP_PAIRS = (0, 2, 1, 4, 3, 6, 5)


def from_behind(block, axis, distance):
    devices = range(lax.axis_size(axis))
    route = [(i - distance, i) for i in devices if i - distance in devices]
    return lax.ppermute(block, axis, route)


def block_layers(block_cube):
    channels, edge_cells = (block_cube.shape[0], block_cube.shape[1])
    side_layers = [
        block_cube[:, :, :, 0],
        block_cube[:, :, :, -1],
        block_cube[:, :, 0, :],
        block_cube[:, :, -1, :],
        block_cube[:, 0],
        block_cube[:, -1],
    ]
    return jnp.stack(side_layers).reshape(6, channels, edge_cells * edge_cells)


def block_views(block_cube, halo_layers):
    channels, edge_cells = (block_cube.shape[0], block_cube.shape[1])
    sheets = halo_layers.reshape(6, channels, edge_cells, edge_cells)
    minus_x = jnp.concatenate([sheets[0][:, :, :, None], block_cube[:, :, :, :-1]], axis=3)
    plus_x = jnp.concatenate([block_cube[:, :, :, 1:], sheets[1][:, :, :, None]], axis=3)
    minus_y = jnp.concatenate([sheets[2][:, :, None, :], block_cube[:, :, :-1, :]], axis=2)
    plus_y = jnp.concatenate([block_cube[:, :, 1:, :], sheets[3][:, :, None, :]], axis=2)
    minus_z = jnp.concatenate([sheets[4][:, None], block_cube[:, :-1]], axis=1)
    plus_z = jnp.concatenate([block_cube[:, 1:], sheets[5][:, None]], axis=1)
    stacked = jnp.stack([block_cube, minus_x, plus_x, minus_y, plus_y, minus_z, plus_z])
    return stacked.reshape(7 * channels, edge_cells**3)


def flat_views(cubes, halo_layers):
    count, channels, cells = cubes.shape
    edge = EDGE
    position = jnp.arange(cells, dtype=jnp.int32)
    x_pos = position % edge
    y_pos = position // edge % edge
    z_pos = position // (edge * edge)
    sheets = halo_layers.reshape(count, 6, channels, edge * edge)
    zeros = jnp.zeros((count, channels, edge * edge), cubes.dtype)

    def back(step):
        return jnp.concatenate([zeros[:, :, :step], cubes[:, :, : cells - step]], axis=2)

    def ahead(step):
        return jnp.concatenate([cubes[:, :, step:], zeros[:, :, :step]], axis=2)

    def yz_sheet(sheet):
        return jnp.repeat(sheet, edge, axis=2)

    def zx_sheet(sheet):
        shaped = sheet.reshape(count, channels, edge, 1, edge)
        return jnp.broadcast_to(shaped, (count, channels, edge, edge, edge)).reshape(
            count, channels, cells
        )

    def yx_sheet(sheet):
        return jnp.tile(sheet, (1, 1, edge))

    minus_x = jnp.where(x_pos == 0, yz_sheet(sheets[:, 0]), back(1))
    plus_x = jnp.where(x_pos == edge - 1, yz_sheet(sheets[:, 1]), ahead(1))
    minus_y = jnp.where(y_pos == 0, zx_sheet(sheets[:, 2]), back(edge))
    plus_y = jnp.where(y_pos == edge - 1, zx_sheet(sheets[:, 3]), ahead(edge))
    minus_z = jnp.where(z_pos == 0, yx_sheet(sheets[:, 4]), back(edge * edge))
    plus_z = jnp.where(z_pos == edge - 1, yx_sheet(sheets[:, 5]), ahead(edge * edge))
    stacked = jnp.stack([cubes, minus_x, plus_x, minus_y, plus_y, minus_z, plus_z], axis=1)
    return stacked.reshape(count, 7 * channels, cells)


def chan_gather(value):
    size = lax.axis_size("chan")
    me = lax.axis_index("chan")
    got = [value] + [
        lax.ppermute(value, "chan", [(j, (j + k) % size) for j in range(size)])
        for k in range(1, size)
    ]
    return jnp.concatenate(got, axis=1)


def arrival_order(matrix):
    size = lax.axis_size("chan")
    me = lax.axis_index("chan")
    order = (me - jnp.arange(size, dtype=jnp.int32)) % size
    rows, width = matrix.shape
    shaped = matrix.reshape(rows, 7, size, width // (7 * size))
    return jnp.take(shaped, order, axis=2).reshape(rows, width)


def chan_scatter_sum(partial, wire=None):
    size = lax.axis_size("chan")
    me = lax.axis_index("chan")
    width = partial.shape[1] // size
    pieces = partial.reshape((partial.shape[0], size, width) + partial.shape[2:])
    total = lax.dynamic_index_in_dim(pieces, me, 1, keepdims=False)
    for k in range(1, size):
        outgoing = lax.dynamic_index_in_dim(pieces, (me + k) % size, 1, keepdims=False)
        if wire is not None:
            outgoing = outgoing.astype(wire)
        total = total + lax.ppermute(
            outgoing, "chan", [(j, (j + k) % size) for j in range(size)]
        ).astype(total.dtype)
    return total


def natural_order(grad):
    taps, rows, width = grad.shape
    return arrival_order(grad.transpose(1, 0, 2).reshape(rows, taps * width)).reshape(
        rows, taps, width
    ).transpose(1, 0, 2)


def butterfly_sum(value, axis):
    size = lax.axis_size(axis)
    me = lax.axis_index(axis)
    radix = 4
    stride = 1
    while stride * radix <= size and size % (stride * radix) == 0:
        digit = me // stride % radix
        got = [value]
        for k in range(1, radix):
            route = [
                (i, i - (i // stride % radix) * stride + ((i // stride + k) % radix) * stride)
                for i in range(size)
            ]
            got.append(lax.ppermute(value, axis, route))
        stacked = jnp.stack(got)
        ordered = [
            lax.dynamic_index_in_dim(stacked, (digit - m) % radix, 0, keepdims=False)
            for m in range(radix)
        ]
        value = ordered[0]
        for m in range(1, radix):
            value = value + ordered[m]
        stride *= radix
    distance = stride
    while distance < size:
        if size % (distance * 2):
            return lax.psum(value, axis)
        value = value + lax.ppermute(value, axis, [(i, i ^ distance) for i in range(size)])
        distance *= 2
    return value


def slope_of(pre_values):
    sigmoid_values = jax.nn.sigmoid(pre_values)
    return sigmoid_values * (1.0 + pre_values * (1.0 - sigmoid_values))


def fine_halo(layer_table, block_ids, first_block, live_count, total_blocks):
    slot_count = layer_table.shape[0]
    plus_side = layer_table[:, 1::2]
    minus_side = layer_table[:, 0::2]
    tail_layers = lax.dynamic_slice_in_dim(plus_side, live_count - 4, 4, 0)
    from_lower = from_behind(tail_layers, "blocks", 1)
    from_upper = from_behind(minus_side[:4], "blocks", -1)
    table_minus = jnp.concatenate([from_lower, plus_side], axis=0)
    table_plus = jnp.concatenate([minus_side, from_upper], axis=0)
    strides = jnp.array([1, 2, 4], jnp.int32)
    lower_ids = block_ids[:, None] - strides[None, :]
    upper_octant_index = block_ids[:, None] + strides[None, :]
    end_block = first_block + live_count
    rows_minus = jnp.clip(lower_ids - first_block + 4, 0, slot_count + 3)
    rows_plus = jnp.clip(
        jnp.where(
            upper_octant_index < end_block,
            upper_octant_index - first_block,
            slot_count + upper_octant_index - end_block,
        ),
        0,
        slot_count + 3,
    )
    columns = jnp.arange(3, dtype=jnp.int32)[None, :]
    got_minus = table_minus[rows_minus, columns]
    got_plus = table_plus[rows_plus, columns]
    parity_x = block_ids % 2
    parity_y = block_ids // 2 % 2
    keep_minus = jnp.stack([parity_x == 1, parity_y == 1, block_ids >= 4], axis=1)
    keep_plus = jnp.stack([parity_x == 0, parity_y == 0, block_ids + 4 < total_blocks], axis=1)
    zero_value = jnp.zeros((), layer_table.dtype)
    got_minus = jnp.where(keep_minus[:, :, None, None], got_minus, zero_value)
    got_plus = jnp.where(keep_plus[:, :, None, None], got_plus, zero_value)
    merged = jnp.stack([got_minus, got_plus], axis=2)
    return merged.reshape(layer_table.shape)


def coarse_halo(layer_table, coarse_ids, coarse_first, coarse_count, coarse_total):
    slot_count = layer_table.shape[0]
    top_layers = layer_table[:, 5]
    bottom_layers = layer_table[:, 4]
    last_top = lax.dynamic_index_in_dim(top_layers, coarse_count - 1, 0, keepdims=False)
    from_lower = from_behind(last_top, "blocks", 1)
    from_upper = from_behind(bottom_layers[0], "blocks", -1)
    table_minus = jnp.concatenate([from_lower[None], top_layers], axis=0)
    table_plus = jnp.concatenate([bottom_layers, from_upper[None]], axis=0)
    rows_minus = jnp.clip(coarse_ids - coarse_first, 0, slot_count)
    rows_plus = jnp.clip(
        jnp.where(
            coarse_ids + 1 < coarse_first + coarse_count, coarse_ids + 1 - coarse_first, slot_count
        ),
        0,
        slot_count,
    )
    zero_value = jnp.zeros((), layer_table.dtype)
    below_layer = jnp.where((coarse_ids >= 1)[:, None, None], table_minus[rows_minus], zero_value)
    above_layer = jnp.where(
        (coarse_ids + 1 < coarse_total)[:, None, None], table_plus[rows_plus], zero_value
    )
    flat_zero = jnp.zeros_like(below_layer)
    return jnp.stack([flat_zero, flat_zero, flat_zero, flat_zero, below_layer, above_layer], axis=1)


def apply_blocks(matrix, block_cubes, halo_table):

    def one_block(operands):
        return jnp.dot(
            matrix, block_views(operands[0], operands[1]), preferred_element_type=jnp.float32
        )

    return lax.map(one_block, (block_cubes, halo_table))


def weight_block(operands):
    tap_views = block_views(operands[0], operands[1])
    return lax.dot_general(
        operands[2], tap_views, (((1,), (1,)), ((), ())), preferred_element_type=jnp.float32
    )


def restrict_blocks(hidden, half_edge):
    count, width = (hidden.shape[0], hidden.shape[1])
    shaped = hidden.reshape(count, width, half_edge, 2, half_edge, 2, half_edge, 2)
    return (
        (jnp.sum(shaped, axis=(3, 5, 7), dtype=jnp.float32) * 0.125)
        .astype(jnp.bfloat16)
        .reshape(count, width, half_edge**3)
    )


def sum_over_blocks(parts):
    flat = jnp.concatenate([part.reshape(-1) for part in parts])
    summed = butterfly_sum(flat, "blocks")
    pieces = []
    offset = 0
    for part in parts:
        pieces.append(summed[offset : offset + part.size].reshape(part.shape))
        offset += part.size
    return tuple(pieces)


def local(
    fine_input, block_counts, fine_weight, fine_bias, coarse_weight, coarse_bias, coarse_cotangent
):
    slot_count, group_size, cell_count = fine_input.shape
    coarse_slots = coarse_cotangent.shape[0]
    channels = fine_weight.shape[2]
    half_edge = EDGE // 2
    octant_cells = half_edge**3
    pair_index = jnp.array(TAP_PAIRS, jnp.int32)
    device = lax.axis_index("blocks")
    starts = jnp.cumsum(block_counts) - block_counts
    first_block = starts[device]
    live_count = block_counts[device]
    end_block = first_block + live_count
    total_blocks = jnp.sum(block_counts)
    coarse_total = total_blocks // 8
    coarse_first = (first_block + 7) // 8
    coarse_count = (end_block + 7) // 8 - coarse_first
    block_ids = first_block + jnp.arange(slot_count, dtype=jnp.int32)
    coarse_ids = coarse_first + jnp.arange(coarse_slots, dtype=jnp.int32)
    live_mask = (jnp.arange(slot_count) < live_count)[:, None, None]
    coarse_live = (jnp.arange(coarse_slots) < coarse_count)[:, None, None]
    full_input = chan_gather(fine_input)
    fine_cubes = full_input.reshape(slot_count, channels, EDGE, EDGE, EDGE)
    input_halos = fine_halo(
        jax.vmap(block_layers)(fine_cubes), block_ids, first_block, live_count, total_blocks
    )
    forward_fine = arrival_order(fine_weight.transpose(1, 0, 2).reshape(group_size, 7 * channels))
    fine_views = flat_views(full_input, input_halos)
    pre_fine = (
        jnp.einsum("ln,bnp->blp", forward_fine, fine_views, preferred_element_type=jnp.float32)
        + fine_bias[None, :, None]
    )
    octants = restrict_blocks(jax.nn.silu(pre_fine).astype(jnp.bfloat16), half_edge)
    upper_octants = from_behind(octants[:7], "blocks", -1)
    octant_table = jnp.concatenate([octants, upper_octants], axis=0)
    children = coarse_ids[:, None] * 8 + jnp.arange(8, dtype=jnp.int32)[None, :]
    child_rows = jnp.clip(
        jnp.where(children < end_block, children - first_block, slot_count + children - end_block),
        0,
        slot_count + 6,
    )
    gathered = octant_table[child_rows]
    coarse_local = (
        gathered.reshape(coarse_slots, 2, 2, 2, group_size, half_edge, half_edge, half_edge)
        .transpose(0, 4, 1, 5, 2, 6, 3, 7)
        .reshape(coarse_slots, group_size, cell_count)
    )
    coarse_local = jnp.where(coarse_live, coarse_local, jnp.zeros((), jnp.bfloat16))
    coarse_full = chan_gather(coarse_local)
    coarse_cubes = coarse_full.reshape(coarse_slots, channels, EDGE, EDGE, EDGE)
    coarse_in_halos = coarse_halo(
        jax.vmap(block_layers)(coarse_cubes), coarse_ids, coarse_first, coarse_count, coarse_total
    )
    coarser_level_views = flat_views(coarse_full, coarse_in_halos)
    forward_coarser_level = arrival_order(
        coarse_weight.transpose(1, 0, 2).reshape(group_size, 7 * channels)
    )
    pre_coarse = (
        jnp.einsum(
            "ln,enp->elp",
            forward_coarser_level,
            coarser_level_views,
            preferred_element_type=jnp.float32,
        )
        + coarse_bias[None, :, None]
    )
    coarser_level_output = jnp.where(coarse_live, jax.nn.silu(pre_coarse), 0.0).astype(jnp.bfloat16)
    coarser_level_delta = jnp.where(
        coarse_live, coarse_cotangent.astype(jnp.float32) * slope_of(pre_coarse), 0.0
    ).astype(jnp.bfloat16)
    coarse_weight_grad = jnp.einsum(
        "zlc,znc->ln", coarser_level_delta, coarser_level_views, preferred_element_type=jnp.float32
    )
    coarse_weight_grad = coarse_weight_grad.reshape(group_size, 7, channels).transpose(1, 0, 2)
    coarse_bias_grad = jnp.sum(coarser_level_delta, axis=(0, 2), dtype=jnp.float32)
    delta_cubes = coarser_level_delta.reshape(coarse_slots, group_size, EDGE, EDGE, EDGE)
    delta_halos = coarse_halo(
        jax.vmap(block_layers)(delta_cubes), coarse_ids, coarse_first, coarse_count, coarse_total
    )
    delta_window_views = flat_views(coarser_level_delta, delta_halos)
    backward_coarser_level = (
        coarse_weight[pair_index].transpose(2, 0, 1).reshape(channels, 7 * group_size)
    )
    partial_sums = jnp.einsum(
        "ur,mre->mue",
        backward_coarser_level,
        delta_window_views,
        preferred_element_type=jnp.float32,
    )
    coarse_back = chan_scatter_sum(partial_sums, jnp.bfloat16)
    coarse_back = jnp.where(coarse_live, coarse_back, 0.0).astype(jnp.bfloat16)
    coarse_octants = (
        coarse_back.reshape(coarse_slots, group_size, 2, half_edge, 2, half_edge, 2, half_edge)
        .transpose(0, 2, 4, 6, 1, 3, 5, 7)
        .reshape(coarse_slots * 8, group_size, octant_cells)
    )
    last_octants = lax.dynamic_slice_in_dim(coarse_octants, (coarse_count - 1) * 8 + 1, 7, 0)
    lower_octants = from_behind(last_octants, "blocks", 1)
    back_table = jnp.concatenate([coarse_octants, lower_octants], axis=0)
    parents = block_ids // 8
    octant_ids = block_ids % 8
    back_rows = jnp.clip(
        jnp.where(
            parents >= coarse_first,
            (parents - coarse_first) * 8 + octant_ids,
            coarse_slots * 8 + octant_ids - 1,
        ),
        0,
        coarse_slots * 8 + 6,
    )
    picked_rows = back_table[back_rows]
    picked = picked_rows.reshape(slot_count, group_size, half_edge, 1, half_edge, 1, half_edge, 1)
    widened = jnp.broadcast_to(
        picked, (slot_count, group_size, half_edge, 2, half_edge, 2, half_edge, 2)
    ).reshape(slot_count, group_size, cell_count)
    fine_delta = jnp.where(
        live_mask, widened.astype(jnp.float32) * 0.125 * slope_of(pre_fine), 0.0
    ).astype(jnp.bfloat16)
    fine_weight_grad = jnp.einsum(
        "blp,bnp->bln", fine_delta, fine_views, preferred_element_type=jnp.float32
    ).sum(axis=0)
    fine_weight_grad = fine_weight_grad.reshape(group_size, 7, channels).transpose(1, 0, 2)
    fine_bias_grad = jnp.sum(fine_delta, axis=(0, 2), dtype=jnp.float32)
    fine_delta_cubes = fine_delta.reshape(slot_count, group_size, EDGE, EDGE, EDGE)
    fine_delta_halos = fine_halo(
        jax.vmap(block_layers)(fine_delta_cubes), block_ids, first_block, live_count, total_blocks
    )
    back_fine = fine_weight[pair_index].transpose(2, 0, 1).reshape(channels, 7 * group_size)
    fine_delta_views = flat_views(fine_delta, fine_delta_halos)
    fine_partial = jnp.einsum(
        "ur,bre->bue", back_fine, fine_delta_views, preferred_element_type=jnp.float32
    )
    fine_back = chan_scatter_sum(fine_partial, jnp.bfloat16)
    fine_grad = jnp.where(live_mask, fine_back, 0.0).astype(jnp.bfloat16)
    fine_weight_grad, fine_bias_grad, coarse_weight_grad, coarse_bias_grad = sum_over_blocks(
        (fine_weight_grad, fine_bias_grad, coarse_weight_grad, coarse_bias_grad)
    )
    fine_weight_grad = natural_order(fine_weight_grad)
    coarse_weight_grad = natural_order(coarse_weight_grad)
    fine_norm = jnp.sqrt(total_blocks.astype(jnp.float32) * cell_count)
    coarse_norm = jnp.sqrt(coarse_total.astype(jnp.float32) * cell_count)
    return (
        coarser_level_output,
        fine_grad,
        fine_weight_grad / fine_norm,
        fine_bias_grad / fine_norm,
        coarse_weight_grad / coarse_norm,
        coarse_bias_grad / coarse_norm,
    )


def solution(mesh):
    placed = (
        P("blocks", "chan", None),
        P(),
        P(None, "chan", None),
        P("chan"),
        P(None, "chan", None),
        P("chan"),
        P("blocks", "chan", None),
    )
    return jax.shard_map(
        local,
        mesh=mesh,
        in_specs=placed,
        out_specs=(
            P("blocks", "chan", None),
            P("blocks", "chan", None),
            P(None, "chan", None),
            P("chan"),
            P(None, "chan", None),
            P("chan"),
        ),
        check_vma=False,
    )
```

```python
import jax
import jax.numpy as jnp
from jax import lax
from jax.sharding import PartitionSpec as P

EDGE = 8


TAP_PAIRS = (0, 2, 1, 4, 3, 6, 5)


def from_behind(block, axis, distance):
    devices = range(lax.axis_size(axis))
    route = [(i - distance, i) for i in devices if i - distance in devices]
    return lax.ppermute(block, axis, route)


def block_layers(block_cube):
    channels, edge_cells = (block_cube.shape[0], block_cube.shape[1])
    side_layers = [
        block_cube[:, :, :, 0],
        block_cube[:, :, :, -1],
        block_cube[:, :, 0, :],
        block_cube[:, :, -1, :],
        block_cube[:, 0],
        block_cube[:, -1],
    ]
    return jnp.stack(side_layers).reshape(6, channels, edge_cells * edge_cells)


def flat_views(cubes, halo_layers):
    count, channels, cells = cubes.shape
    edge = EDGE
    position = jnp.arange(cells, dtype=jnp.int32)
    x_pos = position % edge
    y_pos = position // edge % edge
    z_pos = position // (edge * edge)
    sheets = halo_layers.reshape(count, 6, channels, edge * edge)
    zeros = jnp.zeros((count, channels, edge * edge), cubes.dtype)

    def back(step):
        return jnp.concatenate([zeros[:, :, :step], cubes[:, :, : cells - step]], axis=2)

    def ahead(step):
        return jnp.concatenate([cubes[:, :, step:], zeros[:, :, :step]], axis=2)

    def yz_sheet(sheet):
        return jnp.repeat(sheet, edge, axis=2)

    def zx_sheet(sheet):
        shaped = sheet.reshape(count, channels, edge, 1, edge)
        return jnp.broadcast_to(shaped, (count, channels, edge, edge, edge)).reshape(
            count, channels, cells
        )

    def yx_sheet(sheet):
        return jnp.tile(sheet, (1, 1, edge))

    minus_x = jnp.where(x_pos == 0, yz_sheet(sheets[:, 0]), back(1))
    plus_x = jnp.where(x_pos == edge - 1, yz_sheet(sheets[:, 1]), ahead(1))
    minus_y = jnp.where(y_pos == 0, zx_sheet(sheets[:, 2]), back(edge))
    plus_y = jnp.where(y_pos == edge - 1, zx_sheet(sheets[:, 3]), ahead(edge))
    minus_z = jnp.where(z_pos == 0, yx_sheet(sheets[:, 4]), back(edge * edge))
    plus_z = jnp.where(z_pos == edge - 1, yx_sheet(sheets[:, 5]), ahead(edge * edge))
    stacked = jnp.stack([cubes, minus_x, plus_x, minus_y, plus_y, minus_z, plus_z], axis=1)
    return stacked.reshape(count, 7 * channels, cells)


def chan_gather(value):
    size = lax.axis_size("chan")
    got = [value] + [
        lax.ppermute(value, "chan", [(j, (j + k) % size) for j in range(size)])
        for k in range(1, size)
    ]
    return jnp.concatenate(got, axis=1)


def arrival_order(matrix):
    size = lax.axis_size("chan")
    me = lax.axis_index("chan")
    order = (me - jnp.arange(size, dtype=jnp.int32)) % size
    rows, width = matrix.shape
    shaped = matrix.reshape(rows, 7, size, width // (7 * size))
    return jnp.take(shaped, order, axis=2).reshape(rows, width)


def chan_scatter_sum(partial, wire=None):
    size = lax.axis_size("chan")
    me = lax.axis_index("chan")
    width = partial.shape[1] // size
    pieces = partial.reshape((partial.shape[0], size, width) + partial.shape[2:])
    total = lax.dynamic_index_in_dim(pieces, me, 1, keepdims=False)
    for k in range(1, size):
        outgoing = lax.dynamic_index_in_dim(pieces, (me + k) % size, 1, keepdims=False)
        if wire is not None:
            outgoing = outgoing.astype(wire)
        total = total + lax.ppermute(
            outgoing, "chan", [(j, (j + k) % size) for j in range(size)]
        ).astype(total.dtype)
    return total


def natural_order(grad):
    taps, rows, width = grad.shape
    return arrival_order(grad.transpose(1, 0, 2).reshape(rows, taps * width)).reshape(
        rows, taps, width
    ).transpose(1, 0, 2)


def butterfly_sum(value, axis):
    size = lax.axis_size(axis)
    me = lax.axis_index(axis)
    radix = 4
    stride = 1
    while stride * radix <= size and size % (stride * radix) == 0:
        digit = me // stride % radix
        got = [value]
        for k in range(1, radix):
            route = [
                (i, i - (i // stride % radix) * stride + ((i // stride + k) % radix) * stride)
                for i in range(size)
            ]
            got.append(lax.ppermute(value, axis, route))
        stacked = jnp.stack(got)
        ordered = [
            lax.dynamic_index_in_dim(stacked, (digit - m) % radix, 0, keepdims=False)
            for m in range(radix)
        ]
        value = ordered[0]
        for m in range(1, radix):
            value = value + ordered[m]
        stride *= radix
    distance = stride
    while distance < size:
        if size % (distance * 2):
            return lax.psum(value, axis)
        value = value + lax.ppermute(value, axis, [(i, i ^ distance) for i in range(size)])
        distance *= 2
    return value


def slope_of(pre_values):
    sigmoid_values = jax.nn.sigmoid(pre_values)
    return sigmoid_values * (1.0 + pre_values * (1.0 - sigmoid_values))


def fine_halo(layer_table, block_ids, first_block, live_count, total_blocks):
    slot_count = layer_table.shape[0]
    plus_side = layer_table[:, 1::2]
    minus_side = layer_table[:, 0::2]
    tail_layers = lax.dynamic_slice_in_dim(plus_side, live_count - 4, 4, 0)
    from_lower = from_behind(tail_layers, "blocks", 1)
    from_upper = from_behind(minus_side[:4], "blocks", -1)
    table_minus = jnp.concatenate([from_lower, plus_side], axis=0)
    table_plus = jnp.concatenate([minus_side, from_upper], axis=0)
    strides = jnp.array([1, 2, 4], jnp.int32)
    lower_ids = block_ids[:, None] - strides[None, :]
    upper_octant_index = block_ids[:, None] + strides[None, :]
    end_block = first_block + live_count
    rows_minus = jnp.clip(lower_ids - first_block + 4, 0, slot_count + 3)
    rows_plus = jnp.clip(
        jnp.where(
            upper_octant_index < end_block,
            upper_octant_index - first_block,
            slot_count + upper_octant_index - end_block,
        ),
        0,
        slot_count + 3,
    )
    columns = jnp.arange(3, dtype=jnp.int32)[None, :]
    got_minus = table_minus[rows_minus, columns]
    got_plus = table_plus[rows_plus, columns]
    parity_x = block_ids % 2
    parity_y = block_ids // 2 % 2
    keep_minus = jnp.stack([parity_x == 1, parity_y == 1, block_ids >= 4], axis=1)
    keep_plus = jnp.stack([parity_x == 0, parity_y == 0, block_ids + 4 < total_blocks], axis=1)
    zero_value = jnp.zeros((), layer_table.dtype)
    got_minus = jnp.where(keep_minus[:, :, None, None], got_minus, zero_value)
    got_plus = jnp.where(keep_plus[:, :, None, None], got_plus, zero_value)
    merged = jnp.stack([got_minus, got_plus], axis=2)
    return merged.reshape(layer_table.shape)


def coarse_halo(layer_table, coarse_ids, coarse_first, coarse_count, coarse_total):
    slot_count = layer_table.shape[0]
    top_layers = layer_table[:, 5]
    bottom_layers = layer_table[:, 4]
    last_top = lax.dynamic_index_in_dim(top_layers, coarse_count - 1, 0, keepdims=False)
    from_lower = from_behind(last_top, "blocks", 1)
    from_upper = from_behind(bottom_layers[0], "blocks", -1)
    table_minus = jnp.concatenate([from_lower[None], top_layers], axis=0)
    table_plus = jnp.concatenate([bottom_layers, from_upper[None]], axis=0)
    rows_minus = jnp.clip(coarse_ids - coarse_first, 0, slot_count)
    rows_plus = jnp.clip(
        jnp.where(
            coarse_ids + 1 < coarse_first + coarse_count, coarse_ids + 1 - coarse_first, slot_count
        ),
        0,
        slot_count,
    )
    zero_value = jnp.zeros((), layer_table.dtype)
    below_layer = jnp.where((coarse_ids >= 1)[:, None, None], table_minus[rows_minus], zero_value)
    above_layer = jnp.where(
        (coarse_ids + 1 < coarse_total)[:, None, None], table_plus[rows_plus], zero_value
    )
    flat_zero = jnp.zeros_like(below_layer)
    return jnp.stack([flat_zero, flat_zero, flat_zero, flat_zero, below_layer, above_layer], axis=1)


def restrict_blocks(hidden, half_edge):
    count, width = (hidden.shape[0], hidden.shape[1])
    shaped = hidden.reshape(count, width, half_edge, 2, half_edge, 2, half_edge, 2)
    return (
        (jnp.sum(shaped, axis=(3, 5, 7), dtype=jnp.float32) * 0.125)
        .astype(jnp.bfloat16)
        .reshape(count, width, half_edge**3)
    )


def sum_over_blocks(parts):
    flat = jnp.concatenate([part.reshape(-1) for part in parts])
    summed = butterfly_sum(flat, "blocks")
    pieces = []
    offset = 0
    for part in parts:
        pieces.append(summed[offset : offset + part.size].reshape(part.shape))
        offset += part.size
    return tuple(pieces)


def local(
    fine_input, block_counts, fine_weight, fine_bias, coarse_weight, coarse_bias, coarse_cotangent
):
    slot_count, group_size, cell_count = fine_input.shape
    coarse_slots = coarse_cotangent.shape[0]
    channels = fine_weight.shape[2]
    half_edge = EDGE // 2
    octant_cells = half_edge**3
    pair_index = jnp.array(TAP_PAIRS, jnp.int32)
    device = lax.axis_index("blocks")
    starts = jnp.cumsum(block_counts) - block_counts
    first_block = starts[device]
    live_count = block_counts[device]
    end_block = first_block + live_count
    total_blocks = jnp.sum(block_counts)
    coarse_total = total_blocks // 8
    coarse_first = (first_block + 7) // 8
    coarse_count = (end_block + 7) // 8 - coarse_first
    block_ids = first_block + jnp.arange(slot_count, dtype=jnp.int32)
    coarse_ids = coarse_first + jnp.arange(coarse_slots, dtype=jnp.int32)
    live_mask = (jnp.arange(slot_count) < live_count)[:, None, None]
    coarse_live = (jnp.arange(coarse_slots) < coarse_count)[:, None, None]
    full_input = chan_gather(fine_input)
    fine_cubes = full_input.reshape(slot_count, channels, EDGE, EDGE, EDGE)
    input_halos = fine_halo(
        jax.vmap(block_layers)(fine_cubes), block_ids, first_block, live_count, total_blocks
    )
    forward_fine = arrival_order(fine_weight.transpose(1, 0, 2).reshape(group_size, 7 * channels))
    fine_views = flat_views(full_input, input_halos)
    pre_fine = (
        jnp.einsum("ln,bnp->blp", forward_fine, fine_views, preferred_element_type=jnp.float32)
        + fine_bias[None, :, None]
    )
    octants = restrict_blocks(jax.nn.silu(pre_fine).astype(jnp.bfloat16), half_edge)
    upper_octants = from_behind(octants[:7], "blocks", -1)
    octant_table = jnp.concatenate([octants, upper_octants], axis=0)
    children = coarse_ids[:, None] * 8 + jnp.arange(8, dtype=jnp.int32)[None, :]
    child_rows = jnp.clip(
        jnp.where(children < end_block, children - first_block, slot_count + children - end_block),
        0,
        slot_count + 6,
    )
    gathered = octant_table[child_rows]
    coarse_local = (
        gathered.reshape(coarse_slots, 2, 2, 2, group_size, half_edge, half_edge, half_edge)
        .transpose(0, 4, 1, 5, 2, 6, 3, 7)
        .reshape(coarse_slots, group_size, cell_count)
    )
    coarse_local = jnp.where(coarse_live, coarse_local, jnp.zeros((), jnp.bfloat16))
    coarse_full = chan_gather(coarse_local)
    coarse_cubes = coarse_full.reshape(coarse_slots, channels, EDGE, EDGE, EDGE)
    coarse_in_halos = coarse_halo(
        jax.vmap(block_layers)(coarse_cubes), coarse_ids, coarse_first, coarse_count, coarse_total
    )
    coarser_level_views = flat_views(coarse_full, coarse_in_halos)
    forward_coarser_level = arrival_order(
        coarse_weight.transpose(1, 0, 2).reshape(group_size, 7 * channels)
    )
    pre_coarse = (
        jnp.einsum(
            "ln,enp->elp",
            forward_coarser_level,
            coarser_level_views,
            preferred_element_type=jnp.float32,
        )
        + coarse_bias[None, :, None]
    )
    coarser_level_output = jnp.where(coarse_live, jax.nn.silu(pre_coarse), 0.0).astype(jnp.bfloat16)
    coarser_level_delta = jnp.where(
        coarse_live, coarse_cotangent.astype(jnp.float32) * slope_of(pre_coarse), 0.0
    ).astype(jnp.bfloat16)
    coarse_weight_grad = jnp.einsum(
        "zlc,znc->ln", coarser_level_delta, coarser_level_views, preferred_element_type=jnp.float32
    )
    coarse_weight_grad = coarse_weight_grad.reshape(group_size, 7, channels).transpose(1, 0, 2)
    coarse_bias_grad = jnp.sum(coarser_level_delta, axis=(0, 2), dtype=jnp.float32)
    delta_cubes = coarser_level_delta.reshape(coarse_slots, group_size, EDGE, EDGE, EDGE)
    delta_halos = coarse_halo(
        jax.vmap(block_layers)(delta_cubes), coarse_ids, coarse_first, coarse_count, coarse_total
    )
    delta_window_views = flat_views(coarser_level_delta, delta_halos)
    backward_coarser_level = (
        coarse_weight[pair_index].transpose(2, 0, 1).reshape(channels, 7 * group_size)
    )
    partial_sums = jnp.einsum(
        "ur,mre->mue",
        backward_coarser_level,
        delta_window_views,
        preferred_element_type=jnp.float32,
    )
    coarse_back = chan_scatter_sum(partial_sums, jnp.bfloat16)
    coarse_back = jnp.where(coarse_live, coarse_back, 0.0).astype(jnp.bfloat16)
    coarse_octants = (
        coarse_back.reshape(coarse_slots, group_size, 2, half_edge, 2, half_edge, 2, half_edge)
        .transpose(0, 2, 4, 6, 1, 3, 5, 7)
        .reshape(coarse_slots * 8, group_size, octant_cells)
    )
    last_octants = lax.dynamic_slice_in_dim(coarse_octants, (coarse_count - 1) * 8 + 1, 7, 0)
    lower_octants = from_behind(last_octants, "blocks", 1)
    back_table = jnp.concatenate([coarse_octants, lower_octants], axis=0)
    parents = block_ids // 8
    octant_ids = block_ids % 8
    back_rows = jnp.clip(
        jnp.where(
            parents >= coarse_first,
            (parents - coarse_first) * 8 + octant_ids,
            coarse_slots * 8 + octant_ids - 1,
        ),
        0,
        coarse_slots * 8 + 6,
    )
    picked_rows = back_table[back_rows]
    picked = picked_rows.reshape(slot_count, group_size, half_edge, 1, half_edge, 1, half_edge, 1)
    widened = jnp.broadcast_to(
        picked, (slot_count, group_size, half_edge, 2, half_edge, 2, half_edge, 2)
    ).reshape(slot_count, group_size, cell_count)
    fine_delta = jnp.where(
        live_mask, widened.astype(jnp.float32) * 0.125 * slope_of(pre_fine), 0.0
    ).astype(jnp.bfloat16)
    fine_weight_grad = jnp.einsum(
        "blp,bnp->bln", fine_delta, fine_views, preferred_element_type=jnp.float32
    ).sum(axis=0)
    fine_weight_grad = fine_weight_grad.reshape(group_size, 7, channels).transpose(1, 0, 2)
    fine_bias_grad = jnp.sum(fine_delta, axis=(0, 2), dtype=jnp.float32)
    fine_delta_cubes = fine_delta.reshape(slot_count, group_size, EDGE, EDGE, EDGE)
    fine_delta_halos = fine_halo(
        jax.vmap(block_layers)(fine_delta_cubes), block_ids, first_block, live_count, total_blocks
    )
    back_fine = fine_weight[pair_index].transpose(2, 0, 1).reshape(channels, 7 * group_size)
    fine_delta_views = flat_views(fine_delta, fine_delta_halos)
    fine_partial = jnp.einsum(
        "ur,bre->bue", back_fine, fine_delta_views, preferred_element_type=jnp.float32
    )
    fine_back = chan_scatter_sum(fine_partial, jnp.bfloat16)
    fine_grad = jnp.where(live_mask, fine_back, 0.0).astype(jnp.bfloat16)
    fine_weight_grad, fine_bias_grad, coarse_weight_grad, coarse_bias_grad = sum_over_blocks(
        (fine_weight_grad, fine_bias_grad, coarse_weight_grad, coarse_bias_grad)
    )
    fine_weight_grad = natural_order(fine_weight_grad)
    coarse_weight_grad = natural_order(coarse_weight_grad)
    fine_norm = jnp.sqrt(total_blocks.astype(jnp.float32) * cell_count)
    coarse_norm = jnp.sqrt(coarse_total.astype(jnp.float32) * cell_count)
    return (
        coarser_level_output,
        fine_grad,
        fine_weight_grad / fine_norm,
        fine_bias_grad / fine_norm,
        coarse_weight_grad / coarse_norm,
        coarse_bias_grad / coarse_norm,
    )


def solution(mesh):
    placed = (
        P("blocks", "chan", None),
        P(),
        P(None, "chan", None),
        P("chan"),
        P(None, "chan", None),
        P("chan"),
        P("blocks", "chan", None),
    )
    return jax.shard_map(
        local,
        mesh=mesh,
        in_specs=placed,
        out_specs=(
            P("blocks", "chan", None),
            P("blocks", "chan", None),
            P(None, "chan", None),
            P("chan"),
            P(None, "chan", None),
            P("chan"),
        ),
        check_vma=False,
    )
```
